32 devices in a mesh: seq: 16 (over z, y, x), head: 2 (over core).
Axes of the slice: x: 2, y: 2, z: 4, core: 2. Of those that a mesh axis runs over, the one named last changes fastest.
Arguments:
- ingest: bfloat16 [256, 128, 1024], P('seq', None, 'head'), may hold values from -6 to 6
- dest_tile: int32 [256], P('seq'), may hold values from 0 to 255, as said below
- doc_start: int32 [256], P('seq'), may hold values from 0 to 128, as said below
- w_zx: bfloat16 [1024, 2, 2048], P(None, None, 'head'), may hold values from -0.1875 to 0.1875
- w_bc: bfloat16 [1024, 256], replicated, may hold values from -0.1875 to 0.1875
- w_dt: bfloat16 [1024, 32], P(None, 'head'), may hold values from -0.1875 to 0.1875
- dt_bias: float32 [32], P('head'), may hold values from -7.5 to -5.5
- a_log: float32 [32], P('head'), may hold values from -10 to 3
- conv_x: float32 [4, 2048], P(None, 'head'), may hold values from -3 to 3
- conv_bc: float32 [4, 256], replicated, may hold values from -3 to 3
- cbias_x: float32 [2048], P('head'), may hold values from -3 to 3
- cbias_bc: float32 [256], replicated, may hold values from -3 to 3
- d_skip: float32 [32], P('head'), may hold values from 0.5 to 1.5
- norm_gain: float32 [2048], P('head'), may hold values from 0.1 to 1.9
Outputs:
- embedded: bfloat16 [32768, 2048], P('seq', 'head')
The draws below stay inside these ranges and needn't reach their ends.
Inputs may be any that keep to these rules, and one draw needn't show every extreme that they name: dest_tile is a permutation of the sequence tiles; the owner of sequence tile p is p // 16; the 16 tiles of one ingest device go to 16 different owners, and every owner receives exactly 16 tiles. `doc_start`: 128 means that no document starts in the tile.
All inputs are finite; a program needn't handle non-finite values.
Results may differ from the reference program's by a relative error of at most 0.0056.
Values may be sent and summed in bfloat16 or wider, within the bound.
No kernel may reach another device: no remote copies, remote signals or barrier semaphores. Data moves between devices by JAX's collectives and lax.ppermute only.
A program may use at most 128 MiB of HBM per device.

```python
import jax
import jax.numpy as jnp
from jax import lax

D = 1024
INNER = 2048
HEADS = 32
HEAD_DIM = 64
STATE = 128
CONV = 4
TILE = 128
TILES_DEV = 16
TILES_ALL = 256
TOKENS = 32768


def draw_dest_tile(key, part):
    shards = TILES_ALL // TILES_DEV
    keys = jax.random.split(jax.random.fold_in(key, 11), 5)
    rank = jax.random.permutation(keys[0], shards)
    place = jax.random.permutation(keys[1], shards)
    shifts = jax.random.permutation(keys[2], shards)[:TILES_DEV]
    order = jax.vmap(lambda single: jax.random.permutation(single, TILES_DEV))(jax.random.split(keys[3], shards))
    slotting = jax.vmap(lambda single: jax.random.permutation(single, TILES_DEV))(jax.random.split(keys[4], shards))
    owner = place[(rank[:, None] + shifts[order]) % shards]
    offset = slotting[owner, order]
    return (owner * TILES_DEV + offset).reshape(-1).astype(jnp.int32)


def draw_doc_start(key, part):
    keys = jax.random.split(jax.random.fold_in(key, 23), 2)
    which = jax.random.randint(keys[0], (2,), 1, TILES_ALL, dtype=jnp.int32)
    spots = jax.random.randint(keys[1], (2,), 0, TILE, dtype=jnp.int32)
    starts = jnp.full((TILES_ALL,), TILE, dtype=jnp.int32)
    return starts.at[which].set(spots).astype(jnp.int32)


def levels(own_key, extent, pieces, least, high):
    level = 1.0
    for axis_at, parts in pieces:
        steps = jax.random.uniform(jax.random.fold_in(jax.random.fold_in(own_key, 6), axis_at), (parts,), jnp.float32, least / len(pieces), high / len(pieces))
        level = level * jnp.repeat(jnp.exp(steps), extent[axis_at] // parts).reshape((-1,) + (1,) * (len(extent) - 1 - axis_at))
    return level


def gaussian(rng, dims, scale, reach, cuts=(), kind=jnp.bfloat16):
    factor_of = levels(rng, dims, cuts, -0.22, 0.18) if cuts else 1.0
    values = jax.random.normal(rng, dims, jnp.float32) * scale * factor_of
    return jnp.minimum(jnp.maximum(values, -reach), reach).astype(kind)


def setup_inputs(seed: int = 0) -> dict:
    arg_keys = jax.random.split(jax.random.key(seed), 15)
    return {
        "ingest": gaussian(arg_keys[0], (TILES_ALL, TILE, D), 1.0, 6.0, ((0, 16), (2, 2))),
        "dest_tile": draw_dest_tile(jax.random.fold_in(arg_keys[14], 71), 0),
        "doc_start": draw_doc_start(jax.random.fold_in(arg_keys[14], 71), 0),
        "w_zx": gaussian(arg_keys[3], (D, 2, INNER), D ** -0.5, 0.1875, ((2, 2),)),
        "w_bc": gaussian(arg_keys[4], (D, 2 * STATE), D ** -0.5, 0.1875),
        "w_dt": gaussian(arg_keys[5], (D, HEADS), D ** -0.5, 0.1875, ((1, 2),)),
        "dt_bias": jnp.clip(-7.5 + 2.0 * jax.random.uniform(arg_keys[6], (HEADS,), jnp.float32) ** levels(arg_keys[6], (HEADS,), ((0, 2),), -0.2, 0.2), -7.5, -5.5),
        "a_log": jnp.clip(-10.0 + 13.0 * jax.random.uniform(arg_keys[7], (HEADS,), jnp.float32) ** levels(arg_keys[7], (HEADS,), ((0, 2),), -0.2, 0.2), -10.0, 3.0),
        "conv_x": gaussian(arg_keys[8], (CONV, INNER), CONV ** -0.5, 3.0, ((1, 2),), jnp.float32),
        "conv_bc": gaussian(arg_keys[9], (CONV, 2 * STATE), CONV ** -0.5, 3.0, (), jnp.float32),
        "cbias_x": gaussian(arg_keys[10], (INNER,), 0.5, 3.0, ((0, 2),), jnp.float32),
        "cbias_bc": gaussian(arg_keys[11], (2 * STATE,), 0.5, 3.0, (), jnp.float32),
        "d_skip": jnp.clip(0.5 + 1.0 * jax.random.uniform(arg_keys[12], (HEADS,), jnp.float32) ** levels(arg_keys[12], (HEADS,), ((0, 2),), -0.2, 0.2), 0.5, 1.5),
        "norm_gain": jnp.clip(1.0 + 0.18 * jax.random.normal(arg_keys[13], (INNER,), jnp.float32), 0.1, 1.9),
    }


EPSILON = 1e-05

def reference(ingest, dest_tile, doc_start, w_zx, w_bc, w_dt, dt_bias, a_log, conv_x, conv_bc, cbias_x, cbias_bc, d_skip, norm_gain):
    ordered = jnp.zeros_like(ingest).at[dest_tile].set(ingest)
    within = jnp.arange(TILE, dtype=jnp.int32)
    flags = (within[None, :] == doc_start[:, None]).astype(jnp.int32)
    segment = jnp.cumsum(flags.reshape(-1)).astype(jnp.int32).reshape(TILES_ALL, TILE)
    zx_cols = w_zx.reshape(D, 2 * INNER)
    conv_weight = jnp.concatenate([conv_x, conv_bc], 1).astype(jnp.float32)
    conv_bias = jnp.concatenate([cbias_x, cbias_bc], 0).astype(jnp.float32)
    rate = -jnp.exp(a_log.astype(jnp.float32))
    causal = within[:, None] >= within[None, :]
    keep_rows = CONV - 1

    def step(carry, inputs):
        state, tail, tail_seg = carry
        block, seg_rows, bound = inputs
        zx = jnp.dot(block, zx_cols, preferred_element_type=jnp.float32).astype(jnp.bfloat16)
        bc = jnp.dot(block, w_bc, preferred_element_type=jnp.float32).astype(jnp.bfloat16)
        step_dt = jax.nn.softplus(jnp.dot(block, w_dt, preferred_element_type=jnp.float32) + dt_bias.astype(jnp.float32)[None, :])
        gate = zx[:, :INNER]
        conv_in = jnp.concatenate([zx[:, INNER:], bc], 1)
        extended = jnp.concatenate([tail, conv_in], 0)
        ext_seg = jnp.concatenate([tail_seg, seg_rows], 0)
        total = conv_bias[None, :] + conv_weight[CONV - 1][None, :] * conv_in.astype(jnp.float32)
        for back_step in range(keep_rows):
            same = ext_seg[back_step:back_step + TILE] == seg_rows
            total = total + jnp.where(same[:, None], conv_weight[back_step][None, :] * extended[back_step:back_step + TILE].astype(jnp.float32), 0.0)
        conv_out = jax.nn.silu(total).astype(jnp.bfloat16)
        x_heads = conv_out[:, :INNER].reshape(TILE, HEADS, HEAD_DIM).astype(jnp.float32)
        b_part = conv_out[:, INNER:INNER + STATE]
        c_part = conv_out[:, INNER + STATE:]
        cumul = jnp.cumsum(step_dt * rate[None, :], 0)
        later = within >= bound
        keep = causal & (later[:, None] == later[None, :])
        diff = cumul[:, None, :] - cumul[None, :, :]
        decay = jnp.where(keep[:, :, None], jnp.exp(jnp.where(keep[:, :, None], diff, 0.0)), 0.0)
        scores = jnp.dot(c_part, b_part.T, preferred_element_type=jnp.float32)
        weights = (scores[:, :, None] * decay * step_dt[None, :, :]).astype(jnp.bfloat16)
        intra = jnp.einsum('ish,shp->ihp', weights.astype(jnp.float32), x_heads)
        tail_keep = (later == later[TILE - 1]).astype(jnp.float32)
        to_end = jnp.exp(cumul[TILE - 1][None, :] - cumul) * step_dt * tail_keep[:, None]
        scaled = (x_heads * to_end[:, :, None]).astype(jnp.bfloat16)
        contrib = jnp.einsum('shp,sn->hpn', scaled.astype(jnp.float32), b_part.astype(jnp.float32))
        passing = jnp.exp(cumul[TILE - 1]) * jnp.where(bound < TILE, 0.0, 1.0)
        carried = lax.optimization_barrier(state.astype(jnp.bfloat16)).astype(jnp.float32)
        earlier = 1.0 - later.astype(jnp.float32)
        inter = jnp.exp(cumul)[:, :, None] * earlier[:, None, None] * jnp.einsum('in,hpn->ihp', c_part.astype(jnp.float32), carried)
        mixed = intra + inter + d_skip.astype(jnp.float32)[None, :, None] * x_heads
        gated = mixed.reshape(TILE, INNER) * jax.nn.silu(gate.astype(jnp.float32))
        meansq = lax.optimization_barrier(jnp.sum(gated * gated, 1)) / INNER
        result = (gated * lax.rsqrt(meansq + EPSILON)[:, None] * norm_gain.astype(jnp.float32)[None, :]).astype(jnp.bfloat16)
        new_state = passing[:, None, None] * state + contrib
        return ((new_state, conv_in[TILE - keep_rows:], seg_rows[TILE - keep_rows:]), result)
    start = (jnp.zeros((HEADS, HEAD_DIM, STATE), jnp.float32), jnp.zeros((keep_rows, INNER + 2 * STATE), jnp.bfloat16), jnp.zeros((keep_rows,), jnp.int32))
    final, outputs = lax.scan(step, start, (ordered, segment, doc_start))
    return outputs.reshape(TOKENS, INNER)
```

```python
import jax
import jax.numpy as jnp
from jax import lax
from jax.sharding import PartitionSpec as P

INNER = 2048


EPSILON = 1e-05


def shifted(x, axis, by):
    devices = lax.axis_size(axis)
    pairs = [(i, i + by) for i in range(devices) if 0 <= i + by < devices]
    return lax.ppermute(x, axis, pairs)


def shards(
    ingest,
    dest_tile,
    doc_start,
    w_zx,
    w_bc,
    w_dt,
    dt_bias,
    a_log,
    conv_x,
    conv_bc,
    cbias_x,
    cbias_bc,
    d_skip,
    norm_gain,
):
    seq_count = lax.axis_size("seq")
    tiles_dev = ingest.shape[0]
    tile_len = ingest.shape[1]
    columns = ingest.shape[2]
    row_count = tiles_dev * tile_len
    heads_here = a_log.shape[0]
    inner_here = conv_x.shape[1]
    head_dim = inner_here // heads_here
    state_dim = conv_bc.shape[1] // 2
    taps = conv_x.shape[0]
    keep_rows = taps - 1
    owner = dest_tile // tiles_dev
    offset = dest_tile % tiles_dev
    slots = jnp.arange(seq_count, dtype=jnp.int32)
    pick = (owner[None, :] == slots[:, None]).astype(jnp.float32)
    outgoing = jnp.einsum(
        "sj,jrc->src", pick.astype(jnp.bfloat16), ingest, preferred_element_type=jnp.float32
    ).astype(jnp.bfloat16)
    marks = (
        jnp.dot(pick, (offset + 1).astype(jnp.float32), precision=lax.Precision.HIGHEST) - 1.0
    ).astype(jnp.bfloat16)
    incoming, got_marks = (
        lax.all_to_all(outgoing, "seq", split_axis=0, concat_axis=0, tiled=True),
        lax.all_to_all(marks, "seq", split_axis=0, concat_axis=0, tiled=True),
    )
    local_slots = jnp.arange(tiles_dev, dtype=jnp.float32)
    place = (got_marks.astype(jnp.float32)[None, :] == local_slots[:, None]).astype(jnp.bfloat16)
    arrived = jnp.einsum("js,src->jrc", place, incoming, preferred_element_type=jnp.float32).astype(
        jnp.bfloat16
    )
    own_rows = arrived.reshape(row_count, columns)
    zx_cols = w_zx.reshape(w_zx.shape[0], -1)
    weight_set = (zx_cols, w_bc, w_dt)
    piece = lax.all_gather(own_rows, "head", axis=1, tiled=True)
    acc_zx, acc_bc, acc_dt = tuple(
        (jnp.dot(piece, weight, preferred_element_type=jnp.float32) for weight in weight_set)
    )
    gate = acc_zx[:, :inner_here].astype(jnp.bfloat16)
    x_in = acc_zx[:, inner_here:].astype(jnp.bfloat16)
    bc_all = acc_bc.astype(jnp.bfloat16)
    step_dt = jax.nn.softplus(acc_dt + dt_bias[None, :])
    within = jnp.arange(tile_len, dtype=jnp.int32)
    has_bound = (doc_start < tile_len).astype(jnp.float32)
    before_count = jnp.cumsum(has_bound) - has_bound
    later = (within[None, :] >= doc_start[:, None]).astype(jnp.float32)
    segment = (before_count[:, None] + later).reshape(row_count)
    conv_in = jnp.concatenate([x_in, bc_all], 1)
    tail = conv_in[row_count - keep_rows :]
    tail_seg = (segment[row_count - keep_rows :] - segment[row_count - 1]).astype(jnp.bfloat16)
    got_tail, got_seg = shifted((tail, tail_seg), "seq", 1)
    extended = jnp.concatenate([got_tail, conv_in], 0)
    ext_seg = jnp.concatenate([got_seg.astype(jnp.float32), segment], 0)
    conv_weight = jnp.concatenate([conv_x, conv_bc], 1)
    conv_bias = jnp.concatenate([cbias_x, cbias_bc], 0)
    total = conv_bias[None, :] + conv_weight[taps - 1][None, :] * conv_in.astype(jnp.float32)
    for back_step in range(keep_rows):
        same = ext_seg[back_step : back_step + row_count] == segment
        total = total + jnp.where(
            same[:, None],
            conv_weight[back_step][None, :]
            * extended[back_step : back_step + row_count].astype(jnp.float32),
            0.0,
        )
    conv_out = jax.nn.silu(total).astype(jnp.bfloat16)
    x_heads = conv_out[:, :inner_here].reshape(tiles_dev, tile_len, heads_here, head_dim)
    b_part = conv_out[:, inner_here : inner_here + state_dim].reshape(
        tiles_dev, tile_len, state_dim
    )
    c_part = conv_out[:, inner_here + state_dim :].reshape(tiles_dev, tile_len, state_dim)
    rate = -jnp.exp(a_log)
    tile_dt = step_dt.reshape(tiles_dev, tile_len, heads_here)
    cumul = jnp.cumsum(tile_dt * rate[None, None, :], 1)
    cumul_t = cumul.transpose(0, 2, 1)
    dt_t = tile_dt.transpose(0, 2, 1)
    causal = within[:, None] >= within[None, :]
    keep = causal[None, :, :] & (later[:, :, None] == later[:, None, :])
    mask_four = keep[:, None, :, :]
    diff = cumul_t[:, :, :, None] - cumul_t[:, :, None, :]
    decay = jnp.where(mask_four, jnp.exp(jnp.where(mask_four, diff, 0.0)), 0.0)
    scores = jnp.einsum("jin,jsn->jis", c_part, b_part, preferred_element_type=jnp.float32)
    weights = (scores[:, None, :, :] * decay * dt_t[:, :, None, :]).astype(jnp.bfloat16)
    intra = jnp.einsum("jhis,jshp->jihp", weights, x_heads, preferred_element_type=jnp.float32)
    last_part = later[:, tile_len - 1]
    tail_keep = (later == last_part[:, None]).astype(jnp.float32)
    to_end = jnp.exp(cumul[:, tile_len - 1 :, :] - cumul) * tile_dt * tail_keep[:, :, None]
    scaled = (x_heads.astype(jnp.float32) * to_end[:, :, :, None]).astype(jnp.bfloat16)
    contrib = jnp.einsum("jshp,jsn->jhpn", scaled, b_part, preferred_element_type=jnp.float32)
    passing = jnp.exp(cumul[:, tile_len - 1, :]) * (1.0 - has_bound)[:, None]
    tile_ids = jnp.arange(tiles_dev + 1, dtype=jnp.int32)
    src_ids = jnp.arange(tiles_dev, dtype=jnp.int32)
    between_tiles = (src_ids[None, :, None] < src_ids[None, None, :]) & (
        src_ids[None, None, :] < tile_ids[:, None, None]
    )
    spans = jnp.prod(
        jnp.where(between_tiles[:, :, :, None], passing[None, None, :, :], 1.0), 2
    ) * (src_ids[None, :] < tile_ids[:, None]).astype(jnp.float32)[:, :, None]
    flat_contrib = contrib.reshape(tiles_dev, heads_here, head_dim * state_dim)
    local_state = jnp.einsum(
        "cjh,jhq->chq", spans, flat_contrib, precision=lax.Precision.HIGHEST
    ).reshape(tiles_dev + 1, heads_here, head_dim, state_dim)
    before_tile = local_state[:tiles_dev]
    through = jnp.cumprod(passing, 0)
    prefix = jnp.concatenate([jnp.ones((1, heads_here), jnp.float32), through[:-1]], 0)
    position = lax.axis_index("seq")
    run_decay = through[tiles_dev - 1]
    run_state = local_state[tiles_dev]
    distance = 1
    while distance < seq_count:
        got_decay, got_state = shifted((run_decay, run_state), "seq", distance)
        run_state = run_state + run_decay[:, None, None] * got_state
        run_decay = jnp.where(position >= distance, run_decay * got_decay, run_decay)
        distance *= 2
    entering = shifted(run_state, "seq", 1)
    tile_state = before_tile + prefix[:, :, None, None] * entering[None]
    carried = tile_state.astype(jnp.bfloat16)
    inter = (
        jnp.exp(cumul)[:, :, :, None]
        * (1.0 - later)[:, :, None, None]
        * jnp.einsum("jin,jhpn->jihp", c_part, carried, preferred_element_type=jnp.float32)
    )
    mixed = intra + inter + d_skip[None, None, :, None] * x_heads.astype(jnp.float32)
    gated = mixed.reshape(row_count, inner_here) * jax.nn.silu(gate.astype(jnp.float32))
    sums = lax.psum(jnp.sum(gated * gated, 1), "head")
    return (gated * lax.rsqrt(sums / INNER + EPSILON)[:, None] * norm_gain[None, :]).astype(
        jnp.bfloat16
    )


def solution(mesh):
    return jax.shard_map(
        shards,
        mesh=mesh,
        in_specs=(
            P("seq", None, "head"),
            P("seq"),
            P("seq"),
            P(None, None, "head"),
            P(),
            P(None, "head"),
            P("head"),
            P("head"),
            P(None, "head"),
            P(),
            P("head"),
            P(),
            P("head"),
            P("head"),
        ),
        out_specs=P("seq", "head"),
        check_vma=False,
    )
```

```python
import jax
import jax.numpy as jnp
from jax import lax
from jax.sharding import PartitionSpec as P

INNER = 2048


EPSILON = 1e-05


def shifted(x, axis, by):
    devices = lax.axis_size(axis)
    pairs = [(i, i + by) for i in range(devices) if 0 <= i + by < devices]
    return lax.ppermute(x, axis, pairs)


def shards(
    ingest,
    dest_tile,
    doc_start,
    w_zx,
    w_bc,
    w_dt,
    dt_bias,
    a_log,
    conv_x,
    conv_bc,
    cbias_x,
    cbias_bc,
    d_skip,
    norm_gain,
):
    seq_count = lax.axis_size("seq")
    tiles_dev = ingest.shape[0]
    tile_len = ingest.shape[1]
    columns = ingest.shape[2]
    row_count = tiles_dev * tile_len
    heads_here = a_log.shape[0]
    inner_here = conv_x.shape[1]
    head_dim = inner_here // heads_here
    state_dim = conv_bc.shape[1] // 2
    taps = conv_x.shape[0]
    keep_rows = taps - 1
    owner = dest_tile // tiles_dev
    offset = dest_tile % tiles_dev
    slots = jnp.arange(seq_count, dtype=jnp.int32)
    pick = (owner[None, :] == slots[:, None]).astype(jnp.float32)
    outgoing = jnp.einsum(
        "sj,jrc->src", pick.astype(jnp.bfloat16), ingest, preferred_element_type=jnp.float32
    ).astype(jnp.bfloat16)
    marks = (
        jnp.dot(pick, (offset + 1).astype(jnp.float32), precision=lax.Precision.HIGHEST) - 1.0
    ).astype(jnp.bfloat16)
    incoming, got_marks = (
        lax.all_to_all(outgoing, "seq", split_axis=0, concat_axis=0, tiled=True),
        lax.all_to_all(marks, "seq", split_axis=0, concat_axis=0, tiled=True),
    )
    local_slots = jnp.arange(tiles_dev, dtype=jnp.float32)
    place = (got_marks.astype(jnp.float32)[None, :] == local_slots[:, None]).astype(jnp.bfloat16)
    arrived = jnp.einsum("js,src->jrc", place, incoming, preferred_element_type=jnp.float32).astype(
        jnp.bfloat16
    )
    own_rows = arrived.reshape(row_count, columns)
    zx_cols = w_zx.reshape(w_zx.shape[0], -1)
    weight_set = (zx_cols, w_bc, w_dt)
    piece = lax.all_gather(own_rows, "head", axis=1, tiled=True)
    acc_zx, acc_bc, acc_dt = tuple(
        (jnp.dot(piece, weight, preferred_element_type=jnp.float32) for weight in weight_set)
    )
    gate = acc_zx[:, :inner_here].astype(jnp.bfloat16)
    x_in = acc_zx[:, inner_here:].astype(jnp.bfloat16)
    bc_all = acc_bc.astype(jnp.bfloat16)
    step_dt = jax.nn.softplus(acc_dt + dt_bias[None, :])
    within = jnp.arange(tile_len, dtype=jnp.int32)
    has_bound = (doc_start < tile_len).astype(jnp.float32)
    before_count = jnp.cumsum(has_bound) - has_bound
    later = (within[None, :] >= doc_start[:, None]).astype(jnp.float32)
    segment = (before_count[:, None] + later).reshape(row_count)
    conv_in = jnp.concatenate([x_in, bc_all], 1)
    tail = conv_in[row_count - keep_rows :]
    tail_seg = (segment[row_count - keep_rows :] - segment[row_count - 1]).astype(jnp.bfloat16)
    got_tail, got_seg = shifted((tail, tail_seg), "seq", 1)
    extended = jnp.concatenate([got_tail, conv_in], 0)
    ext_seg = jnp.concatenate([got_seg.astype(jnp.float32), segment], 0)
    conv_weight = jnp.concatenate([conv_x, conv_bc], 1)
    conv_bias = jnp.concatenate([cbias_x, cbias_bc], 0)
    total = conv_bias[None, :] + conv_weight[taps - 1][None, :] * conv_in.astype(jnp.float32)
    for back_step in range(keep_rows):
        same = ext_seg[back_step : back_step + row_count] == segment
        total = total + jnp.where(
            same[:, None],
            conv_weight[back_step][None, :]
            * extended[back_step : back_step + row_count].astype(jnp.float32),
            0.0,
        )
    conv_out = jax.nn.silu(total).astype(jnp.bfloat16)
    x_heads = conv_out[:, :inner_here].reshape(tiles_dev, tile_len, heads_here, head_dim)
    b_part = conv_out[:, inner_here : inner_here + state_dim].reshape(
        tiles_dev, tile_len, state_dim
    )
    c_part = conv_out[:, inner_here + state_dim :].reshape(tiles_dev, tile_len, state_dim)
    rate = -jnp.exp(a_log)
    tile_dt = step_dt.reshape(tiles_dev, tile_len, heads_here)
    cumul = jnp.cumsum(tile_dt * rate[None, None, :], 1)
    cumul_t = cumul.transpose(0, 2, 1)
    dt_t = tile_dt.transpose(0, 2, 1)
    causal = within[:, None] >= within[None, :]
    keep = causal[None, :, :] & (later[:, :, None] == later[:, None, :])
    mask_four = keep[:, None, :, :]
    diff = cumul_t[:, :, :, None] - cumul_t[:, :, None, :]
    decay = jnp.where(mask_four, jnp.exp(jnp.where(mask_four, diff, 0.0)), 0.0)
    scores = jnp.einsum("jin,jsn->jis", c_part, b_part, preferred_element_type=jnp.float32)
    weights = (scores[:, None, :, :] * decay * dt_t[:, :, None, :]).astype(jnp.bfloat16)
    intra = jnp.einsum("jhis,jshp->jihp", weights, x_heads, preferred_element_type=jnp.float32)
    last_part = later[:, tile_len - 1]
    tail_keep = (later == last_part[:, None]).astype(jnp.float32)
    to_end = jnp.exp(cumul[:, tile_len - 1 :, :] - cumul) * tile_dt * tail_keep[:, :, None]
    scaled = (x_heads.astype(jnp.float32) * to_end[:, :, :, None]).astype(jnp.bfloat16)
    contrib = jnp.einsum("jshp,jsn->jhpn", scaled, b_part, preferred_element_type=jnp.float32)
    passing = jnp.exp(cumul[:, tile_len - 1, :]) * (1.0 - has_bound)[:, None]
    flat_contrib = contrib.reshape(tiles_dev, heads_here, head_dim * state_dim)
    through = jnp.cumprod(passing, 0)
    prefix = jnp.concatenate([jnp.ones((1, heads_here), jnp.float32), through[:-1]], 0)
    reverse = jnp.cumprod(passing[::-1], 0)[::-1]
    to_last = jnp.concatenate([reverse[1:], jnp.ones((1, heads_here), jnp.float32)], 0)
    run_state = jnp.sum(to_last[:, :, None] * flat_contrib, 0).reshape(
        heads_here, head_dim, state_dim
    )
    running = jnp.zeros((heads_here, head_dim * state_dim), jnp.float32)
    states = []
    for tile in range(tiles_dev):
        states.append(running)
        running = passing[tile][:, None] * running + flat_contrib[tile]
    before_tile = jnp.stack(states).reshape(tiles_dev, heads_here, head_dim, state_dim)
    position = lax.axis_index("seq")
    run_decay = through[tiles_dev - 1]
    distance = 1
    while distance < seq_count:
        got_decay, got_state = shifted((run_decay, run_state), "seq", distance)
        run_state = run_state + run_decay[:, None, None] * got_state
        run_decay = jnp.where(position >= distance, run_decay * got_decay, run_decay)
        distance *= 2
    entering = shifted(run_state, "seq", 1)
    tile_state = before_tile + prefix[:, :, None, None] * entering[None]
    carried = tile_state.astype(jnp.bfloat16)
    inter = (
        jnp.exp(cumul)[:, :, :, None]
        * (1.0 - later)[:, :, None, None]
        * jnp.einsum("jin,jhpn->jihp", c_part, carried, preferred_element_type=jnp.float32)
    )
    mixed = intra + inter + d_skip[None, None, :, None] * x_heads.astype(jnp.float32)
    gated = mixed.reshape(row_count, inner_here) * jax.nn.silu(gate.astype(jnp.float32))
    sums = lax.psum(jnp.sum(gated * gated, 1), "head")
    return (gated * lax.rsqrt(sums / INNER + EPSILON)[:, None] * norm_gain[None, :]).astype(
        jnp.bfloat16
    )


def solution(mesh):
    return jax.shard_map(
        shards,
        mesh=mesh,
        in_specs=(
            P("seq", None, "head"),
            P("seq"),
            P("seq"),
            P(None, None, "head"),
            P(),
            P(None, "head"),
            P("head"),
            P("head"),
            P(None, "head"),
            P(),
            P("head"),
            P(),
            P("head"),
            P("head"),
        ),
        out_specs=P("seq", "head"),
        check_vma=False,
    )
```

```python
import jax
import jax.numpy as jnp
from jax import lax
from jax.sharding import PartitionSpec as P

INNER = 2048


EPSILON = 1e-05


def shifted(x, axis, by):
    devices = lax.axis_size(axis)
    pairs = [(i, i + by) for i in range(devices) if 0 <= i + by < devices]
    return lax.ppermute(x, axis, pairs)


def shards(
    ingest,
    dest_tile,
    doc_start,
    w_zx,
    w_bc,
    w_dt,
    dt_bias,
    a_log,
    conv_x,
    conv_bc,
    cbias_x,
    cbias_bc,
    d_skip,
    norm_gain,
):
    seq_count = lax.axis_size("seq")
    tiles_dev = ingest.shape[0]
    tile_len = ingest.shape[1]
    columns = ingest.shape[2]
    row_count = tiles_dev * tile_len
    heads_here = a_log.shape[0]
    inner_here = conv_x.shape[1]
    head_dim = inner_here // heads_here
    state_dim = conv_bc.shape[1] // 2
    taps = conv_x.shape[0]
    keep_rows = taps - 1
    owner = dest_tile // tiles_dev
    offset = dest_tile % tiles_dev
    slots = jnp.arange(seq_count, dtype=jnp.int32)
    pick = (owner[None, :] == slots[:, None]).astype(jnp.float32)
    outgoing = jnp.einsum(
        "sj,jrc->src", pick.astype(jnp.bfloat16), ingest, preferred_element_type=jnp.float32
    ).astype(jnp.bfloat16)
    marks = (
        jnp.dot(pick, (offset + 1).astype(jnp.float32), precision=lax.Precision.HIGHEST) - 1.0
    ).astype(jnp.bfloat16)
    incoming, got_marks = (
        lax.all_to_all(outgoing, "seq", split_axis=0, concat_axis=0, tiled=True),
        lax.all_to_all(marks, "seq", split_axis=0, concat_axis=0, tiled=True),
    )
    local_slots = jnp.arange(tiles_dev, dtype=jnp.float32)
    place = (got_marks.astype(jnp.float32)[None, :] == local_slots[:, None]).astype(jnp.bfloat16)
    arrived = jnp.einsum("js,src->jrc", place, incoming, preferred_element_type=jnp.float32).astype(
        jnp.bfloat16
    )
    own_rows = arrived.reshape(row_count, columns)
    zx_cols = w_zx.reshape(w_zx.shape[0], -1)
    weight_set = (zx_cols, w_bc, w_dt)
    piece = lax.all_gather(own_rows, "head", axis=1, tiled=True)
    acc_zx, acc_bc, acc_dt = tuple(
        (jnp.dot(piece, weight, preferred_element_type=jnp.float32) for weight in weight_set)
    )
    gate = acc_zx[:, :inner_here].astype(jnp.bfloat16)
    x_in = acc_zx[:, inner_here:].astype(jnp.bfloat16)
    bc_all = acc_bc.astype(jnp.bfloat16)
    step_dt = jax.nn.softplus(acc_dt + dt_bias[None, :])
    within = jnp.arange(tile_len, dtype=jnp.int32)
    has_bound = (doc_start < tile_len).astype(jnp.float32)
    before_count = jnp.cumsum(has_bound) - has_bound
    later = (within[None, :] >= doc_start[:, None]).astype(jnp.float32)
    segment = (before_count[:, None] + later).reshape(row_count)
    conv_in = jnp.concatenate([x_in, bc_all], 1)
    tail = conv_in[row_count - keep_rows :]
    tail_seg = (segment[row_count - keep_rows :] - segment[row_count - 1]).astype(jnp.bfloat16)
    got_tail, got_seg = shifted((tail, tail_seg), "seq", 1)
    extended = jnp.concatenate([got_tail, conv_in], 0)
    ext_seg = jnp.concatenate([got_seg.astype(jnp.float32), segment], 0)
    conv_weight = jnp.concatenate([conv_x, conv_bc], 1)
    conv_bias = jnp.concatenate([cbias_x, cbias_bc], 0)
    total = conv_bias[None, :] + conv_weight[taps - 1][None, :] * conv_in.astype(jnp.float32)
    for back_step in range(keep_rows):
        same = ext_seg[back_step : back_step + row_count] == segment
        total = total + jnp.where(
            same[:, None],
            conv_weight[back_step][None, :]
            * extended[back_step : back_step + row_count].astype(jnp.float32),
            0.0,
        )
    conv_out = jax.nn.silu(total).astype(jnp.bfloat16)
    x_heads = conv_out[:, :inner_here].reshape(tiles_dev, tile_len, heads_here, head_dim)
    b_part = conv_out[:, inner_here : inner_here + state_dim].reshape(
        tiles_dev, tile_len, state_dim
    )
    c_part = conv_out[:, inner_here + state_dim :].reshape(tiles_dev, tile_len, state_dim)
    rate = -jnp.exp(a_log)
    tile_dt = step_dt.reshape(tiles_dev, tile_len, heads_here)
    cumul = jnp.cumsum(tile_dt * rate[None, None, :], 1)
    cumul_t = cumul.transpose(0, 2, 1)
    dt_t = tile_dt.transpose(0, 2, 1)
    last_part = later[:, tile_len - 1]
    tail_keep = (later == last_part[:, None]).astype(jnp.float32)
    to_end = jnp.exp(cumul[:, tile_len - 1 :, :] - cumul) * tile_dt * tail_keep[:, :, None]
    scaled = (x_heads.astype(jnp.float32) * to_end[:, :, :, None]).astype(jnp.bfloat16)
    contrib = jnp.einsum("jshp,jsn->jhpn", scaled, b_part, preferred_element_type=jnp.float32)
    passing = jnp.exp(cumul[:, tile_len - 1, :]) * (1.0 - has_bound)[:, None]
    flat_contrib = contrib.reshape(tiles_dev, heads_here, head_dim * state_dim)
    through = jnp.cumprod(passing, 0)
    prefix = jnp.concatenate([jnp.ones((1, heads_here), jnp.float32), through[:-1]], 0)
    reverse = jnp.cumprod(passing[::-1], 0)[::-1]
    to_last = jnp.concatenate([reverse[1:], jnp.ones((1, heads_here), jnp.float32)], 0)
    run_state = jnp.sum(to_last[:, :, None] * flat_contrib, 0).reshape(
        heads_here, head_dim, state_dim
    )
    run_state, x_heads, b_part, c_part, cumul_t, dt_t = lax.optimization_barrier(
        (run_state, x_heads, b_part, c_part, cumul_t, dt_t)
    )
    causal = within[:, None] >= within[None, :]
    keep = causal[None, :, :] & (later[:, :, None] == later[:, None, :])
    mask_four = keep[:, None, :, :]
    diff = cumul_t[:, :, :, None] - cumul_t[:, :, None, :]
    decay = jnp.where(mask_four, jnp.exp(jnp.where(mask_four, diff, 0.0)), 0.0)
    scores = jnp.einsum("jin,jsn->jis", c_part, b_part, preferred_element_type=jnp.float32)
    weights = (scores[:, None, :, :] * decay * dt_t[:, :, None, :]).astype(jnp.bfloat16)
    intra = jnp.einsum("jhis,jshp->jihp", weights, x_heads, preferred_element_type=jnp.float32)
    running = jnp.zeros((heads_here, head_dim * state_dim), jnp.float32)
    states = []
    for tile in range(tiles_dev):
        states.append(running)
        running = passing[tile][:, None] * running + flat_contrib[tile]
    before_tile = jnp.stack(states).reshape(tiles_dev, heads_here, head_dim, state_dim)
    position = lax.axis_index("seq")
    run_decay = through[tiles_dev - 1]
    distance = 1
    while distance < seq_count:
        got_decay, got_state = shifted((run_decay, run_state), "seq", distance)
        run_state = run_state + run_decay[:, None, None] * got_state
        run_decay = jnp.where(position >= distance, run_decay * got_decay, run_decay)
        distance *= 2
    entering = shifted(run_state, "seq", 1)
    tile_state = before_tile + prefix[:, :, None, None] * entering[None]
    carried = tile_state.astype(jnp.bfloat16)
    inter = (
        jnp.exp(cumul)[:, :, :, None]
        * (1.0 - later)[:, :, None, None]
        * jnp.einsum("jin,jhpn->jihp", c_part, carried, preferred_element_type=jnp.float32)
    )
    mixed = intra + inter + d_skip[None, None, :, None] * x_heads.astype(jnp.float32)
    gated = mixed.reshape(row_count, inner_here) * jax.nn.silu(gate.astype(jnp.float32))
    sums = lax.psum(jnp.sum(gated * gated, 1), "head")
    return (gated * lax.rsqrt(sums / INNER + EPSILON)[:, None] * norm_gain[None, :]).astype(
        jnp.bfloat16
    )


def solution(mesh):
    return jax.shard_map(
        shards,
        mesh=mesh,
        in_specs=(
            P("seq", None, "head"),
            P("seq"),
            P("seq"),
            P(None, None, "head"),
            P(),
            P(None, "head"),
            P("head"),
            P("head"),
            P(None, "head"),
            P(),
            P("head"),
            P(),
            P("head"),
            P("head"),
        ),
        out_specs=P("seq", "head"),
        check_vma=False,
    )
```

```python
import jax
import jax.numpy as jnp
from jax import lax
from jax.experimental import pallas as pl
from jax.experimental.pallas import tpu as pltpu
from jax.sharding import PartitionSpec as P

INNER = 2048


EPSILON = 1e-05


def shifted(x, axis, by):
    devices = lax.axis_size(axis)
    pairs = [(i, i + by) for i in range(devices) if 0 <= i + by < devices]
    return lax.ppermute(x, axis, pairs)


def mix_tile(
    x_ref, b_ref, c_ref, cum_ref, cumt_ref, dtt_ref, partc_ref, partr_ref, car_ref, gate_ref, d_ref,
    out_ref, sq_ref,
):
    f32 = jnp.float32
    tile_len = x_ref.shape[0]
    pairs = x_ref.shape[1] // 128
    b_mat = b_ref[...]
    c_mat = c_ref[...]
    scores = lax.dot_general(
        c_mat, b_mat, (((1,), (1,)), ((), ())), preferred_element_type=f32
    )
    cum = cum_ref[0]
    cumt = cumt_ref[0]
    dtt = dtt_ref[0]
    part_col = partc_ref[0]
    part_row = partr_ref[0]
    row = lax.broadcasted_iota(jnp.int32, (tile_len, tile_len), 0)
    col = lax.broadcasted_iota(jnp.int32, (tile_len, tile_len), 1)
    keep = (row >= col) & (part_col == part_row)
    earlier = 1.0 - part_col
    first_half = lax.broadcasted_iota(jnp.int32, (tile_len, 128), 1) < 64
    total_sq = jnp.zeros((tile_len, 1), f32)
    for pair in range(pairs):
        cols = pl.ds(pair * 128, 128)
        x_pair = x_ref[:, cols]
        slabs = []
        for half in range(2):
            head = 2 * pair + half
            diff = cum[:, head : head + 1] - cumt[head : head + 1, :]
            decay = jnp.where(keep, jnp.exp(jnp.where(keep, diff, 0.0)), 0.0)
            slabs.append((scores * decay * dtt[head : head + 1, :]).astype(jnp.bfloat16))
        weights = jnp.concatenate(slabs, axis=1)
        zero = jnp.zeros_like(x_pair)
        split_x = jnp.concatenate(
            [jnp.where(first_half, x_pair, zero), jnp.where(first_half, zero, x_pair)], axis=0
        )
        intra = jnp.dot(weights, split_x, preferred_element_type=f32)
        carried = car_ref[0, cols, :]
        projected = lax.dot_general(
            c_mat, carried, (((1,), (1,)), ((), ())), preferred_element_type=f32
        )
        grow = jnp.where(
            first_half,
            jnp.exp(cum[:, 2 * pair : 2 * pair + 1]),
            jnp.exp(cum[:, 2 * pair + 1 : 2 * pair + 2]),
        )
        inter = grow * earlier * projected
        mixed = intra + inter + d_ref[:, cols] * x_pair.astype(f32)
        gate = gate_ref[:, cols].astype(f32)
        gated = mixed * (gate / (1.0 + jnp.exp(-gate)))
        out_ref[:, cols] = gated
        total_sq = total_sq + jnp.sum(gated * gated, axis=1, keepdims=True)
    sq_ref[...] = total_sq


def mix_tiles(conv_out, zx, cumul, cumul_t, dt_t, later, carried, d_full):
    tiles_dev, tile_len, heads_here = cumul.shape
    inner_here = carried.shape[1]
    state_dim = carried.shape[2]
    rows = tiles_dev * tile_len
    b_block = inner_here // 128
    c_block = b_block + state_dim // 128
    part_col = later.reshape(tiles_dev, tile_len, 1)
    part_row = later.reshape(tiles_dev, 1, tile_len)
    per_tile = lambda j: (j, 0, 0)
    return pl.pallas_call(
        mix_tile,
        grid=(tiles_dev,),
        in_specs=[
            pl.BlockSpec((tile_len, inner_here), lambda j: (j, 0)),
            pl.BlockSpec((tile_len, state_dim), lambda j: (j, b_block)),
            pl.BlockSpec((tile_len, state_dim), lambda j: (j, c_block)),
            pl.BlockSpec((1, tile_len, heads_here), per_tile),
            pl.BlockSpec((1, heads_here, tile_len), per_tile),
            pl.BlockSpec((1, heads_here, tile_len), per_tile),
            pl.BlockSpec((1, tile_len, 1), per_tile),
            pl.BlockSpec((1, 1, tile_len), per_tile),
            pl.BlockSpec((1, inner_here, state_dim), per_tile),
            pl.BlockSpec((tile_len, inner_here), lambda j: (j, 0)),
            pl.BlockSpec((1, inner_here), lambda j: (0, 0)),
        ],
        out_specs=[
            pl.BlockSpec((tile_len, inner_here), lambda j: (j, 0)),
            pl.BlockSpec((tile_len, 1), lambda j: (j, 0)),
        ],
        out_shape=[
            jax.ShapeDtypeStruct((rows, inner_here), jnp.float32),
            jax.ShapeDtypeStruct((rows, 1), jnp.float32),
        ],
        cost_estimate=pl.CostEstimate(
            flops=tiles_dev * (2 * tile_len * tile_len * (state_dim + 4 * inner_here + 2 * inner_here)),
            transcendentals=tiles_dev * tile_len * (tile_len * heads_here + 2 * inner_here),
            bytes_accessed=rows * inner_here * 10 + tiles_dev * inner_here * state_dim * 2,
        ),
    )(conv_out, conv_out, conv_out, cumul, cumul_t, dt_t, part_col, part_row, carried, zx, d_full)


def shards(
    ingest,
    dest_tile,
    doc_start,
    w_zx,
    w_bc,
    w_dt,
    dt_bias,
    a_log,
    conv_x,
    conv_bc,
    cbias_x,
    cbias_bc,
    d_skip,
    norm_gain,
):
    seq_count = lax.axis_size("seq")
    tiles_dev = ingest.shape[0]
    tile_len = ingest.shape[1]
    columns = ingest.shape[2]
    row_count = tiles_dev * tile_len
    heads_here = a_log.shape[0]
    inner_here = conv_x.shape[1]
    head_dim = inner_here // heads_here
    state_dim = conv_bc.shape[1] // 2
    taps = conv_x.shape[0]
    keep_rows = taps - 1
    owner = dest_tile // tiles_dev
    offset = dest_tile % tiles_dev
    slots = jnp.arange(seq_count, dtype=jnp.int32)
    pick = (owner[None, :] == slots[:, None]).astype(jnp.float32)
    outgoing = jnp.einsum(
        "sj,jrc->src", pick.astype(jnp.bfloat16), ingest, preferred_element_type=jnp.float32
    ).astype(jnp.bfloat16)
    marks = (
        jnp.dot(pick, (offset + 1).astype(jnp.float32), precision=lax.Precision.HIGHEST) - 1.0
    ).astype(jnp.bfloat16)
    incoming, got_marks = (
        lax.all_to_all(outgoing, "seq", split_axis=0, concat_axis=0, tiled=True),
        lax.all_to_all(marks, "seq", split_axis=0, concat_axis=0, tiled=True),
    )
    local_slots = jnp.arange(tiles_dev, dtype=jnp.float32)
    place = (got_marks.astype(jnp.float32)[None, :] == local_slots[:, None]).astype(jnp.bfloat16)
    arrived = jnp.einsum("js,src->jrc", place, incoming, preferred_element_type=jnp.float32).astype(
        jnp.bfloat16
    )
    own_rows = arrived.reshape(row_count, columns)
    zx_cols = w_zx.reshape(w_zx.shape[0], -1)
    weight_set = (zx_cols, w_bc, w_dt)
    piece = lax.all_gather(own_rows, "head", axis=1, tiled=True)
    acc_zx, acc_bc, acc_dt = tuple(
        (jnp.dot(piece, weight, preferred_element_type=jnp.float32) for weight in weight_set)
    )
    zx = acc_zx.astype(jnp.bfloat16)
    x_in = zx[:, inner_here:]
    bc_all = acc_bc.astype(jnp.bfloat16)
    step_dt = jax.nn.softplus(acc_dt + dt_bias[None, :])
    within = jnp.arange(tile_len, dtype=jnp.int32)
    has_bound = (doc_start < tile_len).astype(jnp.float32)
    before_count = jnp.cumsum(has_bound) - has_bound
    later = (within[None, :] >= doc_start[:, None]).astype(jnp.float32)
    segment = (before_count[:, None] + later).reshape(row_count)
    conv_in = jnp.concatenate([x_in, bc_all], 1)
    tail = conv_in[row_count - keep_rows :]
    tail_seg = (segment[row_count - keep_rows :] - segment[row_count - 1]).astype(jnp.bfloat16)
    got_tail, got_seg = shifted((tail, tail_seg), "seq", 1)
    extended = jnp.concatenate([got_tail, conv_in], 0)
    ext_seg = jnp.concatenate([got_seg.astype(jnp.float32), segment], 0)
    conv_weight = jnp.concatenate([conv_x, conv_bc], 1)
    conv_bias = jnp.concatenate([cbias_x, cbias_bc], 0)
    total = conv_bias[None, :] + conv_weight[taps - 1][None, :] * conv_in.astype(jnp.float32)
    for back_step in range(keep_rows):
        same = ext_seg[back_step : back_step + row_count] == segment
        total = total + jnp.where(
            same[:, None],
            conv_weight[back_step][None, :]
            * extended[back_step : back_step + row_count].astype(jnp.float32),
            0.0,
        )
    conv_out = jax.nn.silu(total).astype(jnp.bfloat16)
    x_heads = conv_out[:, :inner_here].reshape(tiles_dev, tile_len, heads_here, head_dim)
    b_part = conv_out[:, inner_here : inner_here + state_dim].reshape(
        tiles_dev, tile_len, state_dim
    )
    c_part = conv_out[:, inner_here + state_dim :].reshape(tiles_dev, tile_len, state_dim)
    rate = -jnp.exp(a_log)
    tile_dt = step_dt.reshape(tiles_dev, tile_len, heads_here)
    cumul = jnp.cumsum(tile_dt * rate[None, None, :], 1)
    cumul_t = cumul.transpose(0, 2, 1)
    dt_t = tile_dt.transpose(0, 2, 1)
    last_part = later[:, tile_len - 1]
    tail_keep = (later == last_part[:, None]).astype(jnp.float32)
    to_end = jnp.exp(cumul[:, tile_len - 1 :, :] - cumul) * tile_dt * tail_keep[:, :, None]
    scaled = (x_heads.astype(jnp.float32) * to_end[:, :, :, None]).astype(jnp.bfloat16)
    contrib = jnp.einsum("jshp,jsn->jhpn", scaled, b_part, preferred_element_type=jnp.float32)
    passing = jnp.exp(cumul[:, tile_len - 1, :]) * (1.0 - has_bound)[:, None]
    flat_contrib = contrib.reshape(tiles_dev, heads_here, head_dim * state_dim)
    through = jnp.cumprod(passing, 0)
    prefix = jnp.concatenate([jnp.ones((1, heads_here), jnp.float32), through[:-1]], 0)
    reverse = jnp.cumprod(passing[::-1], 0)[::-1]
    to_last = jnp.concatenate([reverse[1:], jnp.ones((1, heads_here), jnp.float32)], 0)
    run_state = jnp.sum(to_last[:, :, None] * flat_contrib, 0).reshape(
        heads_here, head_dim, state_dim
    )
    running = jnp.zeros((heads_here, head_dim * state_dim), jnp.float32)
    states = []
    for tile in range(tiles_dev):
        states.append(running)
        running = passing[tile][:, None] * running + flat_contrib[tile]
    before_tile = jnp.stack(states).reshape(tiles_dev, heads_here, head_dim, state_dim)
    position = lax.axis_index("seq")
    run_decay = through[tiles_dev - 1]
    distance = 1
    while distance < seq_count:
        got_decay, got_state = shifted((run_decay, run_state), "seq", distance)
        run_state = run_state + run_decay[:, None, None] * got_state
        run_decay = jnp.where(position >= distance, run_decay * got_decay, run_decay)
        distance *= 2
    entering = shifted(run_state, "seq", 1)
    tile_state = before_tile + prefix[:, :, None, None] * entering[None]
    carried = tile_state.astype(jnp.bfloat16).reshape(tiles_dev, inner_here, state_dim)
    d_full = jnp.repeat(d_skip, head_dim)[None, :]
    gated, row_sq = mix_tiles(conv_out, zx, cumul, cumul_t, dt_t, later, carried, d_full)
    sums = lax.psum(row_sq, "head")
    return (gated * lax.rsqrt(sums / INNER + EPSILON) * norm_gain[None, :]).astype(jnp.bfloat16)


def solution(mesh):
    return jax.shard_map(
        shards,
        mesh=mesh,
        in_specs=(
            P("seq", None, "head"),
            P("seq"),
            P("seq"),
            P(None, None, "head"),
            P(),
            P(None, "head"),
            P("head"),
            P("head"),
            P(None, "head"),
            P(),
            P("head"),
            P(),
            P("head"),
            P("head"),
        ),
        out_specs=P("seq", "head"),
        check_vma=False,
    )
```

```python
import jax
import jax.numpy as jnp
from jax import lax
from jax.experimental import pallas as pl
from jax.experimental.pallas import tpu as pltpu
from jax.sharding import PartitionSpec as P

INNER = 2048


EPSILON = 1e-05


def shifted(x, axis, by):
    devices = lax.axis_size(axis)
    pairs = [(i, i + by) for i in range(devices) if 0 <= i + by < devices]
    return lax.ppermute(x, axis, pairs)


def mix_tile(
    x_ref, b_ref, c_ref, cum_ref, cumt_ref, dtt_ref, partc_ref, partr_ref, car_ref, gate_ref, d_ref,
    out_ref, sq_ref,
):
    f32 = jnp.float32
    tile_len = x_ref.shape[0]
    pairs = x_ref.shape[1] // 128
    b_mat = b_ref[...]
    c_mat = c_ref[...]
    scores = lax.dot_general(
        c_mat, b_mat, (((1,), (1,)), ((), ())), preferred_element_type=f32
    )
    cum = cum_ref[0]
    cumt = cumt_ref[0]
    dtt = dtt_ref[0]
    part_col = partc_ref[0]
    part_row = partr_ref[0]
    row = lax.broadcasted_iota(jnp.int32, (tile_len, tile_len), 0)
    col = lax.broadcasted_iota(jnp.int32, (tile_len, tile_len), 1)
    keep = (row >= col) & (part_col == part_row)
    earlier = 1.0 - part_col
    first_half = lax.broadcasted_iota(jnp.int32, (tile_len, 128), 1) < 64
    total_sq = jnp.zeros((tile_len, 128), f32)
    for pair in range(pairs):
        cols = pl.ds(pair * 128, 128)
        x_pair = x_ref[:, cols]
        slabs = []
        for half in range(2):
            head = 2 * pair + half
            diff = cum[:, head : head + 1] - cumt[head : head + 1, :]
            decay = jnp.where(keep, jnp.exp(jnp.where(keep, diff, 0.0)), 0.0)
            slabs.append((scores * decay * dtt[head : head + 1, :]).astype(jnp.bfloat16))
        weights = jnp.concatenate(slabs, axis=1)
        zero = jnp.zeros_like(x_pair)
        split_x = jnp.concatenate(
            [jnp.where(first_half, x_pair, zero), jnp.where(first_half, zero, x_pair)], axis=0
        )
        intra = jnp.dot(weights, split_x, preferred_element_type=f32)
        carried = car_ref[0, cols, :]
        projected = lax.dot_general(
            c_mat, carried, (((1,), (1,)), ((), ())), preferred_element_type=f32
        )
        grow = jnp.where(
            first_half,
            jnp.exp(cum[:, 2 * pair : 2 * pair + 1]),
            jnp.exp(cum[:, 2 * pair + 1 : 2 * pair + 2]),
        )
        inter = grow * earlier * projected
        mixed = intra + inter + d_ref[:, cols] * x_pair.astype(f32)
        gate = gate_ref[:, cols].astype(f32)
        gated = mixed * (gate * (0.5 + 0.5 * jnp.tanh(0.5 * gate)))
        out_ref[:, cols] = gated
        total_sq = total_sq + gated * gated
    sq_ref[...] = jnp.sum(total_sq, axis=1, keepdims=True)


def contrib_tile(x_ref, b_ref, end_ref, out_ref):
    f32 = jnp.float32
    tile_len = x_ref.shape[0]
    pairs = x_ref.shape[1] // 128
    b_mat = b_ref[...]
    to_end = end_ref[0]
    first_half = lax.broadcasted_iota(jnp.int32, (tile_len, 128), 1) < 64
    for pair in range(pairs):
        cols = pl.ds(pair * 128, 128)
        scale = jnp.where(
            first_half, to_end[:, 2 * pair : 2 * pair + 1], to_end[:, 2 * pair + 1 : 2 * pair + 2]
        )
        scaled = (x_ref[:, cols].astype(f32) * scale).astype(jnp.bfloat16)
        out_ref[0, cols, :] = lax.dot_general(
            scaled, b_mat, (((0,), (0,)), ((), ())), preferred_element_type=f32
        )


def contrib_tiles(conv_out, to_end, inner_here, state_dim):
    tiles_dev, tile_len, heads_here = to_end.shape
    b_block = inner_here // 128
    return pl.pallas_call(
        contrib_tile,
        grid=(tiles_dev,),
        in_specs=[
            pl.BlockSpec((tile_len, inner_here), lambda j: (j, 0)),
            pl.BlockSpec((tile_len, state_dim), lambda j: (j, b_block)),
            pl.BlockSpec((1, tile_len, heads_here), lambda j: (j, 0, 0)),
        ],
        out_specs=pl.BlockSpec((1, inner_here, state_dim), lambda j: (j, 0, 0)),
        out_shape=jax.ShapeDtypeStruct((tiles_dev, inner_here, state_dim), jnp.float32),
        cost_estimate=pl.CostEstimate(
            flops=tiles_dev * 2 * tile_len * inner_here * state_dim,
            transcendentals=0,
            bytes_accessed=tiles_dev * (tile_len * (inner_here + state_dim) * 2 + inner_here * state_dim * 4),
        ),
    )(conv_out, conv_out, to_end)


def mix_tiles(conv_out, zx, cumul, cumul_t, dt_t, later, carried, d_full):
    tiles_dev, tile_len, heads_here = cumul.shape
    inner_here = carried.shape[1]
    state_dim = carried.shape[2]
    rows = tiles_dev * tile_len
    b_block = inner_here // 128
    c_block = b_block + state_dim // 128
    part_col = later.reshape(tiles_dev, tile_len, 1)
    part_row = later.reshape(tiles_dev, 1, tile_len)
    per_tile = lambda j: (j, 0, 0)
    return pl.pallas_call(
        mix_tile,
        grid=(tiles_dev,),
        in_specs=[
            pl.BlockSpec((tile_len, inner_here), lambda j: (j, 0)),
            pl.BlockSpec((tile_len, state_dim), lambda j: (j, b_block)),
            pl.BlockSpec((tile_len, state_dim), lambda j: (j, c_block)),
            pl.BlockSpec((1, tile_len, heads_here), per_tile),
            pl.BlockSpec((1, heads_here, tile_len), per_tile),
            pl.BlockSpec((1, heads_here, tile_len), per_tile),
            pl.BlockSpec((1, tile_len, 1), per_tile),
            pl.BlockSpec((1, 1, tile_len), per_tile),
            pl.BlockSpec((1, inner_here, state_dim), per_tile),
            pl.BlockSpec((tile_len, inner_here), lambda j: (j, 0)),
            pl.BlockSpec((1, inner_here), lambda j: (0, 0)),
        ],
        out_specs=[
            pl.BlockSpec((tile_len, inner_here), lambda j: (j, 0)),
            pl.BlockSpec((tile_len, 1), lambda j: (j, 0)),
        ],
        out_shape=[
            jax.ShapeDtypeStruct((rows, inner_here), jnp.float32),
            jax.ShapeDtypeStruct((rows, 1), jnp.float32),
        ],
        cost_estimate=pl.CostEstimate(
            flops=tiles_dev * (2 * tile_len * tile_len * (state_dim + 4 * inner_here + 2 * inner_here)),
            transcendentals=tiles_dev * tile_len * (tile_len * heads_here + 2 * inner_here),
            bytes_accessed=rows * inner_here * 10 + tiles_dev * inner_here * state_dim * 2,
        ),
    )(conv_out, conv_out, conv_out, cumul, cumul_t, dt_t, part_col, part_row, carried, zx, d_full)


def shards(
    ingest,
    dest_tile,
    doc_start,
    w_zx,
    w_bc,
    w_dt,
    dt_bias,
    a_log,
    conv_x,
    conv_bc,
    cbias_x,
    cbias_bc,
    d_skip,
    norm_gain,
):
    seq_count = lax.axis_size("seq")
    tiles_dev = ingest.shape[0]
    tile_len = ingest.shape[1]
    columns = ingest.shape[2]
    row_count = tiles_dev * tile_len
    heads_here = a_log.shape[0]
    inner_here = conv_x.shape[1]
    head_dim = inner_here // heads_here
    state_dim = conv_bc.shape[1] // 2
    taps = conv_x.shape[0]
    keep_rows = taps - 1
    owner = dest_tile // tiles_dev
    offset = dest_tile % tiles_dev
    slots = jnp.arange(seq_count, dtype=jnp.int32)
    pick = (owner[None, :] == slots[:, None]).astype(jnp.float32)
    outgoing = jnp.einsum(
        "sj,jrc->src", pick.astype(jnp.bfloat16), ingest, preferred_element_type=jnp.float32
    ).astype(jnp.bfloat16)
    marks = (
        jnp.dot(pick, (offset + 1).astype(jnp.float32), precision=lax.Precision.HIGHEST) - 1.0
    ).astype(jnp.bfloat16)
    incoming, got_marks = (
        lax.all_to_all(outgoing, "seq", split_axis=0, concat_axis=0, tiled=True),
        lax.all_to_all(marks, "seq", split_axis=0, concat_axis=0, tiled=True),
    )
    local_slots = jnp.arange(tiles_dev, dtype=jnp.float32)
    place = (got_marks.astype(jnp.float32)[None, :] == local_slots[:, None]).astype(jnp.bfloat16)
    arrived = jnp.einsum("js,src->jrc", place, incoming, preferred_element_type=jnp.float32).astype(
        jnp.bfloat16
    )
    own_rows = arrived.reshape(row_count, columns)
    zx_cols = w_zx.reshape(w_zx.shape[0], -1)
    weight_set = (zx_cols, w_bc, w_dt)
    piece = lax.all_gather(own_rows, "head", axis=1, tiled=True)
    acc_zx, acc_bc, acc_dt = tuple(
        (jnp.dot(piece, weight, preferred_element_type=jnp.float32) for weight in weight_set)
    )
    zx = acc_zx.astype(jnp.bfloat16)
    x_in = zx[:, inner_here:]
    bc_all = acc_bc.astype(jnp.bfloat16)
    step_dt = jax.nn.softplus(acc_dt + dt_bias[None, :])
    within = jnp.arange(tile_len, dtype=jnp.int32)
    has_bound = (doc_start < tile_len).astype(jnp.float32)
    before_count = jnp.cumsum(has_bound) - has_bound
    later = (within[None, :] >= doc_start[:, None]).astype(jnp.float32)
    segment = (before_count[:, None] + later).reshape(row_count)
    conv_in = jnp.concatenate([x_in, bc_all], 1)
    tail = conv_in[row_count - keep_rows :]
    tail_seg = (segment[row_count - keep_rows :] - segment[row_count - 1]).astype(jnp.bfloat16)
    got_tail, got_seg = shifted((tail, tail_seg), "seq", 1)
    extended = jnp.concatenate([got_tail, conv_in], 0)
    ext_seg = jnp.concatenate([got_seg.astype(jnp.float32), segment], 0)
    conv_weight = jnp.concatenate([conv_x, conv_bc], 1)
    conv_bias = jnp.concatenate([cbias_x, cbias_bc], 0)
    total = conv_bias[None, :] + conv_weight[taps - 1][None, :] * conv_in.astype(jnp.float32)
    for back_step in range(keep_rows):
        same = ext_seg[back_step : back_step + row_count] == segment
        total = total + jnp.where(
            same[:, None],
            conv_weight[back_step][None, :]
            * extended[back_step : back_step + row_count].astype(jnp.float32),
            0.0,
        )
    conv_out = jax.nn.silu(total).astype(jnp.bfloat16)
    rate = -jnp.exp(a_log)
    tile_dt = step_dt.reshape(tiles_dev, tile_len, heads_here)
    lower = (within[:, None] >= within[None, :]).astype(jnp.float32)
    cumul = jnp.einsum(
        "is,jsh->jih", lower, tile_dt * rate[None, None, :], precision=lax.Precision.HIGHEST
    )
    cumul_t = cumul.transpose(0, 2, 1)
    dt_t = tile_dt.transpose(0, 2, 1)
    last_part = later[:, tile_len - 1]
    tail_keep = (later == last_part[:, None]).astype(jnp.float32)
    to_end = jnp.exp(cumul[:, tile_len - 1 :, :] - cumul) * tile_dt * tail_keep[:, :, None]
    contrib = contrib_tiles(conv_out, to_end, inner_here, state_dim).reshape(
        tiles_dev, heads_here, head_dim, state_dim
    )
    passing = jnp.exp(cumul[:, tile_len - 1, :]) * (1.0 - has_bound)[:, None]
    through = jnp.cumprod(passing, 0)
    prefix = jnp.concatenate([jnp.ones((1, heads_here), jnp.float32), through[:-1]], 0)
    reverse = jnp.cumprod(passing[::-1], 0)[::-1]
    to_last = jnp.concatenate([reverse[1:], jnp.ones((1, heads_here), jnp.float32)], 0)
    run_state = jnp.sum(to_last[:, :, None, None] * contrib, 0)
    running = jnp.zeros((heads_here, head_dim, state_dim), jnp.float32)
    states = []
    for tile in range(tiles_dev):
        states.append(running)
        running = passing[tile][:, None, None] * running + contrib[tile]
    before_tile = jnp.stack(states)
    position = lax.axis_index("seq")
    run_decay = through[tiles_dev - 1]
    distance = 1
    while distance < seq_count:
        got_decay, got_state = shifted((run_decay, run_state), "seq", distance)
        run_state = run_state + run_decay[:, None, None] * got_state
        run_decay = jnp.where(position >= distance, run_decay * got_decay, run_decay)
        distance *= 2
    entering = shifted(run_state, "seq", 1)
    tile_state = before_tile + prefix[:, :, None, None] * entering[None]
    carried = tile_state.astype(jnp.bfloat16).reshape(tiles_dev, inner_here, state_dim)
    d_full = jnp.repeat(d_skip, head_dim)[None, :]
    gated, row_sq = mix_tiles(conv_out, zx, cumul, cumul_t, dt_t, later, carried, d_full)
    sums = lax.psum(row_sq, "head")
    return (gated * lax.rsqrt(sums / INNER + EPSILON) * norm_gain[None, :]).astype(jnp.bfloat16)


def solution(mesh):
    return jax.shard_map(
        shards,
        mesh=mesh,
        in_specs=(
            P("seq", None, "head"),
            P("seq"),
            P("seq"),
            P(None, None, "head"),
            P(),
            P(None, "head"),
            P("head"),
            P("head"),
            P(None, "head"),
            P(),
            P("head"),
            P(),
            P("head"),
            P("head"),
        ),
        out_specs=P("seq", "head"),
        check_vma=False,
    )
```

```python
import jax
import jax.numpy as jnp
from jax import lax
from jax.experimental import pallas as pl
from jax.experimental.pallas import tpu as pltpu
from jax.sharding import PartitionSpec as P

INNER = 2048


EPSILON = 1e-05


def shifted(x, axis, by):
    devices = lax.axis_size(axis)
    pairs = [(i, i + by) for i in range(devices) if 0 <= i + by < devices]
    return lax.ppermute(x, axis, pairs)


def mix_tile(
    x_ref, b_ref, c_ref, cum_ref, cumt_ref, dtt_ref, partc_ref, partr_ref, car_ref, gate_ref, d_ref,
    out_ref, sq_ref,
):
    f32 = jnp.float32
    tile_len = x_ref.shape[0]
    pairs = x_ref.shape[1] // 128
    b_mat = b_ref[...]
    c_mat = c_ref[...]
    scores = lax.dot_general(
        c_mat, b_mat, (((1,), (1,)), ((), ())), preferred_element_type=f32
    )
    cum = cum_ref[0]
    cumt = cumt_ref[0]
    dtt = dtt_ref[0]
    part_col = partc_ref[0]
    part_row = partr_ref[0]
    row = lax.broadcasted_iota(jnp.int32, (tile_len, tile_len), 0)
    col = lax.broadcasted_iota(jnp.int32, (tile_len, tile_len), 1)
    keep = (row >= col) & (part_col == part_row)
    earlier = 1.0 - part_col
    first_half = lax.broadcasted_iota(jnp.int32, (tile_len, 128), 1) < 64
    total_sq = jnp.zeros((tile_len, 128), f32)
    for pair in range(pairs):
        cols = pl.ds(pair * 128, 128)
        x_pair = x_ref[:, cols]
        slabs = []
        for half in range(2):
            head = 2 * pair + half
            diff = cum[:, head : head + 1] - cumt[head : head + 1, :]
            decay = jnp.where(keep, jnp.exp(jnp.where(keep, diff, 0.0)), 0.0)
            slabs.append((scores * decay * dtt[head : head + 1, :]).astype(jnp.bfloat16))
        weights = jnp.concatenate(slabs, axis=1)
        zero = jnp.zeros_like(x_pair)
        split_x = jnp.concatenate(
            [jnp.where(first_half, x_pair, zero), jnp.where(first_half, zero, x_pair)], axis=0
        )
        intra = jnp.dot(weights, split_x, preferred_element_type=f32)
        projected = jnp.dot(c_mat, car_ref[0, :, cols], preferred_element_type=f32)
        grow = jnp.where(
            first_half,
            jnp.exp(cum[:, 2 * pair : 2 * pair + 1]),
            jnp.exp(cum[:, 2 * pair + 1 : 2 * pair + 2]),
        )
        inter = grow * earlier * projected
        mixed = intra + inter + d_ref[:, cols] * x_pair.astype(f32)
        gate = gate_ref[:, cols].astype(f32)
        gated = mixed * (gate * (0.5 + 0.5 * jnp.tanh(0.5 * gate)))
        out_ref[:, cols] = gated
        total_sq = total_sq + gated * gated
    sq_ref[...] = jnp.sum(total_sq, axis=1, keepdims=True)


def contrib_tile(x_ref, bt_ref, end_ref, out_ref):
    f32 = jnp.float32
    tile_len = x_ref.shape[0]
    pairs = x_ref.shape[1] // 128
    b_t = bt_ref[0]
    to_end = end_ref[0]
    first_half = lax.broadcasted_iota(jnp.int32, (tile_len, 128), 1) < 64
    for pair in range(pairs):
        cols = pl.ds(pair * 128, 128)
        scale = jnp.where(
            first_half, to_end[:, 2 * pair : 2 * pair + 1], to_end[:, 2 * pair + 1 : 2 * pair + 2]
        )
        scaled = (x_ref[:, cols].astype(f32) * scale).astype(jnp.bfloat16)
        out_ref[0, :, cols] = jnp.dot(b_t, scaled, preferred_element_type=f32)


def contrib_tiles(conv_out, b_t, to_end, inner_here, state_dim):
    tiles_dev, tile_len, heads_here = to_end.shape
    return pl.pallas_call(
        contrib_tile,
        grid=(tiles_dev,),
        in_specs=[
            pl.BlockSpec((tile_len, inner_here), lambda j: (j, 0)),
            pl.BlockSpec((1, state_dim, tile_len), lambda j: (j, 0, 0)),
            pl.BlockSpec((1, tile_len, heads_here), lambda j: (j, 0, 0)),
        ],
        out_specs=pl.BlockSpec((1, state_dim, inner_here), lambda j: (j, 0, 0)),
        out_shape=jax.ShapeDtypeStruct((tiles_dev, state_dim, inner_here), jnp.float32),
        cost_estimate=pl.CostEstimate(
            flops=tiles_dev * 2 * tile_len * inner_here * state_dim,
            transcendentals=0,
            bytes_accessed=tiles_dev * (tile_len * (inner_here + state_dim) * 2 + inner_here * state_dim * 4),
        ),
    )(conv_out, b_t, to_end)


def mix_tiles(conv_out, zx, cumul, cumul_t, dt_t, later, carried, d_full):
    tiles_dev, tile_len, heads_here = cumul.shape
    inner_here = carried.shape[2]
    state_dim = carried.shape[1]
    rows = tiles_dev * tile_len
    b_block = inner_here // 128
    c_block = b_block + state_dim // 128
    part_col = later.reshape(tiles_dev, tile_len, 1)
    part_row = later.reshape(tiles_dev, 1, tile_len)
    per_tile = lambda j: (j, 0, 0)
    return pl.pallas_call(
        mix_tile,
        grid=(tiles_dev,),
        in_specs=[
            pl.BlockSpec((tile_len, inner_here), lambda j: (j, 0)),
            pl.BlockSpec((tile_len, state_dim), lambda j: (j, b_block)),
            pl.BlockSpec((tile_len, state_dim), lambda j: (j, c_block)),
            pl.BlockSpec((1, tile_len, heads_here), per_tile),
            pl.BlockSpec((1, heads_here, tile_len), per_tile),
            pl.BlockSpec((1, heads_here, tile_len), per_tile),
            pl.BlockSpec((1, tile_len, 1), per_tile),
            pl.BlockSpec((1, 1, tile_len), per_tile),
            pl.BlockSpec((1, state_dim, inner_here), per_tile),
            pl.BlockSpec((tile_len, inner_here), lambda j: (j, 0)),
            pl.BlockSpec((1, inner_here), lambda j: (0, 0)),
        ],
        out_specs=[
            pl.BlockSpec((tile_len, inner_here), lambda j: (j, 0)),
            pl.BlockSpec((tile_len, 1), lambda j: (j, 0)),
        ],
        out_shape=[
            jax.ShapeDtypeStruct((rows, inner_here), jnp.float32),
            jax.ShapeDtypeStruct((rows, 1), jnp.float32),
        ],
        cost_estimate=pl.CostEstimate(
            flops=tiles_dev * (2 * tile_len * tile_len * (state_dim + 4 * inner_here + 2 * inner_here)),
            transcendentals=tiles_dev * tile_len * (tile_len * heads_here + 2 * inner_here),
            bytes_accessed=rows * inner_here * 10 + tiles_dev * inner_here * state_dim * 2,
        ),
    )(conv_out, conv_out, conv_out, cumul, cumul_t, dt_t, part_col, part_row, carried, zx, d_full)


def shards(
    ingest,
    dest_tile,
    doc_start,
    w_zx,
    w_bc,
    w_dt,
    dt_bias,
    a_log,
    conv_x,
    conv_bc,
    cbias_x,
    cbias_bc,
    d_skip,
    norm_gain,
):
    seq_count = lax.axis_size("seq")
    tiles_dev = ingest.shape[0]
    tile_len = ingest.shape[1]
    columns = ingest.shape[2]
    row_count = tiles_dev * tile_len
    heads_here = a_log.shape[0]
    inner_here = conv_x.shape[1]
    head_dim = inner_here // heads_here
    state_dim = conv_bc.shape[1] // 2
    taps = conv_x.shape[0]
    keep_rows = taps - 1
    owner = dest_tile // tiles_dev
    offset = dest_tile % tiles_dev
    slots = jnp.arange(seq_count, dtype=jnp.int32)
    pick = (owner[None, :] == slots[:, None]).astype(jnp.float32)
    outgoing = jnp.einsum(
        "sj,jrc->src", pick.astype(jnp.bfloat16), ingest, preferred_element_type=jnp.float32
    ).astype(jnp.bfloat16)
    marks = (
        jnp.dot(pick, (offset + 1).astype(jnp.float32), precision=lax.Precision.HIGHEST) - 1.0
    ).astype(jnp.bfloat16)
    incoming, got_marks = (
        lax.all_to_all(outgoing, "seq", split_axis=0, concat_axis=0, tiled=True),
        lax.all_to_all(marks, "seq", split_axis=0, concat_axis=0, tiled=True),
    )
    local_slots = jnp.arange(tiles_dev, dtype=jnp.float32)
    place = (got_marks.astype(jnp.float32)[None, :] == local_slots[:, None]).astype(jnp.bfloat16)
    arrived = jnp.einsum("js,src->jrc", place, incoming, preferred_element_type=jnp.float32).astype(
        jnp.bfloat16
    )
    own_rows = arrived.reshape(row_count, columns)
    zx_cols = w_zx.reshape(w_zx.shape[0], -1)
    weight_set = (zx_cols, w_bc, w_dt)
    piece = lax.all_gather(own_rows, "head", axis=1, tiled=True)
    acc_zx, acc_bc, acc_dt = tuple(
        (jnp.dot(piece, weight, preferred_element_type=jnp.float32) for weight in weight_set)
    )
    zx = acc_zx.astype(jnp.bfloat16)
    x_in = zx[:, inner_here:]
    bc_all = acc_bc.astype(jnp.bfloat16)
    step_dt = jax.nn.softplus(acc_dt + dt_bias[None, :])
    within = jnp.arange(tile_len, dtype=jnp.int32)
    has_bound = (doc_start < tile_len).astype(jnp.float32)
    before_count = jnp.cumsum(has_bound) - has_bound
    later = (within[None, :] >= doc_start[:, None]).astype(jnp.float32)
    segment = (before_count[:, None] + later).reshape(row_count)
    conv_in = jnp.concatenate([x_in, bc_all], 1)
    tail = conv_in[row_count - keep_rows :]
    tail_seg = (segment[row_count - keep_rows :] - segment[row_count - 1]).astype(jnp.bfloat16)
    got_tail, got_seg = shifted((tail, tail_seg), "seq", 1)
    extended = jnp.concatenate([got_tail, conv_in], 0)
    ext_seg = jnp.concatenate([got_seg.astype(jnp.float32), segment], 0)
    conv_weight = jnp.concatenate([conv_x, conv_bc], 1)
    conv_bias = jnp.concatenate([cbias_x, cbias_bc], 0)
    total = conv_bias[None, :] + conv_weight[taps - 1][None, :] * conv_in.astype(jnp.float32)
    for back_step in range(keep_rows):
        same = ext_seg[back_step : back_step + row_count] == segment
        total = total + jnp.where(
            same[:, None],
            conv_weight[back_step][None, :]
            * extended[back_step : back_step + row_count].astype(jnp.float32),
            0.0,
        )
    conv_out = jax.nn.silu(total).astype(jnp.bfloat16)
    rate = -jnp.exp(a_log)
    tile_dt = step_dt.reshape(tiles_dev, tile_len, heads_here)
    lower = (within[:, None] >= within[None, :]).astype(jnp.float32)
    cumul = jnp.einsum(
        "is,jsh->jih", lower, tile_dt * rate[None, None, :], precision=lax.Precision.HIGHEST
    )
    cumul_t = cumul.transpose(0, 2, 1)
    dt_t = tile_dt.transpose(0, 2, 1)
    last_part = later[:, tile_len - 1]
    tail_keep = (later == last_part[:, None]).astype(jnp.float32)
    to_end = jnp.exp(cumul[:, tile_len - 1 :, :] - cumul) * tile_dt * tail_keep[:, :, None]
    b_t = conv_out[:, inner_here : inner_here + state_dim].reshape(
        tiles_dev, tile_len, state_dim
    ).transpose(0, 2, 1)
    contrib = contrib_tiles(conv_out, b_t, to_end, inner_here, state_dim)
    passing = jnp.exp(cumul[:, tile_len - 1, :]) * (1.0 - has_bound)[:, None]
    through = jnp.cumprod(passing, 0)
    prefix = jnp.concatenate([jnp.ones((1, heads_here), jnp.float32), through[:-1]], 0)
    reverse = jnp.cumprod(passing[::-1], 0)[::-1]
    to_last = jnp.concatenate([reverse[1:], jnp.ones((1, heads_here), jnp.float32)], 0)
    widen = lambda per_head: jnp.repeat(per_head, head_dim, axis=-1)
    run_state = jnp.sum(widen(to_last)[:, None, :] * contrib, 0)
    passing_wide = widen(passing)
    running = jnp.zeros((state_dim, inner_here), jnp.float32)
    states = []
    for tile in range(tiles_dev):
        states.append(running)
        running = passing_wide[tile][None, :] * running + contrib[tile]
    before_tile = jnp.stack(states)
    position = lax.axis_index("seq")
    run_decay = widen(through[tiles_dev - 1])
    distance = 1
    while distance < seq_count:
        got_decay, got_state = shifted((run_decay, run_state), "seq", distance)
        run_state = run_state + run_decay[None, :] * got_state
        run_decay = jnp.where(position >= distance, run_decay * got_decay, run_decay)
        distance *= 2
    entering = shifted(run_state, "seq", 1)
    tile_state = before_tile + widen(prefix)[:, None, :] * entering[None]
    carried = tile_state.astype(jnp.bfloat16)
    d_full = jnp.repeat(d_skip, head_dim)[None, :]
    gated, row_sq = mix_tiles(conv_out, zx, cumul, cumul_t, dt_t, later, carried, d_full)
    sums = lax.psum(row_sq, "head")
    return (gated * lax.rsqrt(sums / INNER + EPSILON) * norm_gain[None, :]).astype(jnp.bfloat16)


def solution(mesh):
    return jax.shard_map(
        shards,
        mesh=mesh,
        in_specs=(
            P("seq", None, "head"),
            P("seq"),
            P("seq"),
            P(None, None, "head"),
            P(),
            P(None, "head"),
            P("head"),
            P("head"),
            P(None, "head"),
            P(),
            P("head"),
            P(),
            P("head"),
            P("head"),
        ),
        out_specs=P("seq", "head"),
        check_vma=False,
    )
```

```python
import jax
import jax.numpy as jnp
from jax import lax
from jax.experimental import pallas as pl
from jax.experimental.pallas import tpu as pltpu
from jax.sharding import PartitionSpec as P

INNER = 2048


EPSILON = 1e-05


def shifted(x, axis, by):
    devices = lax.axis_size(axis)
    pairs = [(i, i + by) for i in range(devices) if 0 <= i + by < devices]
    return lax.ppermute(x, axis, pairs)


def intra_tile(x_ref, b_ref, c_ref, cumc_ref, cumt_ref, dtt_ref, partc_ref, partr_ref, d_ref, out_ref):
    f32 = jnp.float32
    tile_len = x_ref.shape[0]
    pairs = x_ref.shape[1] // 128
    scores = lax.dot_general(
        c_ref[...], b_ref[...], (((1,), (1,)), ((), ())), preferred_element_type=f32
    )
    cum = cumc_ref[0]
    cumt = cumt_ref[0]
    dtt = dtt_ref[0]
    row = lax.broadcasted_iota(jnp.int32, (tile_len, tile_len), 0)
    col = lax.broadcasted_iota(jnp.int32, (tile_len, tile_len), 1)
    keep = (row >= col) & (partc_ref[0] == partr_ref[0])
    first_half = lax.broadcasted_iota(jnp.int32, (tile_len, 128), 1) < 64
    for pair in range(pairs):
        cols = pl.ds(pair * 128, 128)
        x_pair = x_ref[:, cols]
        slabs = []
        for half in range(2):
            head = 2 * pair + half
            diff = cum[:, head : head + 1] - cumt[head : head + 1, :]
            decay = jnp.where(keep, jnp.exp(jnp.where(keep, diff, 0.0)), 0.0)
            slabs.append((scores * decay * dtt[head : head + 1, :]).astype(jnp.bfloat16))
        weights = jnp.concatenate(slabs, axis=1)
        zero = jnp.zeros_like(x_pair)
        split_x = jnp.concatenate(
            [jnp.where(first_half, x_pair, zero), jnp.where(first_half, zero, x_pair)], axis=0
        )
        intra = jnp.dot(weights, split_x, preferred_element_type=f32)
        out_ref[:, cols] = intra + d_ref[:, cols] * x_pair.astype(f32)


def finish_tile(part_ref, c_ref, cumc_ref, partc_ref, car_ref, gate_ref, out_ref, sq_ref):
    f32 = jnp.float32
    tile_len = part_ref.shape[0]
    pairs = part_ref.shape[1] // 128
    c_mat = c_ref[...]
    cum = cumc_ref[0]
    earlier = 1.0 - partc_ref[0]
    first_half = lax.broadcasted_iota(jnp.int32, (tile_len, 128), 1) < 64
    total_sq = jnp.zeros((tile_len, 128), f32)
    for pair in range(pairs):
        cols = pl.ds(pair * 128, 128)
        projected = jnp.dot(c_mat, car_ref[0, :, cols], preferred_element_type=f32)
        grow = jnp.where(
            first_half,
            jnp.exp(cum[:, 2 * pair : 2 * pair + 1]),
            jnp.exp(cum[:, 2 * pair + 1 : 2 * pair + 2]),
        )
        mixed = part_ref[:, cols] + grow * earlier * projected
        gate = gate_ref[:, cols].astype(f32)
        gated = mixed * (gate * (0.5 + 0.5 * jnp.tanh(0.5 * gate)))
        out_ref[:, cols] = gated
        total_sq = total_sq + gated * gated
    sq_ref[...] = jnp.sum(total_sq, axis=1, keepdims=True)


def contrib_tile(x_ref, bt_ref, end_ref, out_ref):
    f32 = jnp.float32
    tile_len = x_ref.shape[0]
    pairs = x_ref.shape[1] // 128
    b_t = bt_ref[0]
    to_end = end_ref[0]
    first_half = lax.broadcasted_iota(jnp.int32, (tile_len, 128), 1) < 64
    for pair in range(pairs):
        cols = pl.ds(pair * 128, 128)
        scale = jnp.where(
            first_half, to_end[:, 2 * pair : 2 * pair + 1], to_end[:, 2 * pair + 1 : 2 * pair + 2]
        )
        scaled = (x_ref[:, cols].astype(f32) * scale).astype(jnp.bfloat16)
        out_ref[0, :, cols] = jnp.dot(b_t, scaled, preferred_element_type=f32)


def contrib_tiles(conv_out, b_t, to_end, inner_here, state_dim):
    tiles_dev, tile_len, heads_here = to_end.shape
    return pl.pallas_call(
        contrib_tile,
        grid=(tiles_dev,),
        in_specs=[
            pl.BlockSpec((tile_len, inner_here), lambda j: (j, 0)),
            pl.BlockSpec((1, state_dim, tile_len), lambda j: (j, 0, 0)),
            pl.BlockSpec((1, tile_len, heads_here), lambda j: (j, 0, 0)),
        ],
        out_specs=pl.BlockSpec((1, state_dim, inner_here), lambda j: (j, 0, 0)),
        out_shape=jax.ShapeDtypeStruct((tiles_dev, state_dim, inner_here), jnp.float32),
        cost_estimate=pl.CostEstimate(
            flops=tiles_dev * 2 * tile_len * inner_here * state_dim,
            transcendentals=0,
            bytes_accessed=tiles_dev * (tile_len * (inner_here + state_dim) * 2 + inner_here * state_dim * 4),
        ),
    )(conv_out, b_t, to_end)


def intra_tiles(conv_out, cumul, cumul_t, dt_t, later, d_full):
    tiles_dev, tile_len, heads_here = cumul.shape
    inner_here = d_full.shape[1]
    state_dim = 128
    rows = tiles_dev * tile_len
    b_block = inner_here // 128
    c_block = b_block + 1
    per_tile = lambda j: (j, 0, 0)
    return pl.pallas_call(
        intra_tile,
        grid=(tiles_dev,),
        in_specs=[
            pl.BlockSpec((tile_len, inner_here), lambda j: (j, 0)),
            pl.BlockSpec((tile_len, state_dim), lambda j: (j, b_block)),
            pl.BlockSpec((tile_len, state_dim), lambda j: (j, c_block)),
            pl.BlockSpec((1, tile_len, heads_here), per_tile),
            pl.BlockSpec((1, heads_here, tile_len), per_tile),
            pl.BlockSpec((1, heads_here, tile_len), per_tile),
            pl.BlockSpec((1, tile_len, 1), per_tile),
            pl.BlockSpec((1, 1, tile_len), per_tile),
            pl.BlockSpec((1, inner_here), lambda j: (0, 0)),
        ],
        out_specs=pl.BlockSpec((tile_len, inner_here), lambda j: (j, 0)),
        out_shape=jax.ShapeDtypeStruct((rows, inner_here), jnp.float32),
        cost_estimate=pl.CostEstimate(
            flops=tiles_dev * 2 * tile_len * tile_len * (state_dim + 4 * inner_here),
            transcendentals=tiles_dev * tile_len * tile_len * heads_here,
            bytes_accessed=rows * inner_here * 6,
        ),
    )(
        conv_out, conv_out, conv_out, cumul, cumul_t, dt_t,
        later.reshape(tiles_dev, tile_len, 1), later.reshape(tiles_dev, 1, tile_len), d_full,
    )


def finish_tiles(partial, conv_out, zx, cumul, later, carried):
    tiles_dev, tile_len, heads_here = cumul.shape
    state_dim, inner_here = carried.shape[1], carried.shape[2]
    rows = tiles_dev * tile_len
    c_block = inner_here // 128 + 1
    per_tile = lambda j: (j, 0, 0)
    return pl.pallas_call(
        finish_tile,
        grid=(tiles_dev,),
        in_specs=[
            pl.BlockSpec((tile_len, inner_here), lambda j: (j, 0)),
            pl.BlockSpec((tile_len, state_dim), lambda j: (j, c_block)),
            pl.BlockSpec((1, tile_len, heads_here), per_tile),
            pl.BlockSpec((1, tile_len, 1), per_tile),
            pl.BlockSpec((1, state_dim, inner_here), per_tile),
            pl.BlockSpec((tile_len, inner_here), lambda j: (j, 0)),
        ],
        out_specs=[
            pl.BlockSpec((tile_len, inner_here), lambda j: (j, 0)),
            pl.BlockSpec((tile_len, 1), lambda j: (j, 0)),
        ],
        out_shape=[
            jax.ShapeDtypeStruct((rows, inner_here), jnp.float32),
            jax.ShapeDtypeStruct((rows, 1), jnp.float32),
        ],
        cost_estimate=pl.CostEstimate(
            flops=tiles_dev * 2 * tile_len * state_dim * inner_here,
            transcendentals=rows * inner_here * 2,
            bytes_accessed=rows * inner_here * 10 + tiles_dev * inner_here * state_dim * 2,
        ),
    )(partial, conv_out, cumul, later.reshape(tiles_dev, tile_len, 1), carried, zx)

def shards(
    ingest,
    dest_tile,
    doc_start,
    w_zx,
    w_bc,
    w_dt,
    dt_bias,
    a_log,
    conv_x,
    conv_bc,
    cbias_x,
    cbias_bc,
    d_skip,
    norm_gain,
):
    seq_count = lax.axis_size("seq")
    tiles_dev = ingest.shape[0]
    tile_len = ingest.shape[1]
    columns = ingest.shape[2]
    row_count = tiles_dev * tile_len
    heads_here = a_log.shape[0]
    inner_here = conv_x.shape[1]
    head_dim = inner_here // heads_here
    state_dim = conv_bc.shape[1] // 2
    taps = conv_x.shape[0]
    keep_rows = taps - 1
    owner = dest_tile // tiles_dev
    offset = dest_tile % tiles_dev
    slots = jnp.arange(seq_count, dtype=jnp.int32)
    pick = (owner[None, :] == slots[:, None]).astype(jnp.float32)
    outgoing = jnp.einsum(
        "sj,jrc->src", pick.astype(jnp.bfloat16), ingest, preferred_element_type=jnp.float32
    ).astype(jnp.bfloat16)
    marks = (
        jnp.dot(pick, (offset + 1).astype(jnp.float32), precision=lax.Precision.HIGHEST) - 1.0
    ).astype(jnp.bfloat16)
    incoming, got_marks = (
        lax.all_to_all(outgoing, "seq", split_axis=0, concat_axis=0, tiled=True),
        lax.all_to_all(marks, "seq", split_axis=0, concat_axis=0, tiled=True),
    )
    local_slots = jnp.arange(tiles_dev, dtype=jnp.float32)
    place = (got_marks.astype(jnp.float32)[None, :] == local_slots[:, None]).astype(jnp.bfloat16)
    arrived = jnp.einsum("js,src->jrc", place, incoming, preferred_element_type=jnp.float32).astype(
        jnp.bfloat16
    )
    own_rows = arrived.reshape(row_count, columns)
    zx_cols = w_zx.reshape(w_zx.shape[0], -1)
    weight_set = (zx_cols, w_bc, w_dt)
    piece = lax.all_gather(own_rows, "head", axis=1, tiled=True)
    acc_zx, acc_bc, acc_dt = tuple(
        (jnp.dot(piece, weight, preferred_element_type=jnp.float32) for weight in weight_set)
    )
    zx = acc_zx.astype(jnp.bfloat16)
    x_in = zx[:, inner_here:]
    bc_all = acc_bc.astype(jnp.bfloat16)
    step_dt = jax.nn.softplus(acc_dt + dt_bias[None, :])
    within = jnp.arange(tile_len, dtype=jnp.int32)
    has_bound = (doc_start < tile_len).astype(jnp.float32)
    before_count = jnp.cumsum(has_bound) - has_bound
    later = (within[None, :] >= doc_start[:, None]).astype(jnp.float32)
    segment = (before_count[:, None] + later).reshape(row_count)
    conv_in = jnp.concatenate([x_in, bc_all], 1)
    tail = conv_in[row_count - keep_rows :]
    tail_seg = (segment[row_count - keep_rows :] - segment[row_count - 1]).astype(jnp.bfloat16)
    got_tail, got_seg = shifted((tail, tail_seg), "seq", 1)
    extended = jnp.concatenate([got_tail, conv_in], 0)
    ext_seg = jnp.concatenate([got_seg.astype(jnp.float32), segment], 0)
    conv_weight = jnp.concatenate([conv_x, conv_bc], 1)
    conv_bias = jnp.concatenate([cbias_x, cbias_bc], 0)
    total = conv_bias[None, :] + conv_weight[taps - 1][None, :] * conv_in.astype(jnp.float32)
    for back_step in range(keep_rows):
        same = ext_seg[back_step : back_step + row_count] == segment
        total = total + jnp.where(
            same[:, None],
            conv_weight[back_step][None, :]
            * extended[back_step : back_step + row_count].astype(jnp.float32),
            0.0,
        )
    conv_out = jax.nn.silu(total).astype(jnp.bfloat16)
    rate = -jnp.exp(a_log)
    tile_dt = step_dt.reshape(tiles_dev, tile_len, heads_here)
    lower = (within[:, None] >= within[None, :]).astype(jnp.float32)
    cumul = jnp.einsum(
        "is,jsh->jih", lower, tile_dt * rate[None, None, :], precision=lax.Precision.HIGHEST
    )
    cumul_t = cumul.transpose(0, 2, 1)
    dt_t = tile_dt.transpose(0, 2, 1)
    last_part = later[:, tile_len - 1]
    tail_keep = (later == last_part[:, None]).astype(jnp.float32)
    to_end = jnp.exp(cumul[:, tile_len - 1 :, :] - cumul) * tile_dt * tail_keep[:, :, None]
    b_t = conv_out[:, inner_here : inner_here + state_dim].reshape(
        tiles_dev, tile_len, state_dim
    ).transpose(0, 2, 1)
    contrib = contrib_tiles(conv_out, b_t, to_end, inner_here, state_dim)
    passing = jnp.exp(cumul[:, tile_len - 1, :]) * (1.0 - has_bound)[:, None]
    through = jnp.cumprod(passing, 0)
    prefix = jnp.concatenate([jnp.ones((1, heads_here), jnp.float32), through[:-1]], 0)
    reverse = jnp.cumprod(passing[::-1], 0)[::-1]
    to_last = jnp.concatenate([reverse[1:], jnp.ones((1, heads_here), jnp.float32)], 0)
    widen = lambda per_head: jnp.repeat(per_head, head_dim, axis=-1)
    run_state = jnp.sum(widen(to_last)[:, None, :] * contrib, 0)
    passing_wide = widen(passing)
    running = jnp.zeros((state_dim, inner_here), jnp.float32)
    states = []
    for tile in range(tiles_dev):
        states.append(running)
        running = passing_wide[tile][None, :] * running + contrib[tile]
    before_tile = jnp.stack(states)
    d_full = jnp.repeat(d_skip, head_dim)[None, :]
    partial = intra_tiles(conv_out, cumul, cumul_t, dt_t, later, d_full)
    position = lax.axis_index("seq")
    all_decay = widen(through[tiles_dev - 1])
    halves = []
    width = inner_here // 2
    for group in range(2):
        run_decay = all_decay[group * width : (group + 1) * width]
        group_state = run_state[:, group * width : (group + 1) * width]
        distance = 1
        while distance < seq_count:
            got_decay, got_state = shifted((run_decay, group_state), "seq", distance)
            group_state = group_state + run_decay[None, :] * got_state
            run_decay = jnp.where(position >= distance, run_decay * got_decay, run_decay)
            distance *= 2
        halves.append(shifted(group_state, "seq", 1))
    entering = jnp.concatenate(halves, 1)
    tile_state = before_tile + widen(prefix)[:, None, :] * entering[None]
    carried = tile_state.astype(jnp.bfloat16)
    gated, row_sq = finish_tiles(partial, conv_out, zx, cumul, later, carried)
    sums = lax.psum(row_sq, "head")
    return (gated * lax.rsqrt(sums / INNER + EPSILON) * norm_gain[None, :]).astype(jnp.bfloat16)


def solution(mesh):
    return jax.shard_map(
        shards,
        mesh=mesh,
        in_specs=(
            P("seq", None, "head"),
            P("seq"),
            P("seq"),
            P(None, None, "head"),
            P(),
            P(None, "head"),
            P("head"),
            P("head"),
            P(None, "head"),
            P(),
            P("head"),
            P(),
            P("head"),
            P("head"),
        ),
        out_specs=P("seq", "head"),
        check_vma=False,
    )
```

```python
import jax
import jax.numpy as jnp
from jax import lax
from jax.experimental import pallas as pl
from jax.experimental.pallas import tpu as pltpu
from jax.sharding import PartitionSpec as P

INNER = 2048


EPSILON = 1e-05


def shifted(x, axis, by):
    devices = lax.axis_size(axis)
    pairs = [(i, i + by) for i in range(devices) if 0 <= i + by < devices]
    return lax.ppermute(x, axis, pairs)


def mix_tile(
    x_ref, b_ref, c_ref, cum_ref, cumt_ref, dtt_ref, partc_ref, partr_ref, car_ref, gate_ref, d_ref,
    out_ref, sq_ref,
):
    f32 = jnp.float32
    tile_len = x_ref.shape[0]
    pairs = x_ref.shape[1] // 128
    b_mat = b_ref[...]
    c_mat = c_ref[...]
    scores = lax.dot_general(
        c_mat, b_mat, (((1,), (1,)), ((), ())), preferred_element_type=f32
    )
    cum = cum_ref[0]
    cumt = cumt_ref[0]
    dtt = dtt_ref[0]
    part_col = partc_ref[0]
    part_row = partr_ref[0]
    row = lax.broadcasted_iota(jnp.int32, (tile_len, tile_len), 0)
    col = lax.broadcasted_iota(jnp.int32, (tile_len, tile_len), 1)
    keep = (row >= col) & (part_col == part_row)
    earlier = 1.0 - part_col
    first_half = lax.broadcasted_iota(jnp.int32, (tile_len, 128), 1) < 64
    total_sq = jnp.zeros((tile_len, 128), f32)
    for pair in range(pairs):
        cols = pl.ds(pair * 128, 128)
        x_pair = x_ref[:, cols]
        slabs = []
        for half in range(2):
            head = 2 * pair + half
            diff = cum[:, head : head + 1] - cumt[head : head + 1, :]
            decay = jnp.where(keep, jnp.exp(jnp.where(keep, diff, 0.0)), 0.0)
            slabs.append((scores * decay * dtt[head : head + 1, :]).astype(jnp.bfloat16))
        weights = jnp.concatenate(slabs, axis=1)
        zero = jnp.zeros_like(x_pair)
        split_x = jnp.concatenate(
            [jnp.where(first_half, x_pair, zero), jnp.where(first_half, zero, x_pair)], axis=0
        )
        intra = jnp.dot(weights, split_x, preferred_element_type=f32)
        projected = jnp.dot(c_mat, car_ref[0, :, cols], preferred_element_type=f32)
        grow = jnp.where(
            first_half,
            jnp.exp(cum[:, 2 * pair : 2 * pair + 1]),
            jnp.exp(cum[:, 2 * pair + 1 : 2 * pair + 2]),
        )
        inter = grow * earlier * projected
        mixed = intra + inter + d_ref[:, cols] * x_pair.astype(f32)
        gate = gate_ref[:, cols].astype(f32)
        gated = mixed * (gate * (0.5 + 0.5 * jnp.tanh(0.5 * gate)))
        out_ref[:, cols] = gated
        total_sq = total_sq + gated * gated
    sq_ref[...] = jnp.sum(total_sq, axis=1, keepdims=True)


def contrib_tile(x_ref, bt_ref, end_ref, out_ref):
    f32 = jnp.float32
    tile_len = x_ref.shape[0]
    pairs = x_ref.shape[1] // 128
    b_t = bt_ref[0]
    to_end = end_ref[0]
    first_half = lax.broadcasted_iota(jnp.int32, (tile_len, 128), 1) < 64
    for pair in range(pairs):
        cols = pl.ds(pair * 128, 128)
        scale = jnp.where(
            first_half, to_end[:, 2 * pair : 2 * pair + 1], to_end[:, 2 * pair + 1 : 2 * pair + 2]
        )
        scaled = (x_ref[:, cols].astype(f32) * scale).astype(jnp.bfloat16)
        out_ref[0, :, cols] = jnp.dot(b_t, scaled, preferred_element_type=f32)


def contrib_tiles(conv_out, b_t, to_end, inner_here, state_dim):
    tiles_dev, tile_len, heads_here = to_end.shape
    return pl.pallas_call(
        contrib_tile,
        grid=(tiles_dev,),
        in_specs=[
            pl.BlockSpec((tile_len, inner_here), lambda j: (j, 0)),
            pl.BlockSpec((1, state_dim, tile_len), lambda j: (j, 0, 0)),
            pl.BlockSpec((1, tile_len, heads_here), lambda j: (j, 0, 0)),
        ],
        out_specs=pl.BlockSpec((1, state_dim, inner_here), lambda j: (j, 0, 0)),
        out_shape=jax.ShapeDtypeStruct((tiles_dev, state_dim, inner_here), jnp.float32),
        cost_estimate=pl.CostEstimate(
            flops=tiles_dev * 2 * tile_len * inner_here * state_dim,
            transcendentals=0,
            bytes_accessed=tiles_dev * (tile_len * (inner_here + state_dim) * 2 + inner_here * state_dim * 4),
        ),
    )(conv_out, b_t, to_end)


def mix_tiles(conv_out, zx, cumul, cumul_t, dt_t, later, carried, d_full):
    tiles_dev, tile_len, heads_here = cumul.shape
    inner_here = carried.shape[2]
    state_dim = carried.shape[1]
    rows = tiles_dev * tile_len
    b_block = inner_here // 128
    c_block = b_block + state_dim // 128
    part_col = later.reshape(tiles_dev, tile_len, 1)
    part_row = later.reshape(tiles_dev, 1, tile_len)
    per_tile = lambda j: (j, 0, 0)
    return pl.pallas_call(
        mix_tile,
        grid=(tiles_dev,),
        in_specs=[
            pl.BlockSpec((tile_len, inner_here), lambda j: (j, 0)),
            pl.BlockSpec((tile_len, state_dim), lambda j: (j, b_block)),
            pl.BlockSpec((tile_len, state_dim), lambda j: (j, c_block)),
            pl.BlockSpec((1, tile_len, heads_here), per_tile),
            pl.BlockSpec((1, heads_here, tile_len), per_tile),
            pl.BlockSpec((1, heads_here, tile_len), per_tile),
            pl.BlockSpec((1, tile_len, 1), per_tile),
            pl.BlockSpec((1, 1, tile_len), per_tile),
            pl.BlockSpec((1, state_dim, inner_here), per_tile),
            pl.BlockSpec((tile_len, inner_here), lambda j: (j, 0)),
            pl.BlockSpec((1, inner_here), lambda j: (0, 0)),
        ],
        out_specs=[
            pl.BlockSpec((tile_len, inner_here), lambda j: (j, 0)),
            pl.BlockSpec((tile_len, 1), lambda j: (j, 0)),
        ],
        out_shape=[
            jax.ShapeDtypeStruct((rows, inner_here), jnp.float32),
            jax.ShapeDtypeStruct((rows, 1), jnp.float32),
        ],
        cost_estimate=pl.CostEstimate(
            flops=tiles_dev * (2 * tile_len * tile_len * (state_dim + 4 * inner_here + 2 * inner_here)),
            transcendentals=tiles_dev * tile_len * (tile_len * heads_here + 2 * inner_here),
            bytes_accessed=rows * inner_here * 10 + tiles_dev * inner_here * state_dim * 2,
        ),
    )(conv_out, conv_out, conv_out, cumul, cumul_t, dt_t, part_col, part_row, carried, zx, d_full)


def shards(
    ingest,
    dest_tile,
    doc_start,
    w_zx,
    w_bc,
    w_dt,
    dt_bias,
    a_log,
    conv_x,
    conv_bc,
    cbias_x,
    cbias_bc,
    d_skip,
    norm_gain,
):
    seq_count = lax.axis_size("seq")
    tiles_dev = ingest.shape[0]
    tile_len = ingest.shape[1]
    columns = ingest.shape[2]
    row_count = tiles_dev * tile_len
    heads_here = a_log.shape[0]
    inner_here = conv_x.shape[1]
    head_dim = inner_here // heads_here
    state_dim = conv_bc.shape[1] // 2
    taps = conv_x.shape[0]
    keep_rows = taps - 1
    owner = dest_tile // tiles_dev
    offset = dest_tile % tiles_dev
    slots = jnp.arange(seq_count, dtype=jnp.int32)
    pick = (owner[None, :] == slots[:, None]).astype(jnp.float32)
    outgoing = jnp.einsum(
        "sj,jrc->src", pick.astype(jnp.bfloat16), ingest, preferred_element_type=jnp.float32
    ).astype(jnp.bfloat16)
    marks = (
        jnp.dot(pick, (offset + 1).astype(jnp.float32), precision=lax.Precision.HIGHEST) - 1.0
    ).astype(jnp.bfloat16)
    incoming, got_marks = (
        lax.all_to_all(outgoing, "seq", split_axis=0, concat_axis=0, tiled=True),
        lax.all_to_all(marks, "seq", split_axis=0, concat_axis=0, tiled=True),
    )
    local_slots = jnp.arange(tiles_dev, dtype=jnp.float32)
    place = (got_marks.astype(jnp.float32)[None, :] == local_slots[:, None]).astype(jnp.bfloat16)
    arrived = jnp.einsum("js,src->jrc", place, incoming, preferred_element_type=jnp.float32).astype(
        jnp.bfloat16
    )
    own_rows = arrived.reshape(row_count, columns)
    zx_cols = w_zx.reshape(w_zx.shape[0], -1)
    weight_set = (zx_cols, w_bc, w_dt)
    piece = lax.all_gather(own_rows, "head", axis=1, tiled=True)
    acc_zx, acc_bc, acc_dt = tuple(
        (jnp.dot(piece, weight, preferred_element_type=jnp.float32) for weight in weight_set)
    )
    zx = acc_zx.astype(jnp.bfloat16)
    x_in = zx[:, inner_here:]
    bc_all = acc_bc.astype(jnp.bfloat16)
    step_dt = jax.nn.softplus(acc_dt + dt_bias[None, :])
    within = jnp.arange(tile_len, dtype=jnp.int32)
    has_bound = (doc_start < tile_len).astype(jnp.float32)
    before_count = jnp.cumsum(has_bound) - has_bound
    later = (within[None, :] >= doc_start[:, None]).astype(jnp.float32)
    segment = (before_count[:, None] + later).reshape(row_count)
    conv_in = jnp.concatenate([x_in, bc_all], 1)
    tail = conv_in[row_count - keep_rows :]
    tail_seg = (segment[row_count - keep_rows :] - segment[row_count - 1]).astype(jnp.bfloat16)
    got_tail, got_seg = shifted((tail, tail_seg), "seq", 1)
    extended = jnp.concatenate([got_tail, conv_in], 0)
    ext_seg = jnp.concatenate([got_seg.astype(jnp.float32), segment], 0)
    conv_weight = jnp.concatenate([conv_x, conv_bc], 1)
    conv_bias = jnp.concatenate([cbias_x, cbias_bc], 0)
    total = conv_bias[None, :] + conv_weight[taps - 1][None, :] * conv_in.astype(jnp.float32)
    for back_step in range(keep_rows):
        same = ext_seg[back_step : back_step + row_count] == segment
        total = total + jnp.where(
            same[:, None],
            conv_weight[back_step][None, :]
            * extended[back_step : back_step + row_count].astype(jnp.float32),
            0.0,
        )
    conv_out = jax.nn.silu(total).astype(jnp.bfloat16)
    rate = -jnp.exp(a_log)
    tile_dt = step_dt.reshape(tiles_dev, tile_len, heads_here)
    lower = (within[:, None] >= within[None, :]).astype(jnp.float32)
    cumul = jnp.einsum(
        "is,jsh->jih", lower, tile_dt * rate[None, None, :], precision=lax.Precision.HIGHEST
    )
    cumul_t = cumul.transpose(0, 2, 1)
    dt_t = tile_dt.transpose(0, 2, 1)
    last_part = later[:, tile_len - 1]
    tail_keep = (later == last_part[:, None]).astype(jnp.float32)
    to_end = jnp.exp(cumul[:, tile_len - 1 :, :] - cumul) * tile_dt * tail_keep[:, :, None]
    b_t = conv_out[:, inner_here : inner_here + state_dim].reshape(
        tiles_dev, tile_len, state_dim
    ).transpose(0, 2, 1)
    contrib = contrib_tiles(conv_out, b_t, to_end, inner_here, state_dim)
    passing = jnp.exp(cumul[:, tile_len - 1, :]) * (1.0 - has_bound)[:, None]
    through = jnp.cumprod(passing, 0)
    prefix = jnp.concatenate([jnp.ones((1, heads_here), jnp.float32), through[:-1]], 0)
    reverse = jnp.cumprod(passing[::-1], 0)[::-1]
    to_last = jnp.concatenate([reverse[1:], jnp.ones((1, heads_here), jnp.float32)], 0)
    widen = lambda per_head: jnp.repeat(per_head, head_dim, axis=-1)
    run_state = jnp.sum(widen(to_last)[:, None, :] * contrib, 0)
    passing_wide = widen(passing)
    running = jnp.zeros((state_dim, inner_here), jnp.float32)
    states = []
    for tile in range(tiles_dev):
        states.append(running)
        running = passing_wide[tile][None, :] * running + contrib[tile]
    before_tile = jnp.stack(states)
    position = lax.axis_index("seq")
    run_decay = widen(through[tiles_dev - 1])
    distance = 1
    while distance < seq_count:
        got_decay, got_state = shifted((run_decay, run_state.astype(jnp.bfloat16)), "seq", distance)
        run_state = run_state + run_decay[None, :] * got_state.astype(jnp.float32)
        run_decay = jnp.where(position >= distance, run_decay * got_decay, run_decay)
        distance *= 2
    entering = shifted(run_state.astype(jnp.bfloat16), "seq", 1).astype(jnp.float32)
    tile_state = before_tile + widen(prefix)[:, None, :] * entering[None]
    carried = tile_state.astype(jnp.bfloat16)
    d_full = jnp.repeat(d_skip, head_dim)[None, :]
    gated, row_sq = mix_tiles(conv_out, zx, cumul, cumul_t, dt_t, later, carried, d_full)
    sums = lax.psum(row_sq, "head")
    return (gated * lax.rsqrt(sums / INNER + EPSILON) * norm_gain[None, :]).astype(jnp.bfloat16)


def solution(mesh):
    return jax.shard_map(
        shards,
        mesh=mesh,
        in_specs=(
            P("seq", None, "head"),
            P("seq"),
            P("seq"),
            P(None, None, "head"),
            P(),
            P(None, "head"),
            P("head"),
            P("head"),
            P(None, "head"),
            P(),
            P("head"),
            P(),
            P("head"),
            P("head"),
        ),
        out_specs=P("seq", "head"),
        check_vma=False,
    )
```

```python
import jax
import jax.numpy as jnp
from jax import lax
from jax.experimental import pallas as pl
from jax.experimental.pallas import tpu as pltpu
from jax.sharding import PartitionSpec as P

INNER = 2048


EPSILON = 1e-05


def shifted(x, axis, by):
    devices = lax.axis_size(axis)
    pairs = [(i, i + by) for i in range(devices) if 0 <= i + by < devices]
    return lax.ppermute(x, axis, pairs)


def mix_tile(
    x_ref, b_ref, c_ref, cum_ref, cumt_ref, dtt_ref, partc_ref, partr_ref, car_ref, gate_ref, d_ref,
    out_ref, sq_ref,
):
    f32 = jnp.float32
    tile_len = x_ref.shape[0]
    pairs = x_ref.shape[1] // 128
    b_mat = b_ref[...]
    c_mat = c_ref[...]
    scores = lax.dot_general(
        c_mat, b_mat, (((1,), (1,)), ((), ())), preferred_element_type=f32
    )
    cum = cum_ref[0]
    cumt = cumt_ref[0]
    dtt = dtt_ref[0]
    part_col = partc_ref[0]
    part_row = partr_ref[0]
    row = lax.broadcasted_iota(jnp.int32, (tile_len, tile_len), 0)
    col = lax.broadcasted_iota(jnp.int32, (tile_len, tile_len), 1)
    keep = (row >= col) & (part_col == part_row)
    earlier = 1.0 - part_col
    first_half = lax.broadcasted_iota(jnp.int32, (tile_len, 128), 1) < 64
    total_sq = jnp.zeros((tile_len, 128), f32)
    for pair in range(pairs):
        cols = pl.ds(pair * 128, 128)
        x_pair = x_ref[:, cols]
        slabs = []
        for half in range(2):
            head = 2 * pair + half
            diff = cum[:, head : head + 1] - cumt[head : head + 1, :]
            decay = jnp.where(keep, jnp.exp(jnp.where(keep, diff, 0.0)), 0.0)
            slabs.append((scores * decay * dtt[head : head + 1, :]).astype(jnp.bfloat16))
        weights = jnp.concatenate(slabs, axis=1)
        zero = jnp.zeros_like(x_pair)
        split_x = jnp.concatenate(
            [jnp.where(first_half, x_pair, zero), jnp.where(first_half, zero, x_pair)], axis=0
        )
        intra = jnp.dot(weights, split_x, preferred_element_type=f32)
        projected = jnp.dot(c_mat, car_ref[0, :, cols], preferred_element_type=f32)
        grow = jnp.where(
            first_half,
            jnp.exp(cum[:, 2 * pair : 2 * pair + 1]),
            jnp.exp(cum[:, 2 * pair + 1 : 2 * pair + 2]),
        )
        inter = grow * earlier * projected
        mixed = intra + inter + d_ref[:, cols] * x_pair.astype(f32)
        gate = gate_ref[:, cols].astype(f32)
        gated = mixed * (gate * (0.5 + 0.5 * jnp.tanh(0.5 * gate)))
        out_ref[:, cols] = gated
        total_sq = total_sq + gated * gated
    sq_ref[...] = jnp.sum(total_sq, axis=1, keepdims=True)


def contrib_tile(x_ref, bt_ref, end_ref, out_ref):
    f32 = jnp.float32
    tile_len = x_ref.shape[0]
    pairs = x_ref.shape[1] // 128
    b_t = bt_ref[0]
    to_end = end_ref[0]
    first_half = lax.broadcasted_iota(jnp.int32, (tile_len, 128), 1) < 64
    for pair in range(pairs):
        cols = pl.ds(pair * 128, 128)
        scale = jnp.where(
            first_half, to_end[:, 2 * pair : 2 * pair + 1], to_end[:, 2 * pair + 1 : 2 * pair + 2]
        )
        scaled = (x_ref[:, cols].astype(f32) * scale).astype(jnp.bfloat16)
        out_ref[0, :, cols] = jnp.dot(b_t, scaled, preferred_element_type=f32)


def contrib_tiles(conv_out, b_t, to_end, inner_here, state_dim):
    tiles_dev, tile_len, heads_here = to_end.shape
    return pl.pallas_call(
        contrib_tile,
        grid=(tiles_dev,),
        in_specs=[
            pl.BlockSpec((tile_len, inner_here), lambda j: (j, 0)),
            pl.BlockSpec((1, state_dim, tile_len), lambda j: (j, 0, 0)),
            pl.BlockSpec((1, tile_len, heads_here), lambda j: (j, 0, 0)),
        ],
        out_specs=pl.BlockSpec((1, state_dim, inner_here), lambda j: (j, 0, 0)),
        out_shape=jax.ShapeDtypeStruct((tiles_dev, state_dim, inner_here), jnp.float32),
        cost_estimate=pl.CostEstimate(
            flops=tiles_dev * 2 * tile_len * inner_here * state_dim,
            transcendentals=0,
            bytes_accessed=tiles_dev * (tile_len * (inner_here + state_dim) * 2 + inner_here * state_dim * 4),
        ),
    )(conv_out, b_t, to_end)


def mix_tiles(conv_out, zx, cumul, cumul_t, dt_t, later, carried, d_full):
    tiles_dev, tile_len, heads_here = cumul.shape
    inner_here = carried.shape[2]
    state_dim = carried.shape[1]
    rows = tiles_dev * tile_len
    b_block = inner_here // 128
    c_block = b_block + state_dim // 128
    part_col = later.reshape(tiles_dev, tile_len, 1)
    part_row = later.reshape(tiles_dev, 1, tile_len)
    per_tile = lambda j: (j, 0, 0)
    return pl.pallas_call(
        mix_tile,
        grid=(tiles_dev,),
        in_specs=[
            pl.BlockSpec((tile_len, inner_here), lambda j: (j, 0)),
            pl.BlockSpec((tile_len, state_dim), lambda j: (j, b_block)),
            pl.BlockSpec((tile_len, state_dim), lambda j: (j, c_block)),
            pl.BlockSpec((1, tile_len, heads_here), per_tile),
            pl.BlockSpec((1, heads_here, tile_len), per_tile),
            pl.BlockSpec((1, heads_here, tile_len), per_tile),
            pl.BlockSpec((1, tile_len, 1), per_tile),
            pl.BlockSpec((1, 1, tile_len), per_tile),
            pl.BlockSpec((1, state_dim, inner_here), per_tile),
            pl.BlockSpec((tile_len, inner_here), lambda j: (j, 0)),
            pl.BlockSpec((1, inner_here), lambda j: (0, 0)),
        ],
        out_specs=[
            pl.BlockSpec((tile_len, inner_here), lambda j: (j, 0)),
            pl.BlockSpec((tile_len, 1), lambda j: (j, 0)),
        ],
        out_shape=[
            jax.ShapeDtypeStruct((rows, inner_here), jnp.float32),
            jax.ShapeDtypeStruct((rows, 1), jnp.float32),
        ],
        cost_estimate=pl.CostEstimate(
            flops=tiles_dev * (2 * tile_len * tile_len * (state_dim + 4 * inner_here + 2 * inner_here)),
            transcendentals=tiles_dev * tile_len * (tile_len * heads_here + 2 * inner_here),
            bytes_accessed=rows * inner_here * 10 + tiles_dev * inner_here * state_dim * 2,
        ),
    )(conv_out, conv_out, conv_out, cumul, cumul_t, dt_t, part_col, part_row, carried, zx, d_full)


def shards(
    ingest,
    dest_tile,
    doc_start,
    w_zx,
    w_bc,
    w_dt,
    dt_bias,
    a_log,
    conv_x,
    conv_bc,
    cbias_x,
    cbias_bc,
    d_skip,
    norm_gain,
):
    seq_count = lax.axis_size("seq")
    tiles_dev = ingest.shape[0]
    tile_len = ingest.shape[1]
    columns = ingest.shape[2]
    row_count = tiles_dev * tile_len
    heads_here = a_log.shape[0]
    inner_here = conv_x.shape[1]
    head_dim = inner_here // heads_here
    state_dim = conv_bc.shape[1] // 2
    taps = conv_x.shape[0]
    keep_rows = taps - 1
    owner = dest_tile // tiles_dev
    slots = jnp.arange(seq_count, dtype=jnp.int32)
    pick = (owner[None, :] == slots[:, None]).astype(jnp.float32)
    outgoing = jnp.einsum(
        "sj,jrc->src", pick.astype(jnp.bfloat16), ingest, preferred_element_type=jnp.float32
    ).astype(jnp.bfloat16)
    incoming = lax.all_to_all(outgoing, "seq", split_axis=0, concat_axis=0, tiled=True)
    every_dest = lax.all_gather(dest_tile, "seq", tiled=True).reshape(seq_count, tiles_dev)
    mine = every_dest // tiles_dev == lax.axis_index("seq")
    got_slot = jnp.sum(jnp.where(mine, every_dest % tiles_dev, 0), 1)
    local_slots = jnp.arange(tiles_dev, dtype=jnp.int32)
    place = (got_slot[None, :] == local_slots[:, None]).astype(jnp.bfloat16)
    arrived = jnp.einsum("js,src->jrc", place, incoming, preferred_element_type=jnp.float32).astype(
        jnp.bfloat16
    )
    own_rows = arrived.reshape(row_count, columns)
    zx_cols = w_zx.reshape(w_zx.shape[0], -1)
    weight_set = (zx_cols, w_bc, w_dt)
    piece = lax.all_gather(own_rows, "head", axis=1, tiled=True)
    acc_zx, acc_bc, acc_dt = tuple(
        (jnp.dot(piece, weight, preferred_element_type=jnp.float32) for weight in weight_set)
    )
    zx = acc_zx.astype(jnp.bfloat16)
    x_in = zx[:, inner_here:]
    bc_all = acc_bc.astype(jnp.bfloat16)
    step_dt = jax.nn.softplus(acc_dt + dt_bias[None, :])
    within = jnp.arange(tile_len, dtype=jnp.int32)
    has_bound = (doc_start < tile_len).astype(jnp.float32)
    before_count = jnp.cumsum(has_bound) - has_bound
    later = (within[None, :] >= doc_start[:, None]).astype(jnp.float32)
    segment = (before_count[:, None] + later).reshape(row_count)
    conv_in = jnp.concatenate([x_in, bc_all], 1)
    tail = conv_in[row_count - keep_rows :]
    tail_seg = (segment[row_count - keep_rows :] - segment[row_count - 1]).astype(jnp.bfloat16)
    got_tail, got_seg = shifted((tail, tail_seg), "seq", 1)
    extended = jnp.concatenate([got_tail, conv_in], 0)
    ext_seg = jnp.concatenate([got_seg.astype(jnp.float32), segment], 0)
    conv_weight = jnp.concatenate([conv_x, conv_bc], 1)
    conv_bias = jnp.concatenate([cbias_x, cbias_bc], 0)
    total = conv_bias[None, :] + conv_weight[taps - 1][None, :] * conv_in.astype(jnp.float32)
    for back_step in range(keep_rows):
        same = ext_seg[back_step : back_step + row_count] == segment
        total = total + jnp.where(
            same[:, None],
            conv_weight[back_step][None, :]
            * extended[back_step : back_step + row_count].astype(jnp.float32),
            0.0,
        )
    conv_out = jax.nn.silu(total).astype(jnp.bfloat16)
    rate = -jnp.exp(a_log)
    tile_dt = step_dt.reshape(tiles_dev, tile_len, heads_here)
    lower = (within[:, None] >= within[None, :]).astype(jnp.float32)
    cumul = jnp.einsum(
        "is,jsh->jih", lower, tile_dt * rate[None, None, :], precision=lax.Precision.HIGHEST
    )
    cumul_t = cumul.transpose(0, 2, 1)
    dt_t = tile_dt.transpose(0, 2, 1)
    last_part = later[:, tile_len - 1]
    tail_keep = (later == last_part[:, None]).astype(jnp.float32)
    to_end = jnp.exp(cumul[:, tile_len - 1 :, :] - cumul) * tile_dt * tail_keep[:, :, None]
    b_t = conv_out[:, inner_here : inner_here + state_dim].reshape(
        tiles_dev, tile_len, state_dim
    ).transpose(0, 2, 1)
    contrib = contrib_tiles(conv_out, b_t, to_end, inner_here, state_dim)
    passing = jnp.exp(cumul[:, tile_len - 1, :]) * (1.0 - has_bound)[:, None]
    through = jnp.cumprod(passing, 0)
    prefix = jnp.concatenate([jnp.ones((1, heads_here), jnp.float32), through[:-1]], 0)
    reverse = jnp.cumprod(passing[::-1], 0)[::-1]
    to_last = jnp.concatenate([reverse[1:], jnp.ones((1, heads_here), jnp.float32)], 0)
    widen = lambda per_head: jnp.repeat(per_head, head_dim, axis=-1)
    run_state = jnp.sum(widen(to_last)[:, None, :] * contrib, 0)
    passing_wide = widen(passing)
    running = jnp.zeros((state_dim, inner_here), jnp.float32)
    states = []
    for tile in range(tiles_dev):
        states.append(running)
        running = passing_wide[tile][None, :] * running + contrib[tile]
    before_tile = jnp.stack(states)
    position = lax.axis_index("seq")
    run_decay = widen(through[tiles_dev - 1])
    distance = 1
    while distance < seq_count:
        got_decay, got_state = shifted((run_decay, run_state.astype(jnp.bfloat16)), "seq", distance)
        run_state = run_state + run_decay[None, :] * got_state.astype(jnp.float32)
        run_decay = jnp.where(position >= distance, run_decay * got_decay, run_decay)
        distance *= 2
    entering = shifted(run_state.astype(jnp.bfloat16), "seq", 1).astype(jnp.float32)
    tile_state = before_tile + widen(prefix)[:, None, :] * entering[None]
    carried = tile_state.astype(jnp.bfloat16)
    d_full = jnp.repeat(d_skip, head_dim)[None, :]
    gated, row_sq = mix_tiles(conv_out, zx, cumul, cumul_t, dt_t, later, carried, d_full)
    sums = jnp.sum(lax.all_gather(row_sq, "head"), 0)
    return (gated * lax.rsqrt(sums / INNER + EPSILON) * norm_gain[None, :]).astype(jnp.bfloat16)


def solution(mesh):
    return jax.shard_map(
        shards,
        mesh=mesh,
        in_specs=(
            P("seq", None, "head"),
            P("seq"),
            P("seq"),
            P(None, None, "head"),
            P(),
            P(None, "head"),
            P("head"),
            P("head"),
            P(None, "head"),
            P(),
            P("head"),
            P(),
            P("head"),
            P("head"),
        ),
        out_specs=P("seq", "head"),
        check_vma=False,
    )
```

```python
import jax
import jax.numpy as jnp
from jax import lax
from jax.experimental import pallas as pl
from jax.experimental.pallas import tpu as pltpu
from jax.sharding import PartitionSpec as P

INNER = 2048


EPSILON = 1e-05


def shifted(x, axis, by):
    devices = lax.axis_size(axis)
    pairs = [(i, i + by) for i in range(devices) if 0 <= i + by < devices]
    return lax.ppermute(x, axis, pairs)


def mix_tile(
    x_ref, b_ref, c_ref, cum_ref, cumt_ref, dtt_ref, partc_ref, partr_ref, car_ref, gate_ref, d_ref,
    out_ref, sq_ref,
):
    f32 = jnp.float32
    tile_len = x_ref.shape[0]
    pairs = x_ref.shape[1] // 128
    b_mat = b_ref[...]
    c_mat = c_ref[...]
    scores = lax.dot_general(
        c_mat, b_mat, (((1,), (1,)), ((), ())), preferred_element_type=f32
    )
    cum = cum_ref[0]
    cumt = cumt_ref[0]
    dtt = dtt_ref[0]
    part_col = partc_ref[0]
    part_row = partr_ref[0]
    row = lax.broadcasted_iota(jnp.int32, (tile_len, tile_len), 0)
    col = lax.broadcasted_iota(jnp.int32, (tile_len, tile_len), 1)
    keep = (row >= col) & (part_col == part_row)
    earlier = 1.0 - part_col
    first_half = lax.broadcasted_iota(jnp.int32, (tile_len, 128), 1) < 64
    total_sq = jnp.zeros((tile_len, 128), f32)
    for pair in range(pairs):
        cols = pl.ds(pair * 128, 128)
        x_pair = x_ref[:, cols]
        slabs = []
        for half in range(2):
            head = 2 * pair + half
            diff = cum[:, head : head + 1] - cumt[head : head + 1, :]
            decay = jnp.where(keep, jnp.exp(jnp.where(keep, diff, 0.0)), 0.0)
            slabs.append((scores * decay * dtt[head : head + 1, :]).astype(jnp.bfloat16))
        weights = jnp.concatenate(slabs, axis=1)
        zero = jnp.zeros_like(x_pair)
        split_x = jnp.concatenate(
            [jnp.where(first_half, x_pair, zero), jnp.where(first_half, zero, x_pair)], axis=0
        )
        intra = jnp.dot(weights, split_x, preferred_element_type=f32)
        projected = jnp.dot(c_mat, car_ref[0, :, cols], preferred_element_type=f32)
        grow = jnp.where(
            first_half,
            jnp.exp(cum[:, 2 * pair : 2 * pair + 1]),
            jnp.exp(cum[:, 2 * pair + 1 : 2 * pair + 2]),
        )
        inter = grow * earlier * projected
        mixed = intra + inter + d_ref[:, cols] * x_pair.astype(f32)
        gate = gate_ref[:, cols].astype(f32)
        gated = mixed * (gate * (0.5 + 0.5 * jnp.tanh(0.5 * gate)))
        out_ref[:, cols] = gated
        total_sq = total_sq + gated * gated
    sq_ref[...] = jnp.sum(total_sq, axis=1, keepdims=True)


def contrib_tile(x_ref, bt_ref, end_ref, out_ref):
    f32 = jnp.float32
    tile_len = x_ref.shape[0]
    pairs = x_ref.shape[1] // 128
    b_t = bt_ref[0]
    to_end = end_ref[0]
    first_half = lax.broadcasted_iota(jnp.int32, (tile_len, 128), 1) < 64
    for pair in range(pairs):
        cols = pl.ds(pair * 128, 128)
        scale = jnp.where(
            first_half, to_end[:, 2 * pair : 2 * pair + 1], to_end[:, 2 * pair + 1 : 2 * pair + 2]
        )
        scaled = (x_ref[:, cols].astype(f32) * scale).astype(jnp.bfloat16)
        out_ref[0, :, cols] = jnp.dot(b_t, scaled, preferred_element_type=f32)


def contrib_tiles(conv_out, b_t, to_end, inner_here, state_dim):
    tiles_dev, tile_len, heads_here = to_end.shape
    return pl.pallas_call(
        contrib_tile,
        grid=(tiles_dev,),
        in_specs=[
            pl.BlockSpec((tile_len, inner_here), lambda j: (j, 0)),
            pl.BlockSpec((1, state_dim, tile_len), lambda j: (j, 0, 0)),
            pl.BlockSpec((1, tile_len, heads_here), lambda j: (j, 0, 0)),
        ],
        out_specs=pl.BlockSpec((1, state_dim, inner_here), lambda j: (j, 0, 0)),
        out_shape=jax.ShapeDtypeStruct((tiles_dev, state_dim, inner_here), jnp.float32),
        cost_estimate=pl.CostEstimate(
            flops=tiles_dev * 2 * tile_len * inner_here * state_dim,
            transcendentals=0,
            bytes_accessed=tiles_dev * (tile_len * (inner_here + state_dim) * 2 + inner_here * state_dim * 4),
        ),
    )(conv_out, b_t, to_end)


def mix_tiles(conv_out, zx, cumul, cumul_t, dt_t, later, carried, d_full):
    tiles_dev, tile_len, heads_here = cumul.shape
    inner_here = carried.shape[2]
    state_dim = carried.shape[1]
    rows = tiles_dev * tile_len
    b_block = inner_here // 128
    c_block = b_block + state_dim // 128
    part_col = later.reshape(tiles_dev, tile_len, 1)
    part_row = later.reshape(tiles_dev, 1, tile_len)
    per_tile = lambda j: (j, 0, 0)
    return pl.pallas_call(
        mix_tile,
        grid=(tiles_dev,),
        in_specs=[
            pl.BlockSpec((tile_len, inner_here), lambda j: (j, 0)),
            pl.BlockSpec((tile_len, state_dim), lambda j: (j, b_block)),
            pl.BlockSpec((tile_len, state_dim), lambda j: (j, c_block)),
            pl.BlockSpec((1, tile_len, heads_here), per_tile),
            pl.BlockSpec((1, heads_here, tile_len), per_tile),
            pl.BlockSpec((1, heads_here, tile_len), per_tile),
            pl.BlockSpec((1, tile_len, 1), per_tile),
            pl.BlockSpec((1, 1, tile_len), per_tile),
            pl.BlockSpec((1, state_dim, inner_here), per_tile),
            pl.BlockSpec((tile_len, inner_here), lambda j: (j, 0)),
            pl.BlockSpec((1, inner_here), lambda j: (0, 0)),
        ],
        out_specs=[
            pl.BlockSpec((tile_len, inner_here), lambda j: (j, 0)),
            pl.BlockSpec((tile_len, 1), lambda j: (j, 0)),
        ],
        out_shape=[
            jax.ShapeDtypeStruct((rows, inner_here), jnp.float32),
            jax.ShapeDtypeStruct((rows, 1), jnp.float32),
        ],
        cost_estimate=pl.CostEstimate(
            flops=tiles_dev * (2 * tile_len * tile_len * (state_dim + 4 * inner_here + 2 * inner_here)),
            transcendentals=tiles_dev * tile_len * (tile_len * heads_here + 2 * inner_here),
            bytes_accessed=rows * inner_here * 10 + tiles_dev * inner_here * state_dim * 2,
        ),
    )(conv_out, conv_out, conv_out, cumul, cumul_t, dt_t, part_col, part_row, carried, zx, d_full)


def shards(
    ingest,
    dest_tile,
    doc_start,
    w_zx,
    w_bc,
    w_dt,
    dt_bias,
    a_log,
    conv_x,
    conv_bc,
    cbias_x,
    cbias_bc,
    d_skip,
    norm_gain,
):
    seq_count = lax.axis_size("seq")
    tiles_dev = ingest.shape[0]
    tile_len = ingest.shape[1]
    columns = ingest.shape[2]
    row_count = tiles_dev * tile_len
    heads_here = a_log.shape[0]
    inner_here = conv_x.shape[1]
    head_dim = inner_here // heads_here
    state_dim = conv_bc.shape[1] // 2
    taps = conv_x.shape[0]
    keep_rows = taps - 1
    owner = dest_tile // tiles_dev
    slots = jnp.arange(seq_count, dtype=jnp.int32)
    pick = (owner[None, :] == slots[:, None]).astype(jnp.float32)
    outgoing = jnp.einsum(
        "sj,jrc->src", pick.astype(jnp.bfloat16), ingest, preferred_element_type=jnp.float32
    ).astype(jnp.bfloat16)
    incoming = lax.all_to_all(outgoing, "seq", split_axis=0, concat_axis=0, tiled=True)
    every_dest = lax.all_gather(dest_tile, "seq", tiled=True).reshape(seq_count, tiles_dev)
    mine = every_dest // tiles_dev == lax.axis_index("seq")
    got_slot = jnp.sum(jnp.where(mine, every_dest % tiles_dev, 0), 1)
    local_slots = jnp.arange(tiles_dev, dtype=jnp.int32)
    place = (got_slot[None, :] == local_slots[:, None]).astype(jnp.bfloat16)
    arrived = jnp.einsum("js,src->jrc", place, incoming, preferred_element_type=jnp.float32).astype(
        jnp.bfloat16
    )
    own_rows = arrived.reshape(row_count, columns)
    zx_cols = w_zx.reshape(w_zx.shape[0], -1)
    weight_set = (zx_cols, w_bc, w_dt)
    piece = lax.all_gather(own_rows, "head", axis=1, tiled=True)
    acc_zx, acc_bc, acc_dt = tuple(
        (jnp.dot(piece, weight, preferred_element_type=jnp.float32) for weight in weight_set)
    )
    zx = acc_zx.astype(jnp.bfloat16)
    x_in = zx[:, inner_here:]
    bc_all = acc_bc.astype(jnp.bfloat16)
    step_dt = jax.nn.softplus(acc_dt + dt_bias[None, :])
    within = jnp.arange(tile_len, dtype=jnp.int32)
    has_bound = (doc_start < tile_len).astype(jnp.float32)
    before_count = jnp.cumsum(has_bound) - has_bound
    later = (within[None, :] >= doc_start[:, None]).astype(jnp.float32)
    segment = (before_count[:, None] + later).reshape(row_count)
    conv_in = jnp.concatenate([x_in, bc_all], 1)
    tail = conv_in[row_count - keep_rows :]
    tail_seg = (segment[row_count - keep_rows :] - segment[row_count - 1]).astype(jnp.bfloat16)
    got_tail, got_seg = shifted((tail, tail_seg), "seq", 1)
    extended = jnp.concatenate([got_tail, conv_in], 0)
    ext_seg = jnp.concatenate([got_seg.astype(jnp.float32), segment], 0)
    conv_weight = jnp.concatenate([conv_x, conv_bc], 1)
    conv_bias = jnp.concatenate([cbias_x, cbias_bc], 0)
    total = conv_bias[None, :] + conv_weight[taps - 1][None, :] * conv_in.astype(jnp.float32)
    for back_step in range(keep_rows):
        same = ext_seg[back_step : back_step + row_count] == segment
        total = total + jnp.where(
            same[:, None],
            conv_weight[back_step][None, :]
            * extended[back_step : back_step + row_count].astype(jnp.float32),
            0.0,
        )
    conv_out = jax.nn.silu(total).astype(jnp.bfloat16)
    rate = -jnp.exp(a_log)
    tile_dt = step_dt.reshape(tiles_dev, tile_len, heads_here)
    lower = (within[:, None] >= within[None, :]).astype(jnp.float32)
    cumul = jnp.einsum(
        "is,jsh->jih", lower, tile_dt * rate[None, None, :], precision=lax.Precision.HIGHEST
    )
    cumul_t = cumul.transpose(0, 2, 1)
    dt_t = tile_dt.transpose(0, 2, 1)
    last_part = later[:, tile_len - 1]
    tail_keep = (later == last_part[:, None]).astype(jnp.float32)
    to_end = jnp.exp(cumul[:, tile_len - 1 :, :] - cumul) * tile_dt * tail_keep[:, :, None]
    b_t = conv_out[:, inner_here : inner_here + state_dim].reshape(
        tiles_dev, tile_len, state_dim
    ).transpose(0, 2, 1)
    contrib = contrib_tiles(conv_out, b_t, to_end, inner_here, state_dim)
    passing = jnp.exp(cumul[:, tile_len - 1, :]) * (1.0 - has_bound)[:, None]
    through = jnp.cumprod(passing, 0)
    prefix = jnp.concatenate([jnp.ones((1, heads_here), jnp.float32), through[:-1]], 0)
    reverse = jnp.cumprod(passing[::-1], 0)[::-1]
    to_last = jnp.concatenate([reverse[1:], jnp.ones((1, heads_here), jnp.float32)], 0)
    widen = lambda per_head: jnp.repeat(per_head, head_dim, axis=-1)
    run_state = jnp.sum(widen(to_last)[:, None, :] * contrib, 0)
    passing_wide = widen(passing)
    running = jnp.zeros((state_dim, inner_here), jnp.float32)
    states = []
    for tile in range(tiles_dev):
        states.append(running)
        running = passing_wide[tile][None, :] * running + contrib[tile]
    before_tile = jnp.stack(states)
    position = lax.axis_index("seq")
    run_decay = widen(through[tiles_dev - 1])
    distance = 1
    while distance < seq_count:
        high = run_decay.astype(jnp.bfloat16)
        rest = run_decay - high.astype(jnp.float32)
        middle = rest.astype(jnp.bfloat16)
        low = (rest - middle.astype(jnp.float32)).astype(jnp.bfloat16)
        payload = jnp.concatenate(
            [run_state.astype(jnp.bfloat16), high[None], middle[None], low[None]], 0
        )
        got = shifted(payload, "seq", distance).astype(jnp.float32)
        got_decay = got[state_dim] + got[state_dim + 1] + got[state_dim + 2]
        run_state = run_state + run_decay[None, :] * got[:state_dim]
        run_decay = jnp.where(position >= distance, run_decay * got_decay, run_decay)
        distance *= 2
    entering = shifted(run_state.astype(jnp.bfloat16), "seq", 1).astype(jnp.float32)
    tile_state = before_tile + widen(prefix)[:, None, :] * entering[None]
    carried = tile_state.astype(jnp.bfloat16)
    d_full = jnp.repeat(d_skip, head_dim)[None, :]
    gated, row_sq = mix_tiles(conv_out, zx, cumul, cumul_t, dt_t, later, carried, d_full)
    sums = jnp.sum(lax.all_gather(row_sq, "head"), 0)
    return (gated * lax.rsqrt(sums / INNER + EPSILON) * norm_gain[None, :]).astype(jnp.bfloat16)


def solution(mesh):
    return jax.shard_map(
        shards,
        mesh=mesh,
        in_specs=(
            P("seq", None, "head"),
            P("seq"),
            P("seq"),
            P(None, None, "head"),
            P(),
            P(None, "head"),
            P("head"),
            P("head"),
            P(None, "head"),
            P(),
            P("head"),
            P(),
            P("head"),
            P("head"),
        ),
        out_specs=P("seq", "head"),
        check_vma=False,
    )
```

```python
import jax
import jax.numpy as jnp
from jax import lax
from jax.experimental import pallas as pl
from jax.experimental.pallas import tpu as pltpu
from jax.sharding import PartitionSpec as P

INNER = 2048


EPSILON = 1e-05


def shifted(x, axis, by):
    devices = lax.axis_size(axis)
    pairs = [(i, i + by) for i in range(devices) if 0 <= i + by < devices]
    return lax.ppermute(x, axis, pairs)


def mix_tile(
    x_ref, b_ref, c_ref, cum_ref, cumt_ref, dtt_ref, partc_ref, partr_ref, car_ref, gate_ref, d_ref,
    out_ref, sq_ref,
):
    f32 = jnp.float32
    tile_len = x_ref.shape[0]
    pairs = x_ref.shape[1] // 128
    b_mat = b_ref[...]
    c_mat = c_ref[...]
    scores = lax.dot_general(
        c_mat, b_mat, (((1,), (1,)), ((), ())), preferred_element_type=f32
    )
    cum = cum_ref[0]
    cumt = cumt_ref[0]
    dtt = dtt_ref[0]
    part_col = partc_ref[0]
    part_row = partr_ref[0]
    row = lax.broadcasted_iota(jnp.int32, (tile_len, tile_len), 0)
    col = lax.broadcasted_iota(jnp.int32, (tile_len, tile_len), 1)
    keep = (row >= col) & (part_col == part_row)
    earlier = 1.0 - part_col
    first_half = lax.broadcasted_iota(jnp.int32, (tile_len, 128), 1) < 64
    total_sq = jnp.zeros((tile_len, 128), f32)
    for pair in range(pairs):
        cols = pl.ds(pair * 128, 128)
        x_pair = x_ref[:, cols]
        slabs = []
        for half in range(2):
            head = 2 * pair + half
            diff = cum[:, head : head + 1] - cumt[head : head + 1, :]
            decay = jnp.where(keep, jnp.exp(jnp.where(keep, diff, 0.0)), 0.0)
            slabs.append((scores * decay * dtt[head : head + 1, :]).astype(jnp.bfloat16))
        weights = jnp.concatenate(slabs, axis=1)
        zero = jnp.zeros_like(x_pair)
        split_x = jnp.concatenate(
            [jnp.where(first_half, x_pair, zero), jnp.where(first_half, zero, x_pair)], axis=0
        )
        intra = jnp.dot(weights, split_x, preferred_element_type=f32)
        projected = jnp.dot(c_mat, car_ref[0, :, cols], preferred_element_type=f32)
        grow = jnp.where(
            first_half,
            jnp.exp(cum[:, 2 * pair : 2 * pair + 1]),
            jnp.exp(cum[:, 2 * pair + 1 : 2 * pair + 2]),
        )
        inter = grow * earlier * projected
        mixed = intra + inter + d_ref[:, cols] * x_pair.astype(f32)
        gate = gate_ref[:, cols].astype(f32)
        gated = mixed * (gate * (0.5 + 0.5 * jnp.tanh(0.5 * gate)))
        out_ref[:, cols] = gated
        total_sq = total_sq + gated * gated
    sq_ref[...] = jnp.sum(total_sq, axis=1, keepdims=True)


def contrib_tile(x_ref, bt_ref, end_ref, out_ref):
    f32 = jnp.float32
    tile_len = x_ref.shape[0]
    pairs = x_ref.shape[1] // 128
    b_t = bt_ref[0]
    to_end = end_ref[0]
    first_half = lax.broadcasted_iota(jnp.int32, (tile_len, 128), 1) < 64
    for pair in range(pairs):
        cols = pl.ds(pair * 128, 128)
        scale = jnp.where(
            first_half, to_end[:, 2 * pair : 2 * pair + 1], to_end[:, 2 * pair + 1 : 2 * pair + 2]
        )
        scaled = (x_ref[:, cols].astype(f32) * scale).astype(jnp.bfloat16)
        out_ref[0, :, cols] = jnp.dot(b_t, scaled, preferred_element_type=f32)


def contrib_tiles(conv_out, b_t, to_end, inner_here, state_dim):
    tiles_dev, tile_len, heads_here = to_end.shape
    return pl.pallas_call(
        contrib_tile,
        grid=(tiles_dev,),
        in_specs=[
            pl.BlockSpec((tile_len, inner_here), lambda j: (j, 0)),
            pl.BlockSpec((1, state_dim, tile_len), lambda j: (j, 0, 0)),
            pl.BlockSpec((1, tile_len, heads_here), lambda j: (j, 0, 0)),
        ],
        out_specs=pl.BlockSpec((1, state_dim, inner_here), lambda j: (j, 0, 0)),
        out_shape=jax.ShapeDtypeStruct((tiles_dev, state_dim, inner_here), jnp.float32),
        cost_estimate=pl.CostEstimate(
            flops=tiles_dev * 2 * tile_len * inner_here * state_dim,
            transcendentals=0,
            bytes_accessed=tiles_dev * (tile_len * (inner_here + state_dim) * 2 + inner_here * state_dim * 4),
        ),
    )(conv_out, b_t, to_end)


def mix_tiles(conv_out, zx, cumul, cumul_t, dt_t, later, carried, d_full):
    tiles_dev, tile_len, heads_here = cumul.shape
    inner_here = carried.shape[2]
    state_dim = carried.shape[1]
    rows = tiles_dev * tile_len
    b_block = inner_here // 128
    c_block = b_block + state_dim // 128
    part_col = later.reshape(tiles_dev, tile_len, 1)
    part_row = later.reshape(tiles_dev, 1, tile_len)
    per_tile = lambda j: (j, 0, 0)
    return pl.pallas_call(
        mix_tile,
        grid=(tiles_dev,),
        in_specs=[
            pl.BlockSpec((tile_len, inner_here), lambda j: (j, 0)),
            pl.BlockSpec((tile_len, state_dim), lambda j: (j, b_block)),
            pl.BlockSpec((tile_len, state_dim), lambda j: (j, c_block)),
            pl.BlockSpec((1, tile_len, heads_here), per_tile),
            pl.BlockSpec((1, heads_here, tile_len), per_tile),
            pl.BlockSpec((1, heads_here, tile_len), per_tile),
            pl.BlockSpec((1, tile_len, 1), per_tile),
            pl.BlockSpec((1, 1, tile_len), per_tile),
            pl.BlockSpec((1, state_dim, inner_here), per_tile),
            pl.BlockSpec((tile_len, inner_here), lambda j: (j, 0)),
            pl.BlockSpec((1, inner_here), lambda j: (0, 0)),
        ],
        out_specs=[
            pl.BlockSpec((tile_len, inner_here), lambda j: (j, 0)),
            pl.BlockSpec((tile_len, 1), lambda j: (j, 0)),
        ],
        out_shape=[
            jax.ShapeDtypeStruct((rows, inner_here), jnp.float32),
            jax.ShapeDtypeStruct((rows, 1), jnp.float32),
        ],
        cost_estimate=pl.CostEstimate(
            flops=tiles_dev * (2 * tile_len * tile_len * (state_dim + 4 * inner_here + 2 * inner_here)),
            transcendentals=tiles_dev * tile_len * (tile_len * heads_here + 2 * inner_here),
            bytes_accessed=rows * inner_here * 10 + tiles_dev * inner_here * state_dim * 2,
        ),
    )(conv_out, conv_out, conv_out, cumul, cumul_t, dt_t, part_col, part_row, carried, zx, d_full)


def shards(
    ingest,
    dest_tile,
    doc_start,
    w_zx,
    w_bc,
    w_dt,
    dt_bias,
    a_log,
    conv_x,
    conv_bc,
    cbias_x,
    cbias_bc,
    d_skip,
    norm_gain,
):
    seq_count = lax.axis_size("seq")
    tiles_dev = ingest.shape[0]
    tile_len = ingest.shape[1]
    columns = ingest.shape[2]
    row_count = tiles_dev * tile_len
    heads_here = a_log.shape[0]
    inner_here = conv_x.shape[1]
    head_dim = inner_here // heads_here
    state_dim = conv_bc.shape[1] // 2
    taps = conv_x.shape[0]
    keep_rows = taps - 1
    owner = dest_tile // tiles_dev
    slots = jnp.arange(seq_count, dtype=jnp.int32)
    pick = (owner[None, :] == slots[:, None]).astype(jnp.float32)
    outgoing = jnp.einsum(
        "sj,jrc->src", pick.astype(jnp.bfloat16), ingest, preferred_element_type=jnp.float32
    ).astype(jnp.bfloat16)
    incoming = lax.all_to_all(outgoing, "seq", split_axis=0, concat_axis=0, tiled=True)
    every_dest = lax.all_gather(dest_tile, "seq", tiled=True).reshape(seq_count, tiles_dev)
    mine = every_dest // tiles_dev == lax.axis_index("seq")
    got_slot = jnp.sum(jnp.where(mine, every_dest % tiles_dev, 0), 1)
    local_slots = jnp.arange(tiles_dev, dtype=jnp.int32)
    place = (got_slot[None, :] == local_slots[:, None]).astype(jnp.bfloat16)
    arrived = jnp.einsum("js,src->jrc", place, incoming, preferred_element_type=jnp.float32).astype(
        jnp.bfloat16
    )
    own_rows = arrived.reshape(row_count, columns)
    zx_cols = w_zx.reshape(w_zx.shape[0], -1)
    weight_set = (zx_cols, w_bc, w_dt)
    piece = lax.all_gather(own_rows, "head", axis=1, tiled=True)
    acc_zx, acc_bc, acc_dt = tuple(
        (jnp.dot(piece, weight, preferred_element_type=jnp.float32) for weight in weight_set)
    )
    zx = acc_zx.astype(jnp.bfloat16)
    x_in = zx[:, inner_here:]
    bc_all = acc_bc.astype(jnp.bfloat16)
    step_dt = jax.nn.softplus(acc_dt + dt_bias[None, :])
    within = jnp.arange(tile_len, dtype=jnp.int32)
    has_bound = (doc_start < tile_len).astype(jnp.float32)
    before_count = jnp.cumsum(has_bound) - has_bound
    later = (within[None, :] >= doc_start[:, None]).astype(jnp.float32)
    segment = (before_count[:, None] + later).reshape(row_count)
    conv_in = jnp.concatenate([x_in, bc_all], 1)
    tail = conv_in[row_count - keep_rows :]
    tail_seg = (segment[row_count - keep_rows :] - segment[row_count - 1]).astype(jnp.bfloat16)
    got_tail, got_seg = shifted((tail, tail_seg), "seq", 1)
    extended = jnp.concatenate([got_tail, conv_in], 0)
    ext_seg = jnp.concatenate([got_seg.astype(jnp.float32), segment], 0)
    conv_weight = jnp.concatenate([conv_x, conv_bc], 1)
    conv_bias = jnp.concatenate([cbias_x, cbias_bc], 0)
    total = conv_bias[None, :] + conv_weight[taps - 1][None, :] * conv_in.astype(jnp.float32)
    for back_step in range(keep_rows):
        same = ext_seg[back_step : back_step + row_count] == segment
        total = total + jnp.where(
            same[:, None],
            conv_weight[back_step][None, :]
            * extended[back_step : back_step + row_count].astype(jnp.float32),
            0.0,
        )
    conv_out = jax.nn.silu(total).astype(jnp.bfloat16)
    rate = -jnp.exp(a_log)
    tile_dt = step_dt.reshape(tiles_dev, tile_len, heads_here)
    lower = (within[:, None] >= within[None, :]).astype(jnp.float32)
    cumul = jnp.einsum(
        "is,jsh->jih", lower, tile_dt * rate[None, None, :], precision=lax.Precision.HIGHEST
    )
    cumul_t = cumul.transpose(0, 2, 1)
    dt_t = tile_dt.transpose(0, 2, 1)
    last_part = later[:, tile_len - 1]
    tail_keep = (later == last_part[:, None]).astype(jnp.float32)
    to_end = jnp.exp(cumul[:, tile_len - 1 :, :] - cumul) * tile_dt * tail_keep[:, :, None]
    b_t = conv_out[:, inner_here : inner_here + state_dim].reshape(
        tiles_dev, tile_len, state_dim
    ).transpose(0, 2, 1)
    contrib = contrib_tiles(conv_out, b_t, to_end, inner_here, state_dim)
    passing = jnp.exp(cumul[:, tile_len - 1, :]) * (1.0 - has_bound)[:, None]
    through = jnp.cumprod(passing, 0)
    prefix = jnp.concatenate([jnp.ones((1, heads_here), jnp.float32), through[:-1]], 0)
    reverse = jnp.cumprod(passing[::-1], 0)[::-1]
    to_last = jnp.concatenate([reverse[1:], jnp.ones((1, heads_here), jnp.float32)], 0)
    widen = lambda per_head: jnp.repeat(per_head, head_dim, axis=-1)
    run_state = jnp.sum(widen(to_last)[:, None, :] * contrib, 0)
    passing_wide = widen(passing)
    running = jnp.zeros((state_dim, inner_here), jnp.float32)
    states = []
    for tile in range(tiles_dev):
        states.append(running)
        running = passing_wide[tile][None, :] * running + contrib[tile]
    before_tile = jnp.stack(states)
    position = lax.axis_index("seq")
    run_decay = widen(through[tiles_dev - 1])
    distance = 1
    def with_decay(state, decay):
        high = decay.astype(jnp.bfloat16)
        rest = decay - high.astype(jnp.float32)
        middle = rest.astype(jnp.bfloat16)
        low = (rest - middle.astype(jnp.float32)).astype(jnp.bfloat16)
        return jnp.concatenate([state.astype(jnp.bfloat16), high[None], middle[None], low[None]], 0)

    def unpack(got):
        got = got.astype(jnp.float32)
        return got[:state_dim], got[state_dim] + got[state_dim + 1] + got[state_dim + 2]

    while 2 * distance < seq_count:
        got_state, got_decay = unpack(shifted(with_decay(run_state, run_decay), "seq", distance))
        run_state = run_state + run_decay[None, :] * got_state
        run_decay = jnp.where(position >= distance, run_decay * got_decay, run_decay)
        distance *= 2
    near_state, near_decay = unpack(shifted(with_decay(run_state, run_decay), "seq", 1))
    far_state = shifted(run_state.astype(jnp.bfloat16), "seq", distance + 1).astype(jnp.float32)
    entering = near_state + near_decay[None, :] * far_state
    tile_state = before_tile + widen(prefix)[:, None, :] * entering[None]
    carried = tile_state.astype(jnp.bfloat16)
    d_full = jnp.repeat(d_skip, head_dim)[None, :]
    gated, row_sq = mix_tiles(conv_out, zx, cumul, cumul_t, dt_t, later, carried, d_full)
    sums = lax.psum(row_sq, "head")
    return (gated * lax.rsqrt(sums / INNER + EPSILON) * norm_gain[None, :]).astype(jnp.bfloat16)


def solution(mesh):
    return jax.shard_map(
        shards,
        mesh=mesh,
        in_specs=(
            P("seq", None, "head"),
            P("seq"),
            P("seq"),
            P(None, None, "head"),
            P(),
            P(None, "head"),
            P("head"),
            P("head"),
            P(None, "head"),
            P(),
            P("head"),
            P(),
            P("head"),
            P("head"),
        ),
        out_specs=P("seq", "head"),
        check_vma=False,
    )
```

```python
import jax
import jax.numpy as jnp
from jax import lax
from jax.experimental import pallas as pl
from jax.experimental.pallas import tpu as pltpu
from jax.sharding import PartitionSpec as P

INNER = 2048


EPSILON = 1e-05


def shifted(x, axis, by):
    devices = lax.axis_size(axis)
    pairs = [(i, i + by) for i in range(devices) if 0 <= i + by < devices]
    return lax.ppermute(x, axis, pairs)


def mix_tile(
    x_ref, b_ref, c_ref, cum_ref, cumt_ref, dtt_ref, partc_ref, partr_ref, car_ref, gate_ref, d_ref,
    out_ref, sq_ref,
):
    f32 = jnp.float32
    tile_len = x_ref.shape[0]
    pairs = x_ref.shape[1] // 128
    b_mat = b_ref[...]
    c_mat = c_ref[...]
    scores = lax.dot_general(
        c_mat, b_mat, (((1,), (1,)), ((), ())), preferred_element_type=f32
    )
    cum = cum_ref[0]
    cumt = cumt_ref[0]
    dtt = dtt_ref[0]
    part_col = partc_ref[0]
    part_row = partr_ref[0]
    row = lax.broadcasted_iota(jnp.int32, (tile_len, tile_len), 0)
    col = lax.broadcasted_iota(jnp.int32, (tile_len, tile_len), 1)
    keep = (row >= col) & (part_col == part_row)
    earlier = 1.0 - part_col
    first_half = lax.broadcasted_iota(jnp.int32, (tile_len, 128), 1) < 64
    total_sq = jnp.zeros((tile_len, 128), f32)
    for pair in range(pairs):
        cols = pl.ds(pair * 128, 128)
        x_pair = x_ref[:, cols]
        slabs = []
        for half in range(2):
            head = 2 * pair + half
            diff = cum[:, head : head + 1] - cumt[head : head + 1, :]
            decay = jnp.where(keep, jnp.exp(jnp.where(keep, diff, 0.0)), 0.0)
            slabs.append((scores * decay * dtt[head : head + 1, :]).astype(jnp.bfloat16))
        weights = jnp.concatenate(slabs, axis=1)
        zero = jnp.zeros_like(x_pair)
        split_x = jnp.concatenate(
            [jnp.where(first_half, x_pair, zero), jnp.where(first_half, zero, x_pair)], axis=0
        )
        intra = jnp.dot(weights, split_x, preferred_element_type=f32)
        projected = jnp.dot(c_mat, car_ref[0, :, cols], preferred_element_type=f32)
        grow = jnp.where(
            first_half,
            jnp.exp(cum[:, 2 * pair : 2 * pair + 1]),
            jnp.exp(cum[:, 2 * pair + 1 : 2 * pair + 2]),
        )
        inter = grow * earlier * projected
        mixed = intra + inter + d_ref[:, cols] * x_pair.astype(f32)
        gate = gate_ref[:, cols].astype(f32)
        gated = mixed * (gate * (0.5 + 0.5 * jnp.tanh(0.5 * gate)))
        out_ref[:, cols] = gated
        total_sq = total_sq + gated * gated
    sq_ref[...] = jnp.sum(total_sq, axis=1, keepdims=True)


def contrib_tile(x_ref, bt_ref, end_ref, out_ref):
    f32 = jnp.float32
    tile_len = x_ref.shape[0]
    pairs = x_ref.shape[1] // 128
    b_t = bt_ref[0]
    to_end = end_ref[0]
    first_half = lax.broadcasted_iota(jnp.int32, (tile_len, 128), 1) < 64
    for pair in range(pairs):
        cols = pl.ds(pair * 128, 128)
        scale = jnp.where(
            first_half, to_end[:, 2 * pair : 2 * pair + 1], to_end[:, 2 * pair + 1 : 2 * pair + 2]
        )
        scaled = (x_ref[:, cols].astype(f32) * scale).astype(jnp.bfloat16)
        out_ref[0, :, cols] = jnp.dot(b_t, scaled, preferred_element_type=f32)


def contrib_tiles(conv_out, b_t, to_end, inner_here, state_dim):
    tiles_dev, tile_len, heads_here = to_end.shape
    return pl.pallas_call(
        contrib_tile,
        grid=(tiles_dev,),
        in_specs=[
            pl.BlockSpec((tile_len, inner_here), lambda j: (j, 0)),
            pl.BlockSpec((1, state_dim, tile_len), lambda j: (j, 0, 0)),
            pl.BlockSpec((1, tile_len, heads_here), lambda j: (j, 0, 0)),
        ],
        out_specs=pl.BlockSpec((1, state_dim, inner_here), lambda j: (j, 0, 0)),
        out_shape=jax.ShapeDtypeStruct((tiles_dev, state_dim, inner_here), jnp.float32),
        cost_estimate=pl.CostEstimate(
            flops=tiles_dev * 2 * tile_len * inner_here * state_dim,
            transcendentals=0,
            bytes_accessed=tiles_dev * (tile_len * (inner_here + state_dim) * 2 + inner_here * state_dim * 4),
        ),
    )(conv_out, b_t, to_end)


def mix_tiles(conv_out, zx, cumul, cumul_t, dt_t, later, carried, d_full):
    tiles_dev, tile_len, heads_here = cumul.shape
    inner_here = carried.shape[2]
    state_dim = carried.shape[1]
    rows = tiles_dev * tile_len
    b_block = inner_here // 128
    c_block = b_block + state_dim // 128
    part_col = later.reshape(tiles_dev, tile_len, 1)
    part_row = later.reshape(tiles_dev, 1, tile_len)
    per_tile = lambda j: (j, 0, 0)
    return pl.pallas_call(
        mix_tile,
        grid=(tiles_dev,),
        in_specs=[
            pl.BlockSpec((tile_len, inner_here), lambda j: (j, 0)),
            pl.BlockSpec((tile_len, state_dim), lambda j: (j, b_block)),
            pl.BlockSpec((tile_len, state_dim), lambda j: (j, c_block)),
            pl.BlockSpec((1, tile_len, heads_here), per_tile),
            pl.BlockSpec((1, heads_here, tile_len), per_tile),
            pl.BlockSpec((1, heads_here, tile_len), per_tile),
            pl.BlockSpec((1, tile_len, 1), per_tile),
            pl.BlockSpec((1, 1, tile_len), per_tile),
            pl.BlockSpec((1, state_dim, inner_here), per_tile),
            pl.BlockSpec((tile_len, inner_here), lambda j: (j, 0)),
            pl.BlockSpec((1, inner_here), lambda j: (0, 0)),
        ],
        out_specs=[
            pl.BlockSpec((tile_len, inner_here), lambda j: (j, 0)),
            pl.BlockSpec((tile_len, 1), lambda j: (j, 0)),
        ],
        out_shape=[
            jax.ShapeDtypeStruct((rows, inner_here), jnp.float32),
            jax.ShapeDtypeStruct((rows, 1), jnp.float32),
        ],
        cost_estimate=pl.CostEstimate(
            flops=tiles_dev * (2 * tile_len * tile_len * (state_dim + 4 * inner_here + 2 * inner_here)),
            transcendentals=tiles_dev * tile_len * (tile_len * heads_here + 2 * inner_here),
            bytes_accessed=rows * inner_here * 10 + tiles_dev * inner_here * state_dim * 2,
        ),
    )(conv_out, conv_out, conv_out, cumul, cumul_t, dt_t, part_col, part_row, carried, zx, d_full)


def shards(
    ingest,
    dest_tile,
    doc_start,
    w_zx,
    w_bc,
    w_dt,
    dt_bias,
    a_log,
    conv_x,
    conv_bc,
    cbias_x,
    cbias_bc,
    d_skip,
    norm_gain,
):
    seq_count = lax.axis_size("seq")
    tiles_dev = ingest.shape[0]
    tile_len = ingest.shape[1]
    columns = ingest.shape[2]
    row_count = tiles_dev * tile_len
    heads_here = a_log.shape[0]
    inner_here = conv_x.shape[1]
    head_dim = inner_here // heads_here
    state_dim = conv_bc.shape[1] // 2
    taps = conv_x.shape[0]
    keep_rows = taps - 1
    owner = dest_tile // tiles_dev
    slots = jnp.arange(seq_count, dtype=jnp.int32)
    pick = (owner[None, :] == slots[:, None]).astype(jnp.float32)
    outgoing = jnp.einsum(
        "sj,jrc->src", pick.astype(jnp.bfloat16), ingest, preferred_element_type=jnp.float32
    ).astype(jnp.bfloat16)
    incoming = lax.all_to_all(outgoing, "seq", split_axis=0, concat_axis=0, tiled=True)
    zx_cols, gather_dest = lax.optimization_barrier((w_zx.reshape(w_zx.shape[0], -1), dest_tile))
    every_dest = lax.all_gather(gather_dest, "seq", tiled=True).reshape(seq_count, tiles_dev)
    mine = every_dest // tiles_dev == lax.axis_index("seq")
    got_slot = jnp.sum(jnp.where(mine, every_dest % tiles_dev, 0), 1)
    local_slots = jnp.arange(tiles_dev, dtype=jnp.int32)
    place = (got_slot[None, :] == local_slots[:, None]).astype(jnp.bfloat16)
    arrived = jnp.einsum("js,src->jrc", place, incoming, preferred_element_type=jnp.float32).astype(
        jnp.bfloat16
    )
    own_rows = arrived.reshape(row_count, columns)
    weight_set = (zx_cols, w_bc, w_dt)
    piece = lax.all_gather(own_rows, "head", axis=1, tiled=True)
    acc_zx, acc_bc, acc_dt = tuple(
        (jnp.dot(piece, weight, preferred_element_type=jnp.float32) for weight in weight_set)
    )
    zx = acc_zx.astype(jnp.bfloat16)
    x_in = zx[:, inner_here:]
    bc_all = acc_bc.astype(jnp.bfloat16)
    step_dt = jax.nn.softplus(acc_dt + dt_bias[None, :])
    within = jnp.arange(tile_len, dtype=jnp.int32)
    has_bound = (doc_start < tile_len).astype(jnp.float32)
    before_count = jnp.cumsum(has_bound) - has_bound
    later = (within[None, :] >= doc_start[:, None]).astype(jnp.float32)
    segment = (before_count[:, None] + later).reshape(row_count)
    conv_in = jnp.concatenate([x_in, bc_all], 1)
    tail = conv_in[row_count - keep_rows :]
    tail_seg = (segment[row_count - keep_rows :] - segment[row_count - 1]).astype(jnp.bfloat16)
    got_tail, got_seg = shifted((tail, tail_seg), "seq", 1)
    extended = jnp.concatenate([got_tail, conv_in], 0)
    ext_seg = jnp.concatenate([got_seg.astype(jnp.float32), segment], 0)
    conv_weight = jnp.concatenate([conv_x, conv_bc], 1)
    conv_bias = jnp.concatenate([cbias_x, cbias_bc], 0)
    total = conv_bias[None, :] + conv_weight[taps - 1][None, :] * conv_in.astype(jnp.float32)
    for back_step in range(keep_rows):
        same = ext_seg[back_step : back_step + row_count] == segment
        total = total + jnp.where(
            same[:, None],
            conv_weight[back_step][None, :]
            * extended[back_step : back_step + row_count].astype(jnp.float32),
            0.0,
        )
    conv_out = jax.nn.silu(total).astype(jnp.bfloat16)
    rate = -jnp.exp(a_log)
    tile_dt = step_dt.reshape(tiles_dev, tile_len, heads_here)
    lower = (within[:, None] >= within[None, :]).astype(jnp.float32)
    cumul = jnp.einsum(
        "is,jsh->jih", lower, tile_dt * rate[None, None, :], precision=lax.Precision.HIGHEST
    )
    cumul_t = cumul.transpose(0, 2, 1)
    dt_t = tile_dt.transpose(0, 2, 1)
    last_part = later[:, tile_len - 1]
    tail_keep = (later == last_part[:, None]).astype(jnp.float32)
    to_end = jnp.exp(cumul[:, tile_len - 1 :, :] - cumul) * tile_dt * tail_keep[:, :, None]
    b_t = conv_out[:, inner_here : inner_here + state_dim].reshape(
        tiles_dev, tile_len, state_dim
    ).transpose(0, 2, 1)
    contrib = contrib_tiles(conv_out, b_t, to_end, inner_here, state_dim)
    passing = jnp.exp(cumul[:, tile_len - 1, :]) * (1.0 - has_bound)[:, None]
    through = jnp.cumprod(passing, 0)
    prefix = jnp.concatenate([jnp.ones((1, heads_here), jnp.float32), through[:-1]], 0)
    reverse = jnp.cumprod(passing[::-1], 0)[::-1]
    to_last = jnp.concatenate([reverse[1:], jnp.ones((1, heads_here), jnp.float32)], 0)
    widen = lambda per_head: jnp.repeat(per_head, head_dim, axis=-1)
    run_state = jnp.sum(widen(to_last)[:, None, :] * contrib, 0)
    passing_wide = widen(passing)
    running = jnp.zeros((state_dim, inner_here), jnp.float32)
    states = []
    for tile in range(tiles_dev):
        states.append(running)
        running = passing_wide[tile][None, :] * running + contrib[tile]
    before_tile = jnp.stack(states)
    position = lax.axis_index("seq")
    run_decay = widen(through[tiles_dev - 1])
    distance = 1
    def with_decay(state, decay):
        high = decay.astype(jnp.bfloat16)
        rest = decay - high.astype(jnp.float32)
        middle = rest.astype(jnp.bfloat16)
        low = (rest - middle.astype(jnp.float32)).astype(jnp.bfloat16)
        return jnp.concatenate([state.astype(jnp.bfloat16), high[None], middle[None], low[None]], 0)

    def unpack(got):
        got = got.astype(jnp.float32)
        return got[:state_dim], got[state_dim] + got[state_dim + 1] + got[state_dim + 2]

    while 2 * distance < seq_count:
        got_state, got_decay = unpack(shifted(with_decay(run_state, run_decay), "seq", distance))
        run_state = run_state + run_decay[None, :] * got_state
        run_decay = jnp.where(position >= distance, run_decay * got_decay, run_decay)
        distance *= 2
    near_state, near_decay = unpack(shifted(with_decay(run_state, run_decay), "seq", 1))
    far_state = shifted(run_state.astype(jnp.bfloat16), "seq", distance + 1).astype(jnp.float32)
    entering = near_state + near_decay[None, :] * far_state
    tile_state = before_tile + widen(prefix)[:, None, :] * entering[None]
    carried = tile_state.astype(jnp.bfloat16)
    d_full = jnp.repeat(d_skip, head_dim)[None, :]
    gated, row_sq = mix_tiles(conv_out, zx, cumul, cumul_t, dt_t, later, carried, d_full)
    sums = lax.psum(row_sq, "head")
    return (gated * lax.rsqrt(sums / INNER + EPSILON) * norm_gain[None, :]).astype(jnp.bfloat16)


def solution(mesh):
    return jax.shard_map(
        shards,
        mesh=mesh,
        in_specs=(
            P("seq", None, "head"),
            P("seq"),
            P("seq"),
            P(None, None, "head"),
            P(),
            P(None, "head"),
            P("head"),
            P("head"),
            P(None, "head"),
            P(),
            P("head"),
            P(),
            P("head"),
            P("head"),
        ),
        out_specs=P("seq", "head"),
        check_vma=False,
    )
```

```python
import jax
import jax.numpy as jnp
from jax import lax
from jax.experimental import pallas as pl
from jax.experimental.pallas import tpu as pltpu
from jax.sharding import PartitionSpec as P

INNER = 2048


EPSILON = 1e-05


def shifted(x, axis, by):
    devices = lax.axis_size(axis)
    pairs = [(i, i + by) for i in range(devices) if 0 <= i + by < devices]
    return lax.ppermute(x, axis, pairs)


def mix_tile(
    x_ref, b_ref, c_ref, cum_ref, cumt_ref, dtt_ref, partc_ref, partr_ref, before_ref, prefix_ref,
    enter_ref, gate_ref, d_ref, out_ref, sq_ref,
):
    f32 = jnp.float32
    tile_len = x_ref.shape[0]
    pairs = x_ref.shape[1] // 128
    b_mat = b_ref[...]
    c_mat = c_ref[...]
    scores = lax.dot_general(
        c_mat, b_mat, (((1,), (1,)), ((), ())), preferred_element_type=f32
    )
    cum = cum_ref[0]
    cumt = cumt_ref[0]
    dtt = dtt_ref[0]
    part_col = partc_ref[0]
    part_row = partr_ref[0]
    row = lax.broadcasted_iota(jnp.int32, (tile_len, tile_len), 0)
    col = lax.broadcasted_iota(jnp.int32, (tile_len, tile_len), 1)
    keep = (row >= col) & (part_col == part_row)
    earlier = 1.0 - part_col
    first_half = lax.broadcasted_iota(jnp.int32, (tile_len, 128), 1) < 64
    total_sq = jnp.zeros((tile_len, 128), f32)
    for pair in range(pairs):
        cols = pl.ds(pair * 128, 128)
        x_pair = x_ref[:, cols]
        slabs = []
        for half in range(2):
            head = 2 * pair + half
            diff = cum[:, head : head + 1] - cumt[head : head + 1, :]
            decay = jnp.where(keep, jnp.exp(jnp.where(keep, diff, 0.0)), 0.0)
            slabs.append((scores * decay * dtt[head : head + 1, :]).astype(jnp.bfloat16))
        weights = jnp.concatenate(slabs, axis=1)
        zero = jnp.zeros_like(x_pair)
        split_x = jnp.concatenate(
            [jnp.where(first_half, x_pair, zero), jnp.where(first_half, zero, x_pair)], axis=0
        )
        intra = jnp.dot(weights, split_x, preferred_element_type=f32)
        carried = (
            before_ref[0, :, cols] + prefix_ref[0, :, cols] * enter_ref[:, cols]
        ).astype(jnp.bfloat16)
        projected = jnp.dot(c_mat, carried, preferred_element_type=f32)
        grow = jnp.where(
            first_half,
            jnp.exp(cum[:, 2 * pair : 2 * pair + 1]),
            jnp.exp(cum[:, 2 * pair + 1 : 2 * pair + 2]),
        )
        inter = grow * earlier * projected
        mixed = intra + inter + d_ref[:, cols] * x_pair.astype(f32)
        gate = gate_ref[:, cols].astype(f32)
        gated = mixed * (gate * (0.5 + 0.5 * jnp.tanh(0.5 * gate)))
        out_ref[:, cols] = gated
        total_sq = total_sq + gated * gated
    sq_ref[...] = jnp.sum(total_sq, axis=1, keepdims=True)


def contrib_tile(x_ref, bt_ref, end_ref, out_ref):
    f32 = jnp.float32
    tile_len = x_ref.shape[0]
    pairs = x_ref.shape[1] // 128
    b_t = bt_ref[0]
    to_end = end_ref[0]
    first_half = lax.broadcasted_iota(jnp.int32, (tile_len, 128), 1) < 64
    for pair in range(pairs):
        cols = pl.ds(pair * 128, 128)
        scale = jnp.where(
            first_half, to_end[:, 2 * pair : 2 * pair + 1], to_end[:, 2 * pair + 1 : 2 * pair + 2]
        )
        scaled = (x_ref[:, cols].astype(f32) * scale).astype(jnp.bfloat16)
        out_ref[0, :, cols] = jnp.dot(b_t, scaled, preferred_element_type=f32)


def contrib_tiles(conv_out, b_t, to_end, inner_here, state_dim):
    tiles_dev, tile_len, heads_here = to_end.shape
    return pl.pallas_call(
        contrib_tile,
        grid=(tiles_dev,),
        in_specs=[
            pl.BlockSpec((tile_len, inner_here), lambda j: (j, 0)),
            pl.BlockSpec((1, state_dim, tile_len), lambda j: (j, 0, 0)),
            pl.BlockSpec((1, tile_len, heads_here), lambda j: (j, 0, 0)),
        ],
        out_specs=pl.BlockSpec((1, state_dim, inner_here), lambda j: (j, 0, 0)),
        out_shape=jax.ShapeDtypeStruct((tiles_dev, state_dim, inner_here), jnp.float32),
        cost_estimate=pl.CostEstimate(
            flops=tiles_dev * 2 * tile_len * inner_here * state_dim,
            transcendentals=0,
            bytes_accessed=tiles_dev * (tile_len * (inner_here + state_dim) * 2 + inner_here * state_dim * 4),
        ),
    )(conv_out, b_t, to_end)


def mix_tiles(conv_out, zx, cumul, cumul_t, dt_t, later, before_tile, prefix_wide, entering, d_full):
    tiles_dev, tile_len, heads_here = cumul.shape
    inner_here = before_tile.shape[2]
    state_dim = before_tile.shape[1]
    rows = tiles_dev * tile_len
    b_block = inner_here // 128
    c_block = b_block + state_dim // 128
    part_col = later.reshape(tiles_dev, tile_len, 1)
    part_row = later.reshape(tiles_dev, 1, tile_len)
    per_tile = lambda j: (j, 0, 0)
    return pl.pallas_call(
        mix_tile,
        grid=(tiles_dev,),
        in_specs=[
            pl.BlockSpec((tile_len, inner_here), lambda j: (j, 0)),
            pl.BlockSpec((tile_len, state_dim), lambda j: (j, b_block)),
            pl.BlockSpec((tile_len, state_dim), lambda j: (j, c_block)),
            pl.BlockSpec((1, tile_len, heads_here), per_tile),
            pl.BlockSpec((1, heads_here, tile_len), per_tile),
            pl.BlockSpec((1, heads_here, tile_len), per_tile),
            pl.BlockSpec((1, tile_len, 1), per_tile),
            pl.BlockSpec((1, 1, tile_len), per_tile),
            pl.BlockSpec((1, state_dim, inner_here), per_tile),
            pl.BlockSpec((1, 1, inner_here), per_tile),
            pl.BlockSpec((state_dim, inner_here), lambda j: (0, 0)),
            pl.BlockSpec((tile_len, inner_here), lambda j: (j, 0)),
            pl.BlockSpec((1, inner_here), lambda j: (0, 0)),
        ],
        out_specs=[
            pl.BlockSpec((tile_len, inner_here), lambda j: (j, 0)),
            pl.BlockSpec((tile_len, 1), lambda j: (j, 0)),
        ],
        out_shape=[
            jax.ShapeDtypeStruct((rows, inner_here), jnp.float32),
            jax.ShapeDtypeStruct((rows, 1), jnp.float32),
        ],
        cost_estimate=pl.CostEstimate(
            flops=tiles_dev * (2 * tile_len * tile_len * (state_dim + 4 * inner_here + 2 * inner_here)),
            transcendentals=tiles_dev * tile_len * (tile_len * heads_here + 2 * inner_here),
            bytes_accessed=rows * inner_here * 10 + tiles_dev * inner_here * state_dim * 4,
        ),
    )(
        conv_out, conv_out, conv_out, cumul, cumul_t, dt_t, part_col, part_row,
        before_tile, prefix_wide, entering, zx, d_full,
    )


def shards(
    ingest,
    dest_tile,
    doc_start,
    w_zx,
    w_bc,
    w_dt,
    dt_bias,
    a_log,
    conv_x,
    conv_bc,
    cbias_x,
    cbias_bc,
    d_skip,
    norm_gain,
):
    seq_count = lax.axis_size("seq")
    tiles_dev = ingest.shape[0]
    tile_len = ingest.shape[1]
    columns = ingest.shape[2]
    row_count = tiles_dev * tile_len
    heads_here = a_log.shape[0]
    inner_here = conv_x.shape[1]
    head_dim = inner_here // heads_here
    state_dim = conv_bc.shape[1] // 2
    taps = conv_x.shape[0]
    keep_rows = taps - 1
    owner = dest_tile // tiles_dev
    slots = jnp.arange(seq_count, dtype=jnp.int32)
    pick = (owner[None, :] == slots[:, None]).astype(jnp.float32)
    outgoing = jnp.einsum(
        "sj,jrc->src", pick.astype(jnp.bfloat16), ingest, preferred_element_type=jnp.float32
    ).astype(jnp.bfloat16)
    incoming = lax.all_to_all(outgoing, "seq", split_axis=0, concat_axis=0, tiled=True)
    zx_cols, gather_dest = lax.optimization_barrier((w_zx.reshape(w_zx.shape[0], -1), dest_tile))
    every_dest = lax.all_gather(gather_dest, "seq", tiled=True).reshape(seq_count, tiles_dev)
    mine = every_dest // tiles_dev == lax.axis_index("seq")
    got_slot = jnp.sum(jnp.where(mine, every_dest % tiles_dev, 0), 1)
    local_slots = jnp.arange(tiles_dev, dtype=jnp.int32)
    place = (got_slot[None, :] == local_slots[:, None]).astype(jnp.bfloat16)
    arrived = jnp.einsum("js,src->jrc", place, incoming, preferred_element_type=jnp.float32).astype(
        jnp.bfloat16
    )
    own_rows = arrived.reshape(row_count, columns)
    weight_set = (zx_cols, w_bc, w_dt)
    piece = lax.all_gather(own_rows, "head", axis=1, tiled=True)
    acc_zx, acc_bc, acc_dt = tuple(
        (jnp.dot(piece, weight, preferred_element_type=jnp.float32) for weight in weight_set)
    )
    zx = acc_zx.astype(jnp.bfloat16)
    x_in = zx[:, inner_here:]
    bc_all = acc_bc.astype(jnp.bfloat16)
    step_dt = jax.nn.softplus(acc_dt + dt_bias[None, :])
    within = jnp.arange(tile_len, dtype=jnp.int32)
    has_bound = (doc_start < tile_len).astype(jnp.float32)
    before_count = jnp.cumsum(has_bound) - has_bound
    later = (within[None, :] >= doc_start[:, None]).astype(jnp.float32)
    segment = (before_count[:, None] + later).reshape(row_count)
    conv_in = jnp.concatenate([x_in, bc_all], 1)
    tail = conv_in[row_count - keep_rows :]
    tail_seg = (segment[row_count - keep_rows :] - segment[row_count - 1]).astype(jnp.bfloat16)
    got_tail, got_seg = shifted((tail, tail_seg), "seq", 1)
    extended = jnp.concatenate([got_tail, conv_in], 0)
    ext_seg = jnp.concatenate([got_seg.astype(jnp.float32), segment], 0)
    conv_weight = jnp.concatenate([conv_x, conv_bc], 1)
    conv_bias = jnp.concatenate([cbias_x, cbias_bc], 0)
    total = conv_bias[None, :] + conv_weight[taps - 1][None, :] * conv_in.astype(jnp.float32)
    for back_step in range(keep_rows):
        same = ext_seg[back_step : back_step + row_count] == segment
        total = total + jnp.where(
            same[:, None],
            conv_weight[back_step][None, :]
            * extended[back_step : back_step + row_count].astype(jnp.float32),
            0.0,
        )
    conv_out = jax.nn.silu(total).astype(jnp.bfloat16)
    rate = -jnp.exp(a_log)
    tile_dt = step_dt.reshape(tiles_dev, tile_len, heads_here)
    lower = (within[:, None] >= within[None, :]).astype(jnp.float32)
    cumul = jnp.einsum(
        "is,jsh->jih", lower, tile_dt * rate[None, None, :], precision=lax.Precision.HIGHEST
    )
    cumul_t = cumul.transpose(0, 2, 1)
    dt_t = tile_dt.transpose(0, 2, 1)
    last_part = later[:, tile_len - 1]
    tail_keep = (later == last_part[:, None]).astype(jnp.float32)
    to_end = jnp.exp(cumul[:, tile_len - 1 :, :] - cumul) * tile_dt * tail_keep[:, :, None]
    b_t = conv_out[:, inner_here : inner_here + state_dim].reshape(
        tiles_dev, tile_len, state_dim
    ).transpose(0, 2, 1)
    contrib = contrib_tiles(conv_out, b_t, to_end, inner_here, state_dim)
    passing = jnp.exp(cumul[:, tile_len - 1, :]) * (1.0 - has_bound)[:, None]
    through = jnp.cumprod(passing, 0)
    prefix = jnp.concatenate([jnp.ones((1, heads_here), jnp.float32), through[:-1]], 0)
    reverse = jnp.cumprod(passing[::-1], 0)[::-1]
    to_last = jnp.concatenate([reverse[1:], jnp.ones((1, heads_here), jnp.float32)], 0)
    widen = lambda per_head: jnp.repeat(per_head, head_dim, axis=-1)
    run_state = jnp.sum(widen(to_last)[:, None, :] * contrib, 0)
    passing_wide = widen(passing)
    running = jnp.zeros((state_dim, inner_here), jnp.float32)
    states = []
    for tile in range(tiles_dev):
        states.append(running)
        running = passing_wide[tile][None, :] * running + contrib[tile]
    before_tile = jnp.stack(states)
    position = lax.axis_index("seq")
    run_decay = widen(through[tiles_dev - 1])
    distance = 1
    def with_decay(state, decay):
        high = decay.astype(jnp.bfloat16)
        rest = decay - high.astype(jnp.float32)
        middle = rest.astype(jnp.bfloat16)
        low = (rest - middle.astype(jnp.float32)).astype(jnp.bfloat16)
        return jnp.concatenate([state.astype(jnp.bfloat16), high[None], middle[None], low[None]], 0)

    def unpack(got):
        got = got.astype(jnp.float32)
        return got[:state_dim], got[state_dim] + got[state_dim + 1] + got[state_dim + 2]

    while 2 * distance < seq_count:
        got_state, got_decay = unpack(shifted(with_decay(run_state, run_decay), "seq", distance))
        run_state = run_state + run_decay[None, :] * got_state
        run_decay = jnp.where(position >= distance, run_decay * got_decay, run_decay)
        distance *= 2
    near_state, near_decay = unpack(shifted(with_decay(run_state, run_decay), "seq", 1))
    far_state = shifted(run_state.astype(jnp.bfloat16), "seq", distance + 1).astype(jnp.float32)
    entering = near_state + near_decay[None, :] * far_state
    d_full = jnp.repeat(d_skip, head_dim)[None, :]
    gated, row_sq = mix_tiles(
        conv_out, zx, cumul, cumul_t, dt_t, later, before_tile, widen(prefix)[:, None, :],
        entering, d_full,
    )
    sums = lax.psum(row_sq, "head")
    return (gated * lax.rsqrt(sums / INNER + EPSILON) * norm_gain[None, :]).astype(jnp.bfloat16)


def solution(mesh):
    return jax.shard_map(
        shards,
        mesh=mesh,
        in_specs=(
            P("seq", None, "head"),
            P("seq"),
            P("seq"),
            P(None, None, "head"),
            P(),
            P(None, "head"),
            P("head"),
            P("head"),
            P(None, "head"),
            P(),
            P("head"),
            P(),
            P("head"),
            P("head"),
        ),
        out_specs=P("seq", "head"),
        check_vma=False,
    )
```

```python
import jax
import jax.numpy as jnp
from jax import lax
from jax.experimental import pallas as pl
from jax.experimental.pallas import tpu as pltpu
from jax.sharding import PartitionSpec as P

INNER = 2048


EPSILON = 1e-05


def shifted(x, axis, by):
    devices = lax.axis_size(axis)
    pairs = [(i, i + by) for i in range(devices) if 0 <= i + by < devices]
    return lax.ppermute(x, axis, pairs)


def mix_tile(
    x_ref, b_ref, c_ref, cum_ref, cumt_ref, dtt_ref, partc_ref, partr_ref, before_ref, prefix_ref,
    enter_ref, gate_ref, d_ref, out_ref, sq_ref,
):
    f32 = jnp.float32
    tile_len = x_ref.shape[0]
    pairs = x_ref.shape[1] // 128
    b_mat = b_ref[...]
    c_mat = c_ref[...]
    scores = lax.dot_general(
        c_mat, b_mat, (((1,), (1,)), ((), ())), preferred_element_type=f32
    )
    cum = cum_ref[0]
    cumt = cumt_ref[0]
    dtt = dtt_ref[0]
    part_col = partc_ref[0]
    part_row = partr_ref[0]
    row = lax.broadcasted_iota(jnp.int32, (tile_len, tile_len), 0)
    col = lax.broadcasted_iota(jnp.int32, (tile_len, tile_len), 1)
    keep = (row >= col) & (part_col == part_row)
    earlier = 1.0 - part_col
    first_half = lax.broadcasted_iota(jnp.int32, (tile_len, 128), 1) < 64
    total_sq = jnp.zeros((tile_len, 128), f32)
    for pair in range(pairs):
        cols = pl.ds(pair * 128, 128)
        x_pair = x_ref[:, cols]
        slabs = []
        for half in range(2):
            head = 2 * pair + half
            diff = cum[:, head : head + 1] - cumt[head : head + 1, :]
            decay = jnp.where(keep, jnp.exp(jnp.where(keep, diff, 0.0)), 0.0)
            slabs.append((scores * decay * dtt[head : head + 1, :]).astype(jnp.bfloat16))
        weights = jnp.concatenate(slabs, axis=1)
        zero = jnp.zeros_like(x_pair)
        split_x = jnp.concatenate(
            [jnp.where(first_half, x_pair, zero), jnp.where(first_half, zero, x_pair)], axis=0
        )
        intra = jnp.dot(weights, split_x, preferred_element_type=f32)
        carried = (
            before_ref[0, :, cols] + prefix_ref[0, :, cols] * enter_ref[:, cols]
        ).astype(jnp.bfloat16)
        projected = jnp.dot(c_mat, carried, preferred_element_type=f32)
        grow = jnp.where(
            first_half,
            jnp.exp(cum[:, 2 * pair : 2 * pair + 1]),
            jnp.exp(cum[:, 2 * pair + 1 : 2 * pair + 2]),
        )
        inter = grow * earlier * projected
        mixed = intra + inter + d_ref[:, cols] * x_pair.astype(f32)
        gate = gate_ref[:, cols].astype(f32)
        gated = mixed * (gate * (0.5 + 0.5 * jnp.tanh(0.5 * gate)))
        out_ref[:, cols] = gated
        total_sq = total_sq + gated * gated
    sq_ref[...] = jnp.sum(total_sq, axis=1, keepdims=True)


def contrib_tile(x_ref, bt_ref, end_ref, pass_ref, before_ref, total_ref):
    f32 = jnp.float32
    tile_len = x_ref.shape[0]
    pairs = x_ref.shape[1] // 128

    @pl.when(pl.program_id(0) == 0)
    def _():
        total_ref[...] = jnp.zeros_like(total_ref)

    b_t = bt_ref[0]
    to_end = end_ref[0]
    first_half = lax.broadcasted_iota(jnp.int32, (tile_len, 128), 1) < 64
    for pair in range(pairs):
        cols = pl.ds(pair * 128, 128)
        scale = jnp.where(
            first_half, to_end[:, 2 * pair : 2 * pair + 1], to_end[:, 2 * pair + 1 : 2 * pair + 2]
        )
        scaled = (x_ref[:, cols].astype(f32) * scale).astype(jnp.bfloat16)
        contrib = jnp.dot(b_t, scaled, preferred_element_type=f32)
        state = total_ref[:, cols]
        before_ref[0, :, cols] = state
        total_ref[:, cols] = pass_ref[0, :, cols] * state + contrib


def contrib_tiles(conv_out, b_t, to_end, passing_wide, inner_here, state_dim):
    tiles_dev, tile_len, heads_here = to_end.shape
    return pl.pallas_call(
        contrib_tile,
        grid=(tiles_dev,),
        in_specs=[
            pl.BlockSpec((tile_len, inner_here), lambda j: (j, 0)),
            pl.BlockSpec((1, state_dim, tile_len), lambda j: (j, 0, 0)),
            pl.BlockSpec((1, tile_len, heads_here), lambda j: (j, 0, 0)),
            pl.BlockSpec((1, 1, inner_here), lambda j: (j, 0, 0)),
        ],
        out_specs=[
            pl.BlockSpec((1, state_dim, inner_here), lambda j: (j, 0, 0)),
            pl.BlockSpec((state_dim, inner_here), lambda j: (0, 0)),
        ],
        out_shape=[
            jax.ShapeDtypeStruct((tiles_dev, state_dim, inner_here), jnp.float32),
            jax.ShapeDtypeStruct((state_dim, inner_here), jnp.float32),
        ],
        compiler_params=pltpu.CompilerParams(dimension_semantics=("arbitrary",)),
        cost_estimate=pl.CostEstimate(
            flops=tiles_dev * 2 * tile_len * inner_here * state_dim,
            transcendentals=0,
            bytes_accessed=tiles_dev * (tile_len * (inner_here + state_dim) * 2 + inner_here * state_dim * 4),
        ),
    )(conv_out, b_t, to_end, passing_wide)


def mix_tiles(conv_out, zx, cumul, cumul_t, dt_t, later, before_tile, prefix_wide, entering, d_full):
    tiles_dev, tile_len, heads_here = cumul.shape
    inner_here = before_tile.shape[2]
    state_dim = before_tile.shape[1]
    rows = tiles_dev * tile_len
    b_block = inner_here // 128
    c_block = b_block + state_dim // 128
    part_col = later.reshape(tiles_dev, tile_len, 1)
    part_row = later.reshape(tiles_dev, 1, tile_len)
    per_tile = lambda j: (j, 0, 0)
    return pl.pallas_call(
        mix_tile,
        grid=(tiles_dev,),
        in_specs=[
            pl.BlockSpec((tile_len, inner_here), lambda j: (j, 0)),
            pl.BlockSpec((tile_len, state_dim), lambda j: (j, b_block)),
            pl.BlockSpec((tile_len, state_dim), lambda j: (j, c_block)),
            pl.BlockSpec((1, tile_len, heads_here), per_tile),
            pl.BlockSpec((1, heads_here, tile_len), per_tile),
            pl.BlockSpec((1, heads_here, tile_len), per_tile),
            pl.BlockSpec((1, tile_len, 1), per_tile),
            pl.BlockSpec((1, 1, tile_len), per_tile),
            pl.BlockSpec((1, state_dim, inner_here), per_tile),
            pl.BlockSpec((1, 1, inner_here), per_tile),
            pl.BlockSpec((state_dim, inner_here), lambda j: (0, 0)),
            pl.BlockSpec((tile_len, inner_here), lambda j: (j, 0)),
            pl.BlockSpec((1, inner_here), lambda j: (0, 0)),
        ],
        out_specs=[
            pl.BlockSpec((tile_len, inner_here), lambda j: (j, 0)),
            pl.BlockSpec((tile_len, 1), lambda j: (j, 0)),
        ],
        out_shape=[
            jax.ShapeDtypeStruct((rows, inner_here), jnp.float32),
            jax.ShapeDtypeStruct((rows, 1), jnp.float32),
        ],
        cost_estimate=pl.CostEstimate(
            flops=tiles_dev * (2 * tile_len * tile_len * (state_dim + 4 * inner_here + 2 * inner_here)),
            transcendentals=tiles_dev * tile_len * (tile_len * heads_here + 2 * inner_here),
            bytes_accessed=rows * inner_here * 10 + tiles_dev * inner_here * state_dim * 4,
        ),
    )(
        conv_out, conv_out, conv_out, cumul, cumul_t, dt_t, part_col, part_row,
        before_tile, prefix_wide, entering, zx, d_full,
    )


def shards(
    ingest,
    dest_tile,
    doc_start,
    w_zx,
    w_bc,
    w_dt,
    dt_bias,
    a_log,
    conv_x,
    conv_bc,
    cbias_x,
    cbias_bc,
    d_skip,
    norm_gain,
):
    seq_count = lax.axis_size("seq")
    tiles_dev = ingest.shape[0]
    tile_len = ingest.shape[1]
    columns = ingest.shape[2]
    row_count = tiles_dev * tile_len
    heads_here = a_log.shape[0]
    inner_here = conv_x.shape[1]
    head_dim = inner_here // heads_here
    state_dim = conv_bc.shape[1] // 2
    taps = conv_x.shape[0]
    keep_rows = taps - 1
    owner = dest_tile // tiles_dev
    slots = jnp.arange(seq_count, dtype=jnp.int32)
    pick = (owner[None, :] == slots[:, None]).astype(jnp.float32)
    outgoing = jnp.einsum(
        "sj,jrc->src", pick.astype(jnp.bfloat16), ingest, preferred_element_type=jnp.float32
    ).astype(jnp.bfloat16)
    incoming = lax.all_to_all(outgoing, "seq", split_axis=0, concat_axis=0, tiled=True)
    zx_cols, gather_dest = lax.optimization_barrier((w_zx.reshape(w_zx.shape[0], -1), dest_tile))
    every_dest = lax.all_gather(gather_dest, "seq", tiled=True).reshape(seq_count, tiles_dev)
    mine = every_dest // tiles_dev == lax.axis_index("seq")
    got_slot = jnp.sum(jnp.where(mine, every_dest % tiles_dev, 0), 1)
    local_slots = jnp.arange(tiles_dev, dtype=jnp.int32)
    place = (got_slot[None, :] == local_slots[:, None]).astype(jnp.bfloat16)
    arrived = jnp.einsum("js,src->jrc", place, incoming, preferred_element_type=jnp.float32).astype(
        jnp.bfloat16
    )
    own_rows = arrived.reshape(row_count, columns)
    weight_set = (zx_cols, w_bc, w_dt)
    piece = lax.all_gather(own_rows, "head", axis=1, tiled=True)
    acc_zx, acc_bc, acc_dt = tuple(
        (jnp.dot(piece, weight, preferred_element_type=jnp.float32) for weight in weight_set)
    )
    zx = acc_zx.astype(jnp.bfloat16)
    x_in = zx[:, inner_here:]
    bc_all = acc_bc.astype(jnp.bfloat16)
    step_dt = jax.nn.softplus(acc_dt + dt_bias[None, :])
    within = jnp.arange(tile_len, dtype=jnp.int32)
    has_bound = (doc_start < tile_len).astype(jnp.float32)
    before_count = jnp.cumsum(has_bound) - has_bound
    later = (within[None, :] >= doc_start[:, None]).astype(jnp.float32)
    segment = (before_count[:, None] + later).reshape(row_count)
    conv_in = jnp.concatenate([x_in, bc_all], 1)
    tail = conv_in[row_count - keep_rows :]
    tail_seg = (segment[row_count - keep_rows :] - segment[row_count - 1]).astype(jnp.bfloat16)
    got_tail, got_seg = shifted((tail, tail_seg), "seq", 1)
    extended = jnp.concatenate([got_tail, conv_in], 0)
    ext_seg = jnp.concatenate([got_seg.astype(jnp.float32), segment], 0)
    conv_weight = jnp.concatenate([conv_x, conv_bc], 1)
    conv_bias = jnp.concatenate([cbias_x, cbias_bc], 0)
    total = conv_bias[None, :] + conv_weight[taps - 1][None, :] * conv_in.astype(jnp.float32)
    for back_step in range(keep_rows):
        same = ext_seg[back_step : back_step + row_count] == segment
        total = total + jnp.where(
            same[:, None],
            conv_weight[back_step][None, :]
            * extended[back_step : back_step + row_count].astype(jnp.float32),
            0.0,
        )
    conv_out = jax.nn.silu(total).astype(jnp.bfloat16)
    rate = -jnp.exp(a_log)
    tile_dt = step_dt.reshape(tiles_dev, tile_len, heads_here)
    lower = (within[:, None] >= within[None, :]).astype(jnp.float32)
    cumul = jnp.einsum(
        "is,jsh->jih", lower, tile_dt * rate[None, None, :], precision=lax.Precision.HIGHEST
    )
    cumul_t = cumul.transpose(0, 2, 1)
    dt_t = tile_dt.transpose(0, 2, 1)
    last_part = later[:, tile_len - 1]
    tail_keep = (later == last_part[:, None]).astype(jnp.float32)
    to_end = jnp.exp(cumul[:, tile_len - 1 :, :] - cumul) * tile_dt * tail_keep[:, :, None]
    b_t = conv_out[:, inner_here : inner_here + state_dim].reshape(
        tiles_dev, tile_len, state_dim
    ).transpose(0, 2, 1)
    passing = jnp.exp(cumul[:, tile_len - 1, :]) * (1.0 - has_bound)[:, None]
    through = jnp.cumprod(passing, 0)
    prefix = jnp.concatenate([jnp.ones((1, heads_here), jnp.float32), through[:-1]], 0)
    widen = lambda per_head: jnp.repeat(per_head, head_dim, axis=-1)
    before_tile, run_state = contrib_tiles(
        conv_out, b_t, to_end, widen(passing)[:, None, :], inner_here, state_dim
    )
    position = lax.axis_index("seq")
    run_decay = widen(through[tiles_dev - 1])
    distance = 1
    def with_decay(state, decay):
        high = decay.astype(jnp.bfloat16)
        rest = decay - high.astype(jnp.float32)
        middle = rest.astype(jnp.bfloat16)
        low = (rest - middle.astype(jnp.float32)).astype(jnp.bfloat16)
        return jnp.concatenate([state.astype(jnp.bfloat16), high[None], middle[None], low[None]], 0)

    def unpack(got):
        got = got.astype(jnp.float32)
        return got[:state_dim], got[state_dim] + got[state_dim + 1] + got[state_dim + 2]

    while 2 * distance < seq_count:
        got_state, got_decay = unpack(shifted(with_decay(run_state, run_decay), "seq", distance))
        run_state = run_state + run_decay[None, :] * got_state
        run_decay = jnp.where(position >= distance, run_decay * got_decay, run_decay)
        distance *= 2
    near_state, near_decay = unpack(shifted(with_decay(run_state, run_decay), "seq", 1))
    far_state = shifted(run_state.astype(jnp.bfloat16), "seq", distance + 1).astype(jnp.float32)
    entering = near_state + near_decay[None, :] * far_state
    d_full = jnp.repeat(d_skip, head_dim)[None, :]
    gated, row_sq = mix_tiles(
        conv_out, zx, cumul, cumul_t, dt_t, later, before_tile, widen(prefix)[:, None, :],
        entering, d_full,
    )
    sums = lax.psum(row_sq, "head")
    return (gated * lax.rsqrt(sums / INNER + EPSILON) * norm_gain[None, :]).astype(jnp.bfloat16)


def solution(mesh):
    return jax.shard_map(
        shards,
        mesh=mesh,
        in_specs=(
            P("seq", None, "head"),
            P("seq"),
            P("seq"),
            P(None, None, "head"),
            P(),
            P(None, "head"),
            P("head"),
            P("head"),
            P(None, "head"),
            P(),
            P("head"),
            P(),
            P("head"),
            P("head"),
        ),
        out_specs=P("seq", "head"),
        check_vma=False,
    )
```

```python
import jax
import jax.numpy as jnp
from jax import lax
from jax.experimental import pallas as pl
from jax.experimental.pallas import tpu as pltpu
from jax.sharding import PartitionSpec as P

INNER = 2048


EPSILON = 1e-05


def shifted(x, axis, by):
    devices = lax.axis_size(axis)
    pairs = [(i, i + by) for i in range(devices) if 0 <= i + by < devices]
    return lax.ppermute(x, axis, pairs)


def mix_tile(
    x_ref, b_ref, c_ref, cum_ref, cumt_ref, dtt_ref, partc_ref, partr_ref, before_ref, prefix_ref,
    enter_ref, gate_ref, d_ref, out_ref, sq_ref,
):
    f32 = jnp.float32
    tile_len = x_ref.shape[0]
    pairs = x_ref.shape[1] // 128
    b_mat = b_ref[...]
    c_mat = c_ref[...]
    scores = lax.dot_general(
        c_mat, b_mat, (((1,), (1,)), ((), ())), preferred_element_type=f32
    )
    cum = cum_ref[0]
    cumt = cumt_ref[0]
    dtt = dtt_ref[0]
    part_col = partc_ref[0]
    part_row = partr_ref[0]
    row = lax.broadcasted_iota(jnp.int32, (tile_len, tile_len), 0)
    col = lax.broadcasted_iota(jnp.int32, (tile_len, tile_len), 1)
    keep = (row >= col) & (part_col == part_row)
    earlier = 1.0 - part_col
    first_half = lax.broadcasted_iota(jnp.int32, (tile_len, 128), 1) < 64
    total_sq = jnp.zeros((tile_len, 128), f32)
    for pair in range(pairs):
        cols = pl.ds(pair * 128, 128)
        x_pair = x_ref[:, cols]
        slabs = []
        for half in range(2):
            head = 2 * pair + half
            diff = cum[:, head : head + 1] - cumt[head : head + 1, :]
            decay = jnp.where(keep, jnp.exp(jnp.where(keep, diff, 0.0)), 0.0)
            slabs.append((scores * decay * dtt[head : head + 1, :]).astype(jnp.bfloat16))
        weights = jnp.concatenate(slabs, axis=1)
        zero = jnp.zeros_like(x_pair)
        split_x = jnp.concatenate(
            [jnp.where(first_half, x_pair, zero), jnp.where(first_half, zero, x_pair)], axis=0
        )
        intra = jnp.dot(weights, split_x, preferred_element_type=f32)
        carried = (
            before_ref[0, :, cols] + prefix_ref[0, :, cols] * enter_ref[:, cols]
        ).astype(jnp.bfloat16)
        projected = jnp.dot(c_mat, carried, preferred_element_type=f32)
        grow = jnp.where(
            first_half,
            jnp.exp(cum[:, 2 * pair : 2 * pair + 1]),
            jnp.exp(cum[:, 2 * pair + 1 : 2 * pair + 2]),
        )
        inter = grow * earlier * projected
        mixed = intra + inter + d_ref[:, cols] * x_pair.astype(f32)
        gate = gate_ref[:, cols].astype(f32)
        gated = mixed * (gate * (0.5 + 0.5 * jnp.tanh(0.5 * gate)))
        out_ref[:, cols] = gated
        total_sq = total_sq + gated * gated
    sq_ref[...] = jnp.sum(total_sq, axis=1, keepdims=True)


def contrib_tile(x_ref, bt_ref, end_ref, pass_ref, before_ref, total_ref):
    f32 = jnp.float32
    tile_len = x_ref.shape[0]
    pairs = x_ref.shape[1] // 128

    @pl.when(pl.program_id(0) == 0)
    def _():
        total_ref[...] = jnp.zeros_like(total_ref)

    b_t = bt_ref[0]
    to_end = end_ref[0]
    first_half = lax.broadcasted_iota(jnp.int32, (tile_len, 128), 1) < 64
    for pair in range(pairs):
        cols = pl.ds(pair * 128, 128)
        scale = jnp.where(
            first_half, to_end[:, 2 * pair : 2 * pair + 1], to_end[:, 2 * pair + 1 : 2 * pair + 2]
        )
        scaled = (x_ref[:, cols].astype(f32) * scale).astype(jnp.bfloat16)
        contrib = jnp.dot(b_t, scaled, preferred_element_type=f32)
        state = total_ref[:, cols]
        before_ref[0, :, cols] = state
        total_ref[:, cols] = pass_ref[0, :, cols] * state + contrib


def contrib_tiles(conv_out, b_t, to_end, passing_wide, inner_here, state_dim):
    tiles_dev, tile_len, heads_here = to_end.shape
    return pl.pallas_call(
        contrib_tile,
        grid=(tiles_dev,),
        in_specs=[
            pl.BlockSpec((tile_len, inner_here), lambda j: (j, 0)),
            pl.BlockSpec((1, state_dim, tile_len), lambda j: (j, 0, 0)),
            pl.BlockSpec((1, tile_len, heads_here), lambda j: (j, 0, 0)),
            pl.BlockSpec((1, 1, inner_here), lambda j: (j, 0, 0)),
        ],
        out_specs=[
            pl.BlockSpec((1, state_dim, inner_here), lambda j: (j, 0, 0)),
            pl.BlockSpec((state_dim, inner_here), lambda j: (0, 0)),
        ],
        out_shape=[
            jax.ShapeDtypeStruct((tiles_dev, state_dim, inner_here), jnp.float32),
            jax.ShapeDtypeStruct((state_dim, inner_here), jnp.float32),
        ],
        compiler_params=pltpu.CompilerParams(dimension_semantics=("arbitrary",)),
        cost_estimate=pl.CostEstimate(
            flops=tiles_dev * 2 * tile_len * inner_here * state_dim,
            transcendentals=0,
            bytes_accessed=tiles_dev * (tile_len * (inner_here + state_dim) * 2 + inner_here * state_dim * 4),
        ),
    )(conv_out, b_t, to_end, passing_wide)


def mix_tiles(conv_out, zx, cumul, cumul_t, dt_t, later, before_tile, prefix_wide, entering, d_full):
    tiles_dev, tile_len, heads_here = cumul.shape
    inner_here = before_tile.shape[2]
    state_dim = before_tile.shape[1]
    rows = tiles_dev * tile_len
    b_block = inner_here // 128
    c_block = b_block + state_dim // 128
    part_col = later.reshape(tiles_dev, tile_len, 1)
    part_row = later.reshape(tiles_dev, 1, tile_len)
    per_tile = lambda j: (j, 0, 0)
    return pl.pallas_call(
        mix_tile,
        grid=(tiles_dev,),
        in_specs=[
            pl.BlockSpec((tile_len, inner_here), lambda j: (j, 0)),
            pl.BlockSpec((tile_len, state_dim), lambda j: (j, b_block)),
            pl.BlockSpec((tile_len, state_dim), lambda j: (j, c_block)),
            pl.BlockSpec((1, tile_len, heads_here), per_tile),
            pl.BlockSpec((1, heads_here, tile_len), per_tile),
            pl.BlockSpec((1, heads_here, tile_len), per_tile),
            pl.BlockSpec((1, tile_len, 1), per_tile),
            pl.BlockSpec((1, 1, tile_len), per_tile),
            pl.BlockSpec((1, state_dim, inner_here), per_tile),
            pl.BlockSpec((1, 1, inner_here), per_tile),
            pl.BlockSpec((state_dim, inner_here), lambda j: (0, 0)),
            pl.BlockSpec((tile_len, inner_here), lambda j: (j, 0)),
            pl.BlockSpec((1, inner_here), lambda j: (0, 0)),
        ],
        out_specs=[
            pl.BlockSpec((tile_len, inner_here), lambda j: (j, 0)),
            pl.BlockSpec((tile_len, 1), lambda j: (j, 0)),
        ],
        out_shape=[
            jax.ShapeDtypeStruct((rows, inner_here), jnp.float32),
            jax.ShapeDtypeStruct((rows, 1), jnp.float32),
        ],
        cost_estimate=pl.CostEstimate(
            flops=tiles_dev * (2 * tile_len * tile_len * (state_dim + 4 * inner_here + 2 * inner_here)),
            transcendentals=tiles_dev * tile_len * (tile_len * heads_here + 2 * inner_here),
            bytes_accessed=rows * inner_here * 10 + tiles_dev * inner_here * state_dim * 4,
        ),
    )(
        conv_out, conv_out, conv_out, cumul, cumul_t, dt_t, part_col, part_row,
        before_tile, prefix_wide, entering, zx, d_full,
    )


def shards(
    ingest,
    dest_tile,
    doc_start,
    w_zx,
    w_bc,
    w_dt,
    dt_bias,
    a_log,
    conv_x,
    conv_bc,
    cbias_x,
    cbias_bc,
    d_skip,
    norm_gain,
):
    seq_count = lax.axis_size("seq")
    tiles_dev = ingest.shape[0]
    tile_len = ingest.shape[1]
    columns = ingest.shape[2]
    row_count = tiles_dev * tile_len
    heads_here = a_log.shape[0]
    inner_here = conv_x.shape[1]
    head_dim = inner_here // heads_here
    state_dim = conv_bc.shape[1] // 2
    taps = conv_x.shape[0]
    keep_rows = taps - 1
    owner = dest_tile // tiles_dev
    slots = jnp.arange(seq_count, dtype=jnp.int32)
    pick = (owner[None, :] == slots[:, None]).astype(jnp.float32)
    outgoing = jnp.einsum(
        "sj,jrc->src", pick.astype(jnp.bfloat16), ingest, preferred_element_type=jnp.float32
    ).astype(jnp.bfloat16)
    incoming = lax.all_to_all(outgoing, "seq", split_axis=0, concat_axis=0, tiled=True)
    zx_cols, gather_dest = lax.optimization_barrier((w_zx.reshape(w_zx.shape[0], -1), dest_tile))
    every_dest = lax.all_gather(gather_dest, "seq", tiled=True).reshape(seq_count, tiles_dev)
    mine = every_dest // tiles_dev == lax.axis_index("seq")
    got_slot = jnp.sum(jnp.where(mine, every_dest % tiles_dev, 0), 1)
    local_slots = jnp.arange(tiles_dev, dtype=jnp.int32)
    place = (got_slot[None, :] == local_slots[:, None]).astype(jnp.bfloat16)
    arrived = jnp.einsum("js,src->jrc", place, incoming, preferred_element_type=jnp.float32).astype(
        jnp.bfloat16
    )
    own_rows = arrived.reshape(row_count, columns)
    weight_set = (zx_cols, w_bc, w_dt)
    piece = lax.all_gather(own_rows, "head", axis=1, tiled=True)
    acc_zx, acc_bc, acc_dt = tuple(
        (jnp.dot(piece, weight, preferred_element_type=jnp.float32) for weight in weight_set)
    )
    zx = acc_zx.astype(jnp.bfloat16)
    x_in = zx[:, inner_here:]
    bc_all = acc_bc.astype(jnp.bfloat16)
    step_dt = jax.nn.softplus(acc_dt + dt_bias[None, :])
    within = jnp.arange(tile_len, dtype=jnp.int32)
    has_bound = (doc_start < tile_len).astype(jnp.float32)
    before_count = jnp.cumsum(has_bound) - has_bound
    later = (within[None, :] >= doc_start[:, None]).astype(jnp.float32)
    segment = (before_count[:, None] + later).reshape(row_count)
    conv_in = jnp.concatenate([x_in, bc_all], 1)
    tail = conv_in[row_count - keep_rows :]
    tail_seg = (segment[row_count - keep_rows :] - segment[row_count - 1]).astype(jnp.bfloat16)
    got_tail, got_seg = shifted((tail, tail_seg), "seq", 1)
    ext_seg = jnp.concatenate([got_seg.astype(jnp.float32), segment], 0)
    conv_weight = jnp.concatenate([conv_x, conv_bc], 1)
    conv_bias = jnp.concatenate([cbias_x, cbias_bc], 0)
    total = conv_bias[None, :] + conv_weight[taps - 1][None, :] * conv_in.astype(jnp.float32)
    for back_step in range(keep_rows):
        same = ext_seg[back_step : back_step + row_count] == segment
        total = total + jnp.where(
            same[:, None],
            conv_weight[back_step][None, :]
            * jnp.concatenate(
                [got_tail[back_step:], conv_in[: row_count - keep_rows + back_step]], 0
            ).astype(jnp.float32),
            0.0,
        )
    conv_out = jax.nn.silu(total).astype(jnp.bfloat16)
    rate = -jnp.exp(a_log)
    tile_dt = step_dt.reshape(tiles_dev, tile_len, heads_here)
    lower = (within[:, None] >= within[None, :]).astype(jnp.float32)
    cumul = jnp.einsum(
        "is,jsh->jih", lower, tile_dt * rate[None, None, :], precision=lax.Precision.HIGHEST
    )
    cumul_t = cumul.transpose(0, 2, 1)
    dt_t = tile_dt.transpose(0, 2, 1)
    last_part = later[:, tile_len - 1]
    tail_keep = (later == last_part[:, None]).astype(jnp.float32)
    to_end = jnp.exp(cumul[:, tile_len - 1 :, :] - cumul) * tile_dt * tail_keep[:, :, None]
    b_t = conv_out[:, inner_here : inner_here + state_dim].reshape(
        tiles_dev, tile_len, state_dim
    ).transpose(0, 2, 1)
    passing = jnp.exp(cumul[:, tile_len - 1, :]) * (1.0 - has_bound)[:, None]
    through = jnp.cumprod(passing, 0)
    prefix = jnp.concatenate([jnp.ones((1, heads_here), jnp.float32), through[:-1]], 0)
    widen = lambda per_head: jnp.repeat(per_head, head_dim, axis=-1)
    before_tile, run_state = contrib_tiles(
        conv_out, b_t, to_end, widen(passing)[:, None, :], inner_here, state_dim
    )
    position = lax.axis_index("seq")
    run_decay = widen(through[tiles_dev - 1])
    distance = 1
    def with_decay(state, decay):
        high = decay.astype(jnp.bfloat16)
        rest = decay - high.astype(jnp.float32)
        middle = rest.astype(jnp.bfloat16)
        low = (rest - middle.astype(jnp.float32)).astype(jnp.bfloat16)
        return jnp.concatenate([state.astype(jnp.bfloat16), high[None], middle[None], low[None]], 0)

    def unpack(got):
        got = got.astype(jnp.float32)
        return got[:state_dim], got[state_dim] + got[state_dim + 1] + got[state_dim + 2]

    while 2 * distance < seq_count:
        got_state, got_decay = unpack(shifted(with_decay(run_state, run_decay), "seq", distance))
        run_state = run_state + run_decay[None, :] * got_state
        run_decay = jnp.where(position >= distance, run_decay * got_decay, run_decay)
        distance *= 2
    near_state, near_decay = unpack(shifted(with_decay(run_state, run_decay), "seq", 1))
    far_state = shifted(run_state.astype(jnp.bfloat16), "seq", distance + 1).astype(jnp.float32)
    entering = near_state + near_decay[None, :] * far_state
    d_full = jnp.repeat(d_skip, head_dim)[None, :]
    gated, row_sq = mix_tiles(
        conv_out, zx, cumul, cumul_t, dt_t, later, before_tile, widen(prefix)[:, None, :],
        entering, d_full,
    )
    sums = lax.psum(row_sq, "head")
    return (gated * lax.rsqrt(sums / INNER + EPSILON) * norm_gain[None, :]).astype(jnp.bfloat16)


def solution(mesh):
    return jax.shard_map(
        shards,
        mesh=mesh,
        in_specs=(
            P("seq", None, "head"),
            P("seq"),
            P("seq"),
            P(None, None, "head"),
            P(),
            P(None, "head"),
            P("head"),
            P("head"),
            P(None, "head"),
            P(),
            P("head"),
            P(),
            P("head"),
            P("head"),
        ),
        out_specs=P("seq", "head"),
        check_vma=False,
    )
```

```python
import jax
import jax.numpy as jnp
from jax import lax
from jax.experimental import pallas as pl
from jax.experimental.pallas import tpu as pltpu
from jax.sharding import PartitionSpec as P

INNER = 2048


EPSILON = 1e-05


def shifted(x, axis, by):
    devices = lax.axis_size(axis)
    pairs = [(i, i + by) for i in range(devices) if 0 <= i + by < devices]
    return lax.ppermute(x, axis, pairs)


def mix_tile(
    x_ref, b_ref, c_ref, cum_ref, cumt_ref, dtt_ref, partc_ref, partr_ref, before_ref, prefix_ref,
    enter_ref, gate_ref, d_ref, out_ref, sq_ref,
):
    f32 = jnp.float32
    tile_len = x_ref.shape[0]
    pairs = x_ref.shape[1] // 128
    b_mat = b_ref[...]
    c_mat = c_ref[...]
    scores = lax.dot_general(
        c_mat, b_mat, (((1,), (1,)), ((), ())), preferred_element_type=f32
    )
    cum = cum_ref[0]
    cumt = cumt_ref[0]
    dtt = dtt_ref[0]
    part_col = partc_ref[0]
    part_row = partr_ref[0]
    row = lax.broadcasted_iota(jnp.int32, (tile_len, tile_len), 0)
    col = lax.broadcasted_iota(jnp.int32, (tile_len, tile_len), 1)
    keep = (row >= col) & (part_col == part_row)
    earlier = 1.0 - part_col
    first_half = lax.broadcasted_iota(jnp.int32, (tile_len, 128), 1) < 64
    total_sq = jnp.zeros((tile_len, 128), f32)
    for pair in range(pairs):
        cols = pl.ds(pair * 128, 128)
        x_pair = x_ref[:, cols]
        slabs = []
        for half in range(2):
            head = 2 * pair + half
            diff = cum[:, head : head + 1] - cumt[head : head + 1, :]
            decay = jnp.where(keep, jnp.exp(jnp.where(keep, diff, 0.0)), 0.0)
            slabs.append((scores * decay * dtt[head : head + 1, :]).astype(jnp.bfloat16))
        weights = jnp.concatenate(slabs, axis=1)
        zero = jnp.zeros_like(x_pair)
        split_x = jnp.concatenate(
            [jnp.where(first_half, x_pair, zero), jnp.where(first_half, zero, x_pair)], axis=0
        )
        intra = jnp.dot(weights, split_x, preferred_element_type=f32)
        carried = (
            before_ref[0, :, cols] + prefix_ref[0, :, cols] * enter_ref[:, cols]
        ).astype(jnp.bfloat16)
        projected = jnp.dot(c_mat, carried, preferred_element_type=f32)
        grow = jnp.where(
            first_half,
            jnp.exp(cum[:, 2 * pair : 2 * pair + 1]),
            jnp.exp(cum[:, 2 * pair + 1 : 2 * pair + 2]),
        )
        inter = grow * earlier * projected
        mixed = intra + inter + d_ref[:, cols] * x_pair.astype(f32)
        gate = gate_ref[:, cols].astype(f32)
        gated = mixed * (gate * (0.5 + 0.5 * jnp.tanh(0.5 * gate)))
        out_ref[:, cols] = gated
        total_sq = total_sq + gated * gated
    sq_ref[...] = jnp.sum(total_sq, axis=1, keepdims=True)


def contrib_tile(x_ref, bt_ref, end_ref, pass_ref, before_ref, total_ref):
    f32 = jnp.float32
    tile_len = x_ref.shape[0]
    pairs = x_ref.shape[1] // 128

    @pl.when(pl.program_id(0) == 0)
    def _():
        total_ref[...] = jnp.zeros_like(total_ref)

    b_t = bt_ref[0]
    to_end = end_ref[0]
    first_half = lax.broadcasted_iota(jnp.int32, (tile_len, 128), 1) < 64
    for pair in range(pairs):
        cols = pl.ds(pair * 128, 128)
        scale = jnp.where(
            first_half, to_end[:, 2 * pair : 2 * pair + 1], to_end[:, 2 * pair + 1 : 2 * pair + 2]
        )
        scaled = (x_ref[:, cols].astype(f32) * scale).astype(jnp.bfloat16)
        contrib = jnp.dot(b_t, scaled, preferred_element_type=f32)
        state = total_ref[:, cols]
        before_ref[0, :, cols] = state
        total_ref[:, cols] = pass_ref[0, :, cols] * state + contrib


def contrib_tiles(conv_out, b_t, to_end, passing_wide, inner_here, state_dim):
    tiles_dev, tile_len, heads_here = to_end.shape
    return pl.pallas_call(
        contrib_tile,
        grid=(tiles_dev,),
        in_specs=[
            pl.BlockSpec((tile_len, inner_here), lambda j: (j, 0)),
            pl.BlockSpec((1, state_dim, tile_len), lambda j: (j, 0, 0)),
            pl.BlockSpec((1, tile_len, heads_here), lambda j: (j, 0, 0)),
            pl.BlockSpec((1, 1, inner_here), lambda j: (j, 0, 0)),
        ],
        out_specs=[
            pl.BlockSpec((1, state_dim, inner_here), lambda j: (j, 0, 0)),
            pl.BlockSpec((state_dim, inner_here), lambda j: (0, 0)),
        ],
        out_shape=[
            jax.ShapeDtypeStruct((tiles_dev, state_dim, inner_here), jnp.float32),
            jax.ShapeDtypeStruct((state_dim, inner_here), jnp.float32),
        ],
        compiler_params=pltpu.CompilerParams(dimension_semantics=("arbitrary",)),
        cost_estimate=pl.CostEstimate(
            flops=tiles_dev * 2 * tile_len * inner_here * state_dim,
            transcendentals=0,
            bytes_accessed=tiles_dev * (tile_len * (inner_here + state_dim) * 2 + inner_here * state_dim * 4),
        ),
    )(conv_out, b_t, to_end, passing_wide)


def mix_tiles(conv_out, zx, cumul, cumul_t, dt_t, later, before_tile, prefix_wide, entering, d_full):
    tiles_dev, tile_len, heads_here = cumul.shape
    inner_here = before_tile.shape[2]
    state_dim = before_tile.shape[1]
    rows = tiles_dev * tile_len
    b_block = inner_here // 128
    c_block = b_block + state_dim // 128
    part_col = later.reshape(tiles_dev, tile_len, 1)
    part_row = later.reshape(tiles_dev, 1, tile_len)
    per_tile = lambda j: (j, 0, 0)
    return pl.pallas_call(
        mix_tile,
        grid=(tiles_dev,),
        in_specs=[
            pl.BlockSpec((tile_len, inner_here), lambda j: (j, 0)),
            pl.BlockSpec((tile_len, state_dim), lambda j: (j, b_block)),
            pl.BlockSpec((tile_len, state_dim), lambda j: (j, c_block)),
            pl.BlockSpec((1, tile_len, heads_here), per_tile),
            pl.BlockSpec((1, heads_here, tile_len), per_tile),
            pl.BlockSpec((1, heads_here, tile_len), per_tile),
            pl.BlockSpec((1, tile_len, 1), per_tile),
            pl.BlockSpec((1, 1, tile_len), per_tile),
            pl.BlockSpec((1, state_dim, inner_here), per_tile),
            pl.BlockSpec((1, 1, inner_here), per_tile),
            pl.BlockSpec((state_dim, inner_here), lambda j: (0, 0)),
            pl.BlockSpec((tile_len, inner_here), lambda j: (j, 0)),
            pl.BlockSpec((1, inner_here), lambda j: (0, 0)),
        ],
        out_specs=[
            pl.BlockSpec((tile_len, inner_here), lambda j: (j, 0)),
            pl.BlockSpec((tile_len, 1), lambda j: (j, 0)),
        ],
        out_shape=[
            jax.ShapeDtypeStruct((rows, inner_here), jnp.float32),
            jax.ShapeDtypeStruct((rows, 1), jnp.float32),
        ],
        cost_estimate=pl.CostEstimate(
            flops=tiles_dev * (2 * tile_len * tile_len * (state_dim + 4 * inner_here + 2 * inner_here)),
            transcendentals=tiles_dev * tile_len * (tile_len * heads_here + 2 * inner_here),
            bytes_accessed=rows * inner_here * 10 + tiles_dev * inner_here * state_dim * 4,
        ),
    )(
        conv_out, conv_out, conv_out, cumul, cumul_t, dt_t, part_col, part_row,
        before_tile, prefix_wide, entering, zx, d_full,
    )


def shards(
    ingest,
    dest_tile,
    doc_start,
    w_zx,
    w_bc,
    w_dt,
    dt_bias,
    a_log,
    conv_x,
    conv_bc,
    cbias_x,
    cbias_bc,
    d_skip,
    norm_gain,
):
    seq_count = lax.axis_size("seq")
    tiles_dev = ingest.shape[0]
    tile_len = ingest.shape[1]
    columns = ingest.shape[2]
    row_count = tiles_dev * tile_len
    heads_here = a_log.shape[0]
    inner_here = conv_x.shape[1]
    head_dim = inner_here // heads_here
    state_dim = conv_bc.shape[1] // 2
    taps = conv_x.shape[0]
    keep_rows = taps - 1
    owner = dest_tile // tiles_dev
    slots = jnp.arange(seq_count, dtype=jnp.int32)
    pick = (owner[None, :] == slots[:, None]).astype(jnp.float32)
    outgoing = jnp.einsum(
        "sj,jrc->src", pick.astype(jnp.bfloat16), ingest, preferred_element_type=jnp.float32
    ).astype(jnp.bfloat16)
    incoming = lax.all_to_all(outgoing, "seq", split_axis=0, concat_axis=0, tiled=True)
    zx_cols, gather_dest = lax.optimization_barrier((w_zx.reshape(w_zx.shape[0], -1), dest_tile))
    every_dest = lax.all_gather(gather_dest, "seq", tiled=True).reshape(seq_count, tiles_dev)
    mine = every_dest // tiles_dev == lax.axis_index("seq")
    got_slot = jnp.sum(jnp.where(mine, every_dest % tiles_dev, 0), 1)
    local_slots = jnp.arange(tiles_dev, dtype=jnp.int32)
    place = (got_slot[None, :] == local_slots[:, None]).astype(jnp.bfloat16)
    arrived = jnp.einsum("js,src->jrc", place, incoming, preferred_element_type=jnp.float32).astype(
        jnp.bfloat16
    )
    own_rows = arrived.reshape(row_count, columns)
    weight_set = (zx_cols, w_bc, w_dt)
    piece = lax.all_gather(own_rows, "head", axis=1, tiled=True)
    acc_zx, acc_bc, acc_dt = tuple(
        (jnp.dot(piece, weight, preferred_element_type=jnp.float32) for weight in weight_set)
    )
    zx = acc_zx.astype(jnp.bfloat16)
    x_in = zx[:, inner_here:]
    bc_all = acc_bc.astype(jnp.bfloat16)
    step_dt = jax.nn.softplus(acc_dt + dt_bias[None, :])
    within = jnp.arange(tile_len, dtype=jnp.int32)
    has_bound = (doc_start < tile_len).astype(jnp.float32)
    before_count = jnp.cumsum(has_bound) - has_bound
    later = (within[None, :] >= doc_start[:, None]).astype(jnp.float32)
    segment = (before_count[:, None] + later).reshape(row_count)
    conv_in = jnp.concatenate([x_in, bc_all], 1)
    tail = conv_in[row_count - keep_rows :]
    tail_seg = (segment[row_count - keep_rows :] - segment[row_count - 1]).astype(jnp.bfloat16)
    got_tail, got_seg = shifted((tail, tail_seg), "seq", 1)
    extended = jnp.concatenate([got_tail, conv_in], 0)
    ext_seg = jnp.concatenate([got_seg.astype(jnp.float32), segment], 0)
    conv_weight = jnp.concatenate([conv_x, conv_bc], 1)
    conv_bias = jnp.concatenate([cbias_x, cbias_bc], 0)
    total = conv_bias[None, :] + conv_weight[taps - 1][None, :] * conv_in.astype(jnp.float32)
    for back_step in range(keep_rows):
        same = ext_seg[back_step : back_step + row_count] == segment
        total = total + jnp.where(
            same[:, None],
            conv_weight[back_step][None, :]
            * extended[back_step : back_step + row_count].astype(jnp.float32),
            0.0,
        )
    conv_out = jax.nn.silu(total).astype(jnp.bfloat16)
    rate = -jnp.exp(a_log)
    tile_dt = step_dt.reshape(tiles_dev, tile_len, heads_here)
    lower = (within[:, None] >= within[None, :]).astype(jnp.float32)
    cumul = jnp.einsum(
        "is,jsh->jih", lower, tile_dt * rate[None, None, :], precision=lax.Precision.HIGHEST
    )
    cumul_t = cumul.transpose(0, 2, 1)
    dt_t = tile_dt.transpose(0, 2, 1)
    last_part = later[:, tile_len - 1]
    tail_keep = (later == last_part[:, None]).astype(jnp.float32)
    to_end = jnp.exp(cumul[:, tile_len - 1 :, :] - cumul) * tile_dt * tail_keep[:, :, None]
    b_t = conv_out[:, inner_here : inner_here + state_dim].reshape(
        tiles_dev, tile_len, state_dim
    ).transpose(0, 2, 1)
    passing = jnp.exp(cumul[:, tile_len - 1, :]) * (1.0 - has_bound)[:, None]
    through = jnp.cumprod(passing, 0)
    prefix = jnp.concatenate([jnp.ones((1, heads_here), jnp.float32), through[:-1]], 0)
    widen = lambda per_head: jnp.repeat(per_head, head_dim, axis=-1)
    before_tile, run_state = contrib_tiles(
        conv_out, b_t, to_end, widen(passing)[:, None, :], inner_here, state_dim
    )
    position = lax.axis_index("seq")
    run_decay = widen(through[tiles_dev - 1])
    distance = 1
    def with_decay(state, decay):
        high = decay.astype(jnp.bfloat16)
        rest = decay - high.astype(jnp.float32)
        middle = rest.astype(jnp.bfloat16)
        low = (rest - middle.astype(jnp.float32)).astype(jnp.bfloat16)
        return jnp.concatenate([state.astype(jnp.bfloat16), high[None], middle[None], low[None]], 0)

    def unpack(got):
        got = got.astype(jnp.float32)
        return got[:state_dim], got[state_dim] + got[state_dim + 1] + got[state_dim + 2]

    while 2 * distance < seq_count:
        got_state, got_decay = unpack(shifted(with_decay(run_state, run_decay), "seq", distance))
        run_state = run_state + run_decay[None, :] * got_state
        run_decay = jnp.where(position >= distance, run_decay * got_decay, run_decay)
        distance *= 2
    near_state, near_decay = unpack(shifted(with_decay(run_state, run_decay), "seq", 1))
    far_state = shifted(run_state.astype(jnp.bfloat16), "seq", distance + 1).astype(jnp.float32)
    entering = near_state + near_decay[None, :] * far_state
    d_full = jnp.repeat(d_skip, head_dim)[None, :]
    gated, row_sq = mix_tiles(
        conv_out, zx, cumul, cumul_t, dt_t, later, before_tile, widen(prefix)[:, None, :],
        entering, d_full,
    )
    sums = lax.psum(row_sq.reshape(tiles_dev, tile_len), "head").reshape(row_count, 1)
    return (gated * lax.rsqrt(sums / INNER + EPSILON) * norm_gain[None, :]).astype(jnp.bfloat16)


def solution(mesh):
    return jax.shard_map(
        shards,
        mesh=mesh,
        in_specs=(
            P("seq", None, "head"),
            P("seq"),
            P("seq"),
            P(None, None, "head"),
            P(),
            P(None, "head"),
            P("head"),
            P("head"),
            P(None, "head"),
            P(),
            P("head"),
            P(),
            P("head"),
            P("head"),
        ),
        out_specs=P("seq", "head"),
        check_vma=False,
    )
```

```python
import jax
import jax.numpy as jnp
from jax import lax
from jax.experimental import pallas as pl
from jax.experimental.pallas import tpu as pltpu
from jax.sharding import PartitionSpec as P

INNER = 2048


EPSILON = 1e-05


def shifted(x, axis, by):
    devices = lax.axis_size(axis)
    pairs = [(i, i + by) for i in range(devices) if 0 <= i + by < devices]
    return lax.ppermute(x, axis, pairs)


def mix_tile(
    x_ref, b_ref, c_ref, cum_ref, cumt_ref, dtt_ref, partc_ref, partr_ref, before_ref, prefix_ref,
    enter_ref, gate_ref, d_ref, out_ref, sq_ref,
):
    f32 = jnp.float32
    tile_len = x_ref.shape[0]
    pairs = x_ref.shape[1] // 128
    b_mat = b_ref[...]
    c_mat = c_ref[...]
    scores = lax.dot_general(
        c_mat, b_mat, (((1,), (1,)), ((), ())), preferred_element_type=f32
    )
    cum = cum_ref[0]
    cumt = cumt_ref[0]
    dtt = dtt_ref[0]
    part_col = partc_ref[0]
    part_row = partr_ref[0]
    row = lax.broadcasted_iota(jnp.int32, (tile_len, tile_len), 0)
    col = lax.broadcasted_iota(jnp.int32, (tile_len, tile_len), 1)
    keep = (row >= col) & (part_col == part_row)
    earlier = 1.0 - part_col
    first_half = lax.broadcasted_iota(jnp.int32, (tile_len, 128), 1) < 64
    total_sq = jnp.zeros((tile_len, 128), f32)
    for pair in range(pairs):
        cols = pl.ds(pair * 128, 128)
        x_pair = x_ref[:, cols]
        slabs = []
        for half in range(2):
            head = 2 * pair + half
            diff = cum[:, head : head + 1] - cumt[head : head + 1, :]
            decay = jnp.where(keep, jnp.exp(jnp.where(keep, diff, 0.0)), 0.0)
            slabs.append((scores * decay * dtt[head : head + 1, :]).astype(jnp.bfloat16))
        weights = jnp.concatenate(slabs, axis=1)
        zero = jnp.zeros_like(x_pair)
        split_x = jnp.concatenate(
            [jnp.where(first_half, x_pair, zero), jnp.where(first_half, zero, x_pair)], axis=0
        )
        intra = jnp.dot(weights, split_x, preferred_element_type=f32)
        carried = (
            before_ref[0, :, cols] + prefix_ref[0, :, cols] * enter_ref[:, cols]
        ).astype(jnp.bfloat16)
        projected = jnp.dot(c_mat, carried, preferred_element_type=f32)
        grow = jnp.where(
            first_half,
            jnp.exp(cum[:, 2 * pair : 2 * pair + 1]),
            jnp.exp(cum[:, 2 * pair + 1 : 2 * pair + 2]),
        )
        inter = grow * earlier * projected
        mixed = intra + inter + d_ref[:, cols] * x_pair.astype(f32)
        gate = gate_ref[:, cols].astype(f32)
        gated = mixed * (gate * (0.5 + 0.5 * jnp.tanh(0.5 * gate)))
        out_ref[:, cols] = gated
        total_sq = total_sq + gated * gated
    sq_ref[...] = jnp.sum(total_sq, axis=1, keepdims=True)


def contrib_tile(x_ref, bt_ref, end_ref, pass_ref, before_ref, total_ref):
    f32 = jnp.float32
    tile_len = x_ref.shape[0]
    pairs = x_ref.shape[1] // 128

    @pl.when(pl.program_id(0) == 0)
    def _():
        total_ref[...] = jnp.zeros_like(total_ref)

    b_t = bt_ref[0]
    to_end = end_ref[0]
    first_half = lax.broadcasted_iota(jnp.int32, (tile_len, 128), 1) < 64
    for pair in range(pairs):
        cols = pl.ds(pair * 128, 128)
        scale = jnp.where(
            first_half, to_end[:, 2 * pair : 2 * pair + 1], to_end[:, 2 * pair + 1 : 2 * pair + 2]
        )
        scaled = (x_ref[:, cols].astype(f32) * scale).astype(jnp.bfloat16)
        contrib = jnp.dot(b_t, scaled, preferred_element_type=f32)
        state = total_ref[:, cols]
        before_ref[0, :, cols] = state
        total_ref[:, cols] = pass_ref[0, :, cols] * state + contrib


def contrib_tiles(conv_out, b_t, to_end, passing_wide, inner_here, state_dim):
    tiles_dev, tile_len, heads_here = to_end.shape
    return pl.pallas_call(
        contrib_tile,
        grid=(tiles_dev,),
        in_specs=[
            pl.BlockSpec((tile_len, inner_here), lambda j: (j, 0)),
            pl.BlockSpec((1, state_dim, tile_len), lambda j: (j, 0, 0)),
            pl.BlockSpec((1, tile_len, heads_here), lambda j: (j, 0, 0)),
            pl.BlockSpec((1, 1, inner_here), lambda j: (j, 0, 0)),
        ],
        out_specs=[
            pl.BlockSpec((1, state_dim, inner_here), lambda j: (j, 0, 0)),
            pl.BlockSpec((state_dim, inner_here), lambda j: (0, 0)),
        ],
        out_shape=[
            jax.ShapeDtypeStruct((tiles_dev, state_dim, inner_here), jnp.float32),
            jax.ShapeDtypeStruct((state_dim, inner_here), jnp.float32),
        ],
        compiler_params=pltpu.CompilerParams(dimension_semantics=("arbitrary",)),
        cost_estimate=pl.CostEstimate(
            flops=tiles_dev * 2 * tile_len * inner_here * state_dim,
            transcendentals=0,
            bytes_accessed=tiles_dev * (tile_len * (inner_here + state_dim) * 2 + inner_here * state_dim * 4),
        ),
    )(conv_out, b_t, to_end, passing_wide)


def mix_tiles(conv_out, zx, cumul, cumul_t, dt_t, later, before_tile, prefix_wide, entering, d_full):
    tiles_dev, tile_len, heads_here = cumul.shape
    inner_here = before_tile.shape[2]
    state_dim = before_tile.shape[1]
    rows = tiles_dev * tile_len
    b_block = inner_here // 128
    c_block = b_block + state_dim // 128
    part_col = later.reshape(tiles_dev, tile_len, 1)
    part_row = later.reshape(tiles_dev, 1, tile_len)
    per_tile = lambda j: (j, 0, 0)
    return pl.pallas_call(
        mix_tile,
        grid=(tiles_dev,),
        in_specs=[
            pl.BlockSpec((tile_len, inner_here), lambda j: (j, 0)),
            pl.BlockSpec((tile_len, state_dim), lambda j: (j, b_block)),
            pl.BlockSpec((tile_len, state_dim), lambda j: (j, c_block)),
            pl.BlockSpec((1, tile_len, heads_here), per_tile),
            pl.BlockSpec((1, heads_here, tile_len), per_tile),
            pl.BlockSpec((1, heads_here, tile_len), per_tile),
            pl.BlockSpec((1, tile_len, 1), per_tile),
            pl.BlockSpec((1, 1, tile_len), per_tile),
            pl.BlockSpec((1, state_dim, inner_here), per_tile),
            pl.BlockSpec((1, 1, inner_here), per_tile),
            pl.BlockSpec((state_dim, inner_here), lambda j: (0, 0)),
            pl.BlockSpec((tile_len, inner_here), lambda j: (j, 0)),
            pl.BlockSpec((1, inner_here), lambda j: (0, 0)),
        ],
        out_specs=[
            pl.BlockSpec((tile_len, inner_here), lambda j: (j, 0)),
            pl.BlockSpec((tile_len, 1), lambda j: (j, 0)),
        ],
        out_shape=[
            jax.ShapeDtypeStruct((rows, inner_here), jnp.float32),
            jax.ShapeDtypeStruct((rows, 1), jnp.float32),
        ],
        cost_estimate=pl.CostEstimate(
            flops=tiles_dev * (2 * tile_len * tile_len * (state_dim + 4 * inner_here + 2 * inner_here)),
            transcendentals=tiles_dev * tile_len * (tile_len * heads_here + 2 * inner_here),
            bytes_accessed=rows * inner_here * 10 + tiles_dev * inner_here * state_dim * 4,
        ),
    )(
        conv_out, conv_out, conv_out, cumul, cumul_t, dt_t, part_col, part_row,
        before_tile, prefix_wide, entering, zx, d_full,
    )


def shards(
    ingest,
    dest_tile,
    doc_start,
    w_zx,
    w_bc,
    w_dt,
    dt_bias,
    a_log,
    conv_x,
    conv_bc,
    cbias_x,
    cbias_bc,
    d_skip,
    norm_gain,
):
    seq_count = lax.axis_size("seq")
    tiles_dev = ingest.shape[0]
    tile_len = ingest.shape[1]
    columns = ingest.shape[2]
    row_count = tiles_dev * tile_len
    heads_here = a_log.shape[0]
    inner_here = conv_x.shape[1]
    head_dim = inner_here // heads_here
    state_dim = conv_bc.shape[1] // 2
    taps = conv_x.shape[0]
    keep_rows = taps - 1
    owner = dest_tile // tiles_dev
    slots = jnp.arange(seq_count, dtype=jnp.int32)
    pick = (owner[None, :] == slots[:, None]).astype(jnp.float32)
    outgoing = jnp.einsum(
        "sj,jrc->src", pick.astype(jnp.bfloat16), ingest, preferred_element_type=jnp.float32
    ).astype(jnp.bfloat16)
    incoming = lax.all_to_all(outgoing, "seq", split_axis=0, concat_axis=0, tiled=True)
    zx_cols, gather_dest = lax.optimization_barrier((w_zx.reshape(w_zx.shape[0], -1), dest_tile))
    every_dest = lax.all_gather(gather_dest, "seq", tiled=True).reshape(seq_count, tiles_dev)
    mine = every_dest // tiles_dev == lax.axis_index("seq")
    got_slot = jnp.sum(jnp.where(mine, every_dest % tiles_dev, 0), 1)
    local_slots = jnp.arange(tiles_dev, dtype=jnp.int32)
    place = (got_slot[None, :] == local_slots[:, None]).astype(jnp.bfloat16)
    arrived = jnp.einsum("js,src->jrc", place, incoming, preferred_element_type=jnp.float32).astype(
        jnp.bfloat16
    )
    own_rows = arrived.reshape(row_count, columns)
    weight_set = (zx_cols, w_bc, w_dt)
    piece = lax.all_gather(own_rows, "head", axis=1, tiled=True)
    acc_zx, acc_bc, acc_dt = tuple(
        (jnp.dot(piece, weight, preferred_element_type=jnp.float32) for weight in weight_set)
    )
    zx = acc_zx.astype(jnp.bfloat16)
    x_in = zx[:, inner_here:]
    bc_all = acc_bc.astype(jnp.bfloat16)
    step_dt = jax.nn.softplus(acc_dt + dt_bias[None, :])
    within = jnp.arange(tile_len, dtype=jnp.int32)
    has_bound = (doc_start < tile_len).astype(jnp.float32)
    before_count = jnp.cumsum(has_bound) - has_bound
    later = (within[None, :] >= doc_start[:, None]).astype(jnp.float32)
    segment = (before_count[:, None] + later).reshape(row_count)
    conv_in = jnp.concatenate([x_in, bc_all], 1)
    tail = conv_in[row_count - keep_rows :]
    tail_seg = (segment[row_count - keep_rows :] - segment[row_count - 1]).astype(jnp.bfloat16)
    got_both = shifted(jnp.concatenate([tail, tail_seg[:, None]], 1), "seq", 1)
    got_tail, got_seg = got_both[:, : tail.shape[1]], got_both[:, tail.shape[1]]
    extended = jnp.concatenate([got_tail, conv_in], 0)
    ext_seg = jnp.concatenate([got_seg.astype(jnp.float32), segment], 0)
    conv_weight = jnp.concatenate([conv_x, conv_bc], 1)
    conv_bias = jnp.concatenate([cbias_x, cbias_bc], 0)
    total = conv_bias[None, :] + conv_weight[taps - 1][None, :] * conv_in.astype(jnp.float32)
    for back_step in range(keep_rows):
        same = ext_seg[back_step : back_step + row_count] == segment
        total = total + jnp.where(
            same[:, None],
            conv_weight[back_step][None, :]
            * extended[back_step : back_step + row_count].astype(jnp.float32),
            0.0,
        )
    conv_out = jax.nn.silu(total).astype(jnp.bfloat16)
    rate = -jnp.exp(a_log)
    tile_dt = step_dt.reshape(tiles_dev, tile_len, heads_here)
    lower = (within[:, None] >= within[None, :]).astype(jnp.float32)
    cumul = jnp.einsum(
        "is,jsh->jih", lower, tile_dt * rate[None, None, :], precision=lax.Precision.HIGHEST
    )
    cumul_t = cumul.transpose(0, 2, 1)
    dt_t = tile_dt.transpose(0, 2, 1)
    last_part = later[:, tile_len - 1]
    tail_keep = (later == last_part[:, None]).astype(jnp.float32)
    to_end = jnp.exp(cumul[:, tile_len - 1 :, :] - cumul) * tile_dt * tail_keep[:, :, None]
    b_t = conv_out[:, inner_here : inner_here + state_dim].reshape(
        tiles_dev, tile_len, state_dim
    ).transpose(0, 2, 1)
    passing = jnp.exp(cumul[:, tile_len - 1, :]) * (1.0 - has_bound)[:, None]
    through = jnp.cumprod(passing, 0)
    prefix = jnp.concatenate([jnp.ones((1, heads_here), jnp.float32), through[:-1]], 0)
    widen = lambda per_head: jnp.repeat(per_head, head_dim, axis=-1)
    before_tile, run_state = contrib_tiles(
        conv_out, b_t, to_end, widen(passing)[:, None, :], inner_here, state_dim
    )
    position = lax.axis_index("seq")
    run_decay = widen(through[tiles_dev - 1])
    distance = 1
    def with_decay(state, decay):
        high = decay.astype(jnp.bfloat16)
        rest = decay - high.astype(jnp.float32)
        middle = rest.astype(jnp.bfloat16)
        low = (rest - middle.astype(jnp.float32)).astype(jnp.bfloat16)
        return jnp.concatenate([state.astype(jnp.bfloat16), high[None], middle[None], low[None]], 0)

    def unpack(got):
        got = got.astype(jnp.float32)
        return got[:state_dim], got[state_dim] + got[state_dim + 1] + got[state_dim + 2]

    while 2 * distance < seq_count:
        got_state, got_decay = unpack(shifted(with_decay(run_state, run_decay), "seq", distance))
        run_state = run_state + run_decay[None, :] * got_state
        run_decay = jnp.where(position >= distance, run_decay * got_decay, run_decay)
        distance *= 2
    near_state, near_decay = unpack(shifted(with_decay(run_state, run_decay), "seq", 1))
    far_state = shifted(run_state.astype(jnp.bfloat16), "seq", distance + 1).astype(jnp.float32)
    entering = near_state + near_decay[None, :] * far_state
    d_full = jnp.repeat(d_skip, head_dim)[None, :]
    gated, row_sq = mix_tiles(
        conv_out, zx, cumul, cumul_t, dt_t, later, before_tile, widen(prefix)[:, None, :],
        entering, d_full,
    )
    sums = lax.psum(row_sq.reshape(tiles_dev, tile_len), "head").reshape(row_count, 1)
    return (gated * lax.rsqrt(sums / INNER + EPSILON) * norm_gain[None, :]).astype(jnp.bfloat16)


def solution(mesh):
    return jax.shard_map(
        shards,
        mesh=mesh,
        in_specs=(
            P("seq", None, "head"),
            P("seq"),
            P("seq"),
            P(None, None, "head"),
            P(),
            P(None, "head"),
            P("head"),
            P("head"),
            P(None, "head"),
            P(),
            P("head"),
            P(),
            P("head"),
            P("head"),
        ),
        out_specs=P("seq", "head"),
        check_vma=False,
    )
```

```python
import jax
import jax.numpy as jnp
from jax import lax
from jax.experimental import pallas as pl
from jax.experimental.pallas import tpu as pltpu
from jax.sharding import PartitionSpec as P

INNER = 2048


EPSILON = 1e-05


def shifted(x, axis, by):
    devices = lax.axis_size(axis)
    pairs = [(i, i + by) for i in range(devices) if 0 <= i + by < devices]
    return lax.ppermute(x, axis, pairs)


def mix_tile(
    x_ref, b_ref, c_ref, cum_ref, cumt_ref, dtt_ref, partc_ref, partr_ref, before_ref, prefix_ref,
    enter_ref, gate_ref, d_ref, out_ref, sq_ref,
):
    f32 = jnp.float32
    tile_len = x_ref.shape[0]
    pairs = x_ref.shape[1] // 128
    b_mat = b_ref[...]
    c_mat = c_ref[...]
    scores = lax.dot_general(
        c_mat, b_mat, (((1,), (1,)), ((), ())), preferred_element_type=f32
    )
    cum = cum_ref[0]
    cumt = cumt_ref[0]
    dtt = dtt_ref[0]
    part_col = partc_ref[0]
    part_row = partr_ref[0]
    row = lax.broadcasted_iota(jnp.int32, (tile_len, tile_len), 0)
    col = lax.broadcasted_iota(jnp.int32, (tile_len, tile_len), 1)
    keep = (row >= col) & (part_col == part_row)
    earlier = 1.0 - part_col
    first_half = lax.broadcasted_iota(jnp.int32, (tile_len, 128), 1) < 64
    total_sq = jnp.zeros((tile_len, 128), f32)
    for pair in range(pairs):
        cols = pl.ds(pair * 128, 128)
        x_pair = x_ref[:, cols]
        slabs = []
        for half in range(2):
            head = 2 * pair + half
            diff = cum[:, head : head + 1] - cumt[head : head + 1, :]
            decay = jnp.where(keep, jnp.exp(jnp.where(keep, diff, 0.0)), 0.0)
            slabs.append((scores * decay * dtt[head : head + 1, :]).astype(jnp.bfloat16))
        weights = jnp.concatenate(slabs, axis=1)
        zero = jnp.zeros_like(x_pair)
        split_x = jnp.concatenate(
            [jnp.where(first_half, x_pair, zero), jnp.where(first_half, zero, x_pair)], axis=0
        )
        intra = jnp.dot(weights, split_x, preferred_element_type=f32)
        carried = (
            before_ref[0, :, cols] + prefix_ref[0, :, cols] * enter_ref[:, cols]
        ).astype(jnp.bfloat16)
        projected = jnp.dot(c_mat, carried, preferred_element_type=f32)
        grow = jnp.where(
            first_half,
            jnp.exp(cum[:, 2 * pair : 2 * pair + 1]),
            jnp.exp(cum[:, 2 * pair + 1 : 2 * pair + 2]),
        )
        inter = grow * earlier * projected
        mixed = intra + inter + d_ref[:, cols] * x_pair.astype(f32)
        gate = gate_ref[:, cols].astype(f32)
        gated = mixed * (gate * (0.5 + 0.5 * jnp.tanh(0.5 * gate)))
        out_ref[:, cols] = gated
        total_sq = total_sq + gated * gated
    sq_ref[...] = jnp.sum(total_sq, axis=1, keepdims=True)


def contrib_tile(x_ref, bt_ref, end_ref, pass_ref, before_ref, total_ref):
    f32 = jnp.float32
    tile_len = x_ref.shape[0]
    pairs = x_ref.shape[1] // 128

    @pl.when(pl.program_id(0) == 0)
    def _():
        total_ref[...] = jnp.zeros_like(total_ref)

    b_t = bt_ref[0]
    to_end = end_ref[0]
    first_half = lax.broadcasted_iota(jnp.int32, (tile_len, 128), 1) < 64
    for pair in range(pairs):
        cols = pl.ds(pair * 128, 128)
        scale = jnp.where(
            first_half, to_end[:, 2 * pair : 2 * pair + 1], to_end[:, 2 * pair + 1 : 2 * pair + 2]
        )
        scaled = (x_ref[:, cols].astype(f32) * scale).astype(jnp.bfloat16)
        contrib = jnp.dot(b_t, scaled, preferred_element_type=f32)
        state = total_ref[:, cols]
        before_ref[0, :, cols] = state
        total_ref[:, cols] = pass_ref[0, :, cols] * state + contrib


def contrib_tiles(conv_out, b_t, to_end, passing_wide, inner_here, state_dim):
    tiles_dev, tile_len, heads_here = to_end.shape
    return pl.pallas_call(
        contrib_tile,
        grid=(tiles_dev,),
        in_specs=[
            pl.BlockSpec((tile_len, inner_here), lambda j: (j, 0)),
            pl.BlockSpec((1, state_dim, tile_len), lambda j: (j, 0, 0)),
            pl.BlockSpec((1, tile_len, heads_here), lambda j: (j, 0, 0)),
            pl.BlockSpec((1, 1, inner_here), lambda j: (j, 0, 0)),
        ],
        out_specs=[
            pl.BlockSpec((1, state_dim, inner_here), lambda j: (j, 0, 0)),
            pl.BlockSpec((state_dim, inner_here), lambda j: (0, 0)),
        ],
        out_shape=[
            jax.ShapeDtypeStruct((tiles_dev, state_dim, inner_here), jnp.float32),
            jax.ShapeDtypeStruct((state_dim, inner_here), jnp.float32),
        ],
        compiler_params=pltpu.CompilerParams(dimension_semantics=("arbitrary",)),
        cost_estimate=pl.CostEstimate(
            flops=tiles_dev * 2 * tile_len * inner_here * state_dim,
            transcendentals=0,
            bytes_accessed=tiles_dev * (tile_len * (inner_here + state_dim) * 2 + inner_here * state_dim * 4),
        ),
    )(conv_out, b_t, to_end, passing_wide)


def mix_tiles(conv_out, zx, cumul, cumul_t, dt_t, later, before_tile, prefix_wide, entering, d_full):
    tiles_dev, tile_len, heads_here = cumul.shape
    inner_here = before_tile.shape[2]
    state_dim = before_tile.shape[1]
    rows = tiles_dev * tile_len
    b_block = inner_here // 128
    c_block = b_block + state_dim // 128
    part_col = later.reshape(tiles_dev, tile_len, 1)
    part_row = later.reshape(tiles_dev, 1, tile_len)
    per_tile = lambda j: (j, 0, 0)
    return pl.pallas_call(
        mix_tile,
        grid=(tiles_dev,),
        in_specs=[
            pl.BlockSpec((tile_len, inner_here), lambda j: (j, 0)),
            pl.BlockSpec((tile_len, state_dim), lambda j: (j, b_block)),
            pl.BlockSpec((tile_len, state_dim), lambda j: (j, c_block)),
            pl.BlockSpec((1, tile_len, heads_here), per_tile),
            pl.BlockSpec((1, heads_here, tile_len), per_tile),
            pl.BlockSpec((1, heads_here, tile_len), per_tile),
            pl.BlockSpec((1, tile_len, 1), per_tile),
            pl.BlockSpec((1, 1, tile_len), per_tile),
            pl.BlockSpec((1, state_dim, inner_here), per_tile),
            pl.BlockSpec((1, 1, inner_here), per_tile),
            pl.BlockSpec((state_dim, inner_here), lambda j: (0, 0)),
            pl.BlockSpec((tile_len, inner_here), lambda j: (j, 0)),
            pl.BlockSpec((1, inner_here), lambda j: (0, 0)),
        ],
        out_specs=[
            pl.BlockSpec((tile_len, inner_here), lambda j: (j, 0)),
            pl.BlockSpec((tile_len, 1), lambda j: (j, 0)),
        ],
        out_shape=[
            jax.ShapeDtypeStruct((rows, inner_here), jnp.float32),
            jax.ShapeDtypeStruct((rows, 1), jnp.float32),
        ],
        cost_estimate=pl.CostEstimate(
            flops=tiles_dev * (2 * tile_len * tile_len * (state_dim + 4 * inner_here + 2 * inner_here)),
            transcendentals=tiles_dev * tile_len * (tile_len * heads_here + 2 * inner_here),
            bytes_accessed=rows * inner_here * 10 + tiles_dev * inner_here * state_dim * 4,
        ),
    )(
        conv_out, conv_out, conv_out, cumul, cumul_t, dt_t, part_col, part_row,
        before_tile, prefix_wide, entering, zx, d_full,
    )


def shards(
    ingest,
    dest_tile,
    doc_start,
    w_zx,
    w_bc,
    w_dt,
    dt_bias,
    a_log,
    conv_x,
    conv_bc,
    cbias_x,
    cbias_bc,
    d_skip,
    norm_gain,
):
    seq_count = lax.axis_size("seq")
    tiles_dev = ingest.shape[0]
    tile_len = ingest.shape[1]
    columns = ingest.shape[2]
    row_count = tiles_dev * tile_len
    heads_here = a_log.shape[0]
    inner_here = conv_x.shape[1]
    head_dim = inner_here // heads_here
    state_dim = conv_bc.shape[1] // 2
    taps = conv_x.shape[0]
    keep_rows = taps - 1
    owner = dest_tile // tiles_dev
    slots = jnp.arange(seq_count, dtype=jnp.int32)
    pick = (owner[None, :] == slots[:, None]).astype(jnp.float32)
    outgoing = jnp.einsum(
        "sj,jrc->src", pick.astype(jnp.bfloat16), ingest, preferred_element_type=jnp.float32
    ).astype(jnp.bfloat16)
    incoming = lax.all_to_all(outgoing, "seq", split_axis=0, concat_axis=0, tiled=True)
    zx_cols, gather_dest = lax.optimization_barrier((w_zx.reshape(w_zx.shape[0], -1), dest_tile))
    every_dest = lax.all_gather(gather_dest, "seq", tiled=True).reshape(seq_count, tiles_dev)
    mine = every_dest // tiles_dev == lax.axis_index("seq")
    got_slot = jnp.sum(jnp.where(mine, every_dest % tiles_dev, 0), 1)
    local_slots = jnp.arange(tiles_dev, dtype=jnp.int32)
    place = (got_slot[None, :] == local_slots[:, None]).astype(jnp.bfloat16)
    arrived = jnp.einsum("js,src->jrc", place, incoming, preferred_element_type=jnp.float32).astype(
        jnp.bfloat16
    )
    own_rows = arrived.reshape(row_count, columns)
    weight_set = (zx_cols, w_bc, w_dt)
    if lax.axis_size("head") == 2:
        partner_rows = lax.ppermute(own_rows, "head", [(0, 1), (1, 0)])
        mine_at = lax.axis_index("head") * columns
        other_at = columns - mine_at

        def project(weight):
            own_part = lax.dynamic_slice_in_dim(weight, mine_at, columns, 0)
            other_part = lax.dynamic_slice_in_dim(weight, other_at, columns, 0)
            return jnp.dot(own_rows, own_part, preferred_element_type=jnp.float32) + jnp.dot(
                partner_rows, other_part, preferred_element_type=jnp.float32
            )

        acc_zx, acc_bc, acc_dt = tuple(project(weight) for weight in weight_set)
    else:
        piece = lax.all_gather(own_rows, "head", axis=1, tiled=True)
        acc_zx, acc_bc, acc_dt = tuple(
            (jnp.dot(piece, weight, preferred_element_type=jnp.float32) for weight in weight_set)
        )
    zx = acc_zx.astype(jnp.bfloat16)
    x_in = zx[:, inner_here:]
    bc_all = acc_bc.astype(jnp.bfloat16)
    step_dt = jax.nn.softplus(acc_dt + dt_bias[None, :])
    within = jnp.arange(tile_len, dtype=jnp.int32)
    has_bound = (doc_start < tile_len).astype(jnp.float32)
    before_count = jnp.cumsum(has_bound) - has_bound
    later = (within[None, :] >= doc_start[:, None]).astype(jnp.float32)
    segment = (before_count[:, None] + later).reshape(row_count)
    conv_in = jnp.concatenate([x_in, bc_all], 1)
    tail = conv_in[row_count - keep_rows :]
    tail_seg = (segment[row_count - keep_rows :] - segment[row_count - 1]).astype(jnp.bfloat16)
    got_both = shifted(jnp.concatenate([tail, tail_seg[:, None]], 1), "seq", 1)
    got_tail, got_seg = got_both[:, : tail.shape[1]], got_both[:, tail.shape[1]]
    extended = jnp.concatenate([got_tail, conv_in], 0)
    ext_seg = jnp.concatenate([got_seg.astype(jnp.float32), segment], 0)
    conv_weight = jnp.concatenate([conv_x, conv_bc], 1)
    conv_bias = jnp.concatenate([cbias_x, cbias_bc], 0)
    total = conv_bias[None, :] + conv_weight[taps - 1][None, :] * conv_in.astype(jnp.float32)
    for back_step in range(keep_rows):
        same = ext_seg[back_step : back_step + row_count] == segment
        total = total + jnp.where(
            same[:, None],
            conv_weight[back_step][None, :]
            * extended[back_step : back_step + row_count].astype(jnp.float32),
            0.0,
        )
    conv_out = jax.nn.silu(total).astype(jnp.bfloat16)
    rate = -jnp.exp(a_log)
    tile_dt = step_dt.reshape(tiles_dev, tile_len, heads_here)
    lower = (within[:, None] >= within[None, :]).astype(jnp.float32)
    cumul = jnp.einsum(
        "is,jsh->jih", lower, tile_dt * rate[None, None, :], precision=lax.Precision.HIGHEST
    )
    cumul_t = cumul.transpose(0, 2, 1)
    dt_t = tile_dt.transpose(0, 2, 1)
    last_part = later[:, tile_len - 1]
    tail_keep = (later == last_part[:, None]).astype(jnp.float32)
    to_end = jnp.exp(cumul[:, tile_len - 1 :, :] - cumul) * tile_dt * tail_keep[:, :, None]
    b_t = conv_out[:, inner_here : inner_here + state_dim].reshape(
        tiles_dev, tile_len, state_dim
    ).transpose(0, 2, 1)
    passing = jnp.exp(cumul[:, tile_len - 1, :]) * (1.0 - has_bound)[:, None]
    through = jnp.cumprod(passing, 0)
    prefix = jnp.concatenate([jnp.ones((1, heads_here), jnp.float32), through[:-1]], 0)
    widen = lambda per_head: jnp.repeat(per_head, head_dim, axis=-1)
    before_tile, run_state = contrib_tiles(
        conv_out, b_t, to_end, widen(passing)[:, None, :], inner_here, state_dim
    )
    position = lax.axis_index("seq")
    run_decay = widen(through[tiles_dev - 1])
    distance = 1
    def with_decay(state, decay):
        high = decay.astype(jnp.bfloat16)
        rest = decay - high.astype(jnp.float32)
        middle = rest.astype(jnp.bfloat16)
        low = (rest - middle.astype(jnp.float32)).astype(jnp.bfloat16)
        return jnp.concatenate([state.astype(jnp.bfloat16), high[None], middle[None], low[None]], 0)

    def unpack(got):
        got = got.astype(jnp.float32)
        return got[:state_dim], got[state_dim] + got[state_dim + 1] + got[state_dim + 2]

    while 2 * distance < seq_count:
        got_state, got_decay = unpack(shifted(with_decay(run_state, run_decay), "seq", distance))
        run_state = run_state + run_decay[None, :] * got_state
        run_decay = jnp.where(position >= distance, run_decay * got_decay, run_decay)
        distance *= 2
    near_state, near_decay = unpack(shifted(with_decay(run_state, run_decay), "seq", 1))
    far_state = shifted(run_state.astype(jnp.bfloat16), "seq", distance + 1).astype(jnp.float32)
    entering = near_state + near_decay[None, :] * far_state
    d_full = jnp.repeat(d_skip, head_dim)[None, :]
    gated, row_sq = mix_tiles(
        conv_out, zx, cumul, cumul_t, dt_t, later, before_tile, widen(prefix)[:, None, :],
        entering, d_full,
    )
    sums = lax.psum(row_sq.reshape(tiles_dev, tile_len), "head").reshape(row_count, 1)
    return (gated * lax.rsqrt(sums / INNER + EPSILON) * norm_gain[None, :]).astype(jnp.bfloat16)


def solution(mesh):
    return jax.shard_map(
        shards,
        mesh=mesh,
        in_specs=(
            P("seq", None, "head"),
            P("seq"),
            P("seq"),
            P(None, None, "head"),
            P(),
            P(None, "head"),
            P("head"),
            P("head"),
            P(None, "head"),
            P(),
            P("head"),
            P(),
            P("head"),
            P("head"),
        ),
        out_specs=P("seq", "head"),
        check_vma=False,
    )
```

```python
import jax
import jax.numpy as jnp
from jax import lax
from jax.experimental import pallas as pl
from jax.experimental.pallas import tpu as pltpu
from jax.sharding import PartitionSpec as P

INNER = 2048


EPSILON = 1e-05


def shifted(x, axis, by):
    devices = lax.axis_size(axis)
    pairs = [(i, i + by) for i in range(devices) if 0 <= i + by < devices]
    return lax.ppermute(x, axis, pairs)


def mix_tile(
    x_ref, b_ref, c_ref, cum_ref, cumt_ref, dtt_ref, partc_ref, partr_ref, before_ref, prefix_ref,
    enter_ref, gate_ref, d_ref, out_ref, sq_ref,
):
    f32 = jnp.float32
    tile_len = x_ref.shape[0]
    pairs = x_ref.shape[1] // 128
    b_mat = b_ref[...]
    c_mat = c_ref[...]
    scores = lax.dot_general(
        c_mat, b_mat, (((1,), (1,)), ((), ())), preferred_element_type=f32
    )
    cum = cum_ref[0]
    cumt = cumt_ref[0]
    dtt = dtt_ref[0]
    part_col = partc_ref[0]
    part_row = partr_ref[0]
    row = lax.broadcasted_iota(jnp.int32, (tile_len, tile_len), 0)
    col = lax.broadcasted_iota(jnp.int32, (tile_len, tile_len), 1)
    keep = (row >= col) & (part_col == part_row)
    earlier = 1.0 - part_col
    first_half = lax.broadcasted_iota(jnp.int32, (tile_len, 128), 1) < 64
    total_sq = jnp.zeros((tile_len, 128), f32)
    for pair in range(pairs):
        cols = pl.ds(pair * 128, 128)
        x_pair = x_ref[:, cols]
        slabs = []
        for half in range(2):
            head = 2 * pair + half
            diff = cum[:, head : head + 1] - cumt[head : head + 1, :]
            decay = jnp.where(keep, jnp.exp(jnp.where(keep, diff, 0.0)), 0.0)
            slabs.append((scores * decay * dtt[head : head + 1, :]).astype(jnp.bfloat16))
        weights = jnp.concatenate(slabs, axis=1)
        zero = jnp.zeros_like(x_pair)
        split_x = jnp.concatenate(
            [jnp.where(first_half, x_pair, zero), jnp.where(first_half, zero, x_pair)], axis=0
        )
        intra = jnp.dot(weights, split_x, preferred_element_type=f32)
        carried = (
            before_ref[0, :, cols] + prefix_ref[0, :, cols] * enter_ref[:, cols]
        ).astype(jnp.bfloat16)
        projected = jnp.dot(c_mat, carried, preferred_element_type=f32)
        grow = jnp.where(
            first_half,
            jnp.exp(cum[:, 2 * pair : 2 * pair + 1]),
            jnp.exp(cum[:, 2 * pair + 1 : 2 * pair + 2]),
        )
        inter = grow * earlier * projected
        mixed = intra + inter + d_ref[:, cols] * x_pair.astype(f32)
        gate = gate_ref[:, cols].astype(f32)
        gated = mixed * (gate * (0.5 + 0.5 * jnp.tanh(0.5 * gate)))
        out_ref[:, cols] = gated
        total_sq = total_sq + gated * gated
    sq_ref[...] = jnp.sum(total_sq, axis=1, keepdims=True)


def contrib_tile(x_ref, bt_ref, end_ref, pass_ref, before_ref, total_ref):
    f32 = jnp.float32
    group = bt_ref.shape[0]
    tile_len = bt_ref.shape[2]
    pairs = x_ref.shape[1] // 128

    @pl.when(pl.program_id(0) == 0)
    def _():
        total_ref[...] = jnp.zeros_like(total_ref)

    first_half = lax.broadcasted_iota(jnp.int32, (tile_len, 128), 1) < 64
    for sub in range(group):
        b_t = bt_ref[sub]
        to_end = end_ref[sub]
        rows = pl.ds(sub * tile_len, tile_len)
        for pair in range(pairs):
            cols = pl.ds(pair * 128, 128)
            scale = jnp.where(
                first_half,
                to_end[:, 2 * pair : 2 * pair + 1],
                to_end[:, 2 * pair + 1 : 2 * pair + 2],
            )
            scaled = (x_ref[rows, cols].astype(f32) * scale).astype(jnp.bfloat16)
            contrib = jnp.dot(b_t, scaled, preferred_element_type=f32)
            state = total_ref[:, cols]
            before_ref[sub, :, cols] = state
            total_ref[:, cols] = pass_ref[sub, :, cols] * state + contrib


def contrib_tiles(conv_out, b_t, to_end, passing_wide, inner_here, state_dim):
    tiles_dev, tile_len, heads_here = to_end.shape
    group = 2 if tiles_dev % 2 == 0 else 1
    return pl.pallas_call(
        contrib_tile,
        grid=(tiles_dev // group,),
        in_specs=[
            pl.BlockSpec((group * tile_len, inner_here), lambda j: (j, 0)),
            pl.BlockSpec((group, state_dim, tile_len), lambda j: (j, 0, 0)),
            pl.BlockSpec((group, tile_len, heads_here), lambda j: (j, 0, 0)),
            pl.BlockSpec((group, 1, inner_here), lambda j: (j, 0, 0)),
        ],
        out_specs=[
            pl.BlockSpec((group, state_dim, inner_here), lambda j: (j, 0, 0)),
            pl.BlockSpec((state_dim, inner_here), lambda j: (0, 0)),
        ],
        out_shape=[
            jax.ShapeDtypeStruct((tiles_dev, state_dim, inner_here), jnp.float32),
            jax.ShapeDtypeStruct((state_dim, inner_here), jnp.float32),
        ],
        compiler_params=pltpu.CompilerParams(dimension_semantics=("arbitrary",)),
        cost_estimate=pl.CostEstimate(
            flops=tiles_dev * 2 * tile_len * inner_here * state_dim,
            transcendentals=0,
            bytes_accessed=tiles_dev * (tile_len * (inner_here + state_dim) * 2 + inner_here * state_dim * 4),
        ),
    )(conv_out, b_t, to_end, passing_wide)


def mix_tiles(conv_out, zx, cumul, cumul_t, dt_t, later, before_tile, prefix_wide, entering, d_full):
    tiles_dev, tile_len, heads_here = cumul.shape
    inner_here = before_tile.shape[2]
    state_dim = before_tile.shape[1]
    rows = tiles_dev * tile_len
    b_block = inner_here // 128
    c_block = b_block + state_dim // 128
    part_col = later.reshape(tiles_dev, tile_len, 1)
    part_row = later.reshape(tiles_dev, 1, tile_len)
    per_tile = lambda j: (j, 0, 0)
    return pl.pallas_call(
        mix_tile,
        grid=(tiles_dev,),
        in_specs=[
            pl.BlockSpec((tile_len, inner_here), lambda j: (j, 0)),
            pl.BlockSpec((tile_len, state_dim), lambda j: (j, b_block)),
            pl.BlockSpec((tile_len, state_dim), lambda j: (j, c_block)),
            pl.BlockSpec((1, tile_len, heads_here), per_tile),
            pl.BlockSpec((1, heads_here, tile_len), per_tile),
            pl.BlockSpec((1, heads_here, tile_len), per_tile),
            pl.BlockSpec((1, tile_len, 1), per_tile),
            pl.BlockSpec((1, 1, tile_len), per_tile),
            pl.BlockSpec((1, state_dim, inner_here), per_tile),
            pl.BlockSpec((1, 1, inner_here), per_tile),
            pl.BlockSpec((state_dim, inner_here), lambda j: (0, 0)),
            pl.BlockSpec((tile_len, inner_here), lambda j: (j, 0)),
            pl.BlockSpec((1, inner_here), lambda j: (0, 0)),
        ],
        out_specs=[
            pl.BlockSpec((tile_len, inner_here), lambda j: (j, 0)),
            pl.BlockSpec((tile_len, 1), lambda j: (j, 0)),
        ],
        out_shape=[
            jax.ShapeDtypeStruct((rows, inner_here), jnp.float32),
            jax.ShapeDtypeStruct((rows, 1), jnp.float32),
        ],
        cost_estimate=pl.CostEstimate(
            flops=tiles_dev * (2 * tile_len * tile_len * (state_dim + 4 * inner_here + 2 * inner_here)),
            transcendentals=tiles_dev * tile_len * (tile_len * heads_here + 2 * inner_here),
            bytes_accessed=rows * inner_here * 10 + tiles_dev * inner_here * state_dim * 4,
        ),
    )(
        conv_out, conv_out, conv_out, cumul, cumul_t, dt_t, part_col, part_row,
        before_tile, prefix_wide, entering, zx, d_full,
    )


def shards(
    ingest,
    dest_tile,
    doc_start,
    w_zx,
    w_bc,
    w_dt,
    dt_bias,
    a_log,
    conv_x,
    conv_bc,
    cbias_x,
    cbias_bc,
    d_skip,
    norm_gain,
):
    seq_count = lax.axis_size("seq")
    tiles_dev = ingest.shape[0]
    tile_len = ingest.shape[1]
    columns = ingest.shape[2]
    row_count = tiles_dev * tile_len
    heads_here = a_log.shape[0]
    inner_here = conv_x.shape[1]
    head_dim = inner_here // heads_here
    state_dim = conv_bc.shape[1] // 2
    taps = conv_x.shape[0]
    keep_rows = taps - 1
    owner = dest_tile // tiles_dev
    slots = jnp.arange(seq_count, dtype=jnp.int32)
    pick = (owner[None, :] == slots[:, None]).astype(jnp.float32)
    outgoing = jnp.einsum(
        "sj,jrc->src", pick.astype(jnp.bfloat16), ingest, preferred_element_type=jnp.float32
    ).astype(jnp.bfloat16)
    incoming = lax.all_to_all(outgoing, "seq", split_axis=0, concat_axis=0, tiled=True)
    zx_cols, gather_dest = lax.optimization_barrier((w_zx.reshape(w_zx.shape[0], -1), dest_tile))
    every_dest = lax.all_gather(gather_dest, "seq", tiled=True).reshape(seq_count, tiles_dev)
    mine = every_dest // tiles_dev == lax.axis_index("seq")
    got_slot = jnp.sum(jnp.where(mine, every_dest % tiles_dev, 0), 1)
    local_slots = jnp.arange(tiles_dev, dtype=jnp.int32)
    place = (got_slot[None, :] == local_slots[:, None]).astype(jnp.bfloat16)
    arrived = jnp.einsum("js,src->jrc", place, incoming, preferred_element_type=jnp.float32).astype(
        jnp.bfloat16
    )
    own_rows = arrived.reshape(row_count, columns)
    weight_set = (zx_cols, w_bc, w_dt)
    if lax.axis_size("head") == 2:
        partner_rows = lax.ppermute(own_rows, "head", [(0, 1), (1, 0)])
        mine_at = lax.axis_index("head") * columns
        other_at = columns - mine_at

        def project(weight):
            own_part = lax.dynamic_slice_in_dim(weight, mine_at, columns, 0)
            other_part = lax.dynamic_slice_in_dim(weight, other_at, columns, 0)
            return jnp.dot(own_rows, own_part, preferred_element_type=jnp.float32) + jnp.dot(
                partner_rows, other_part, preferred_element_type=jnp.float32
            )

        acc_zx, acc_bc, acc_dt = tuple(project(weight) for weight in weight_set)
    else:
        piece = lax.all_gather(own_rows, "head", axis=1, tiled=True)
        acc_zx, acc_bc, acc_dt = tuple(
            (jnp.dot(piece, weight, preferred_element_type=jnp.float32) for weight in weight_set)
        )
    zx = acc_zx.astype(jnp.bfloat16)
    x_in = zx[:, inner_here:]
    bc_all = acc_bc.astype(jnp.bfloat16)
    step_dt = jax.nn.softplus(acc_dt + dt_bias[None, :])
    within = jnp.arange(tile_len, dtype=jnp.int32)
    has_bound = (doc_start < tile_len).astype(jnp.float32)
    before_count = jnp.cumsum(has_bound) - has_bound
    later = (within[None, :] >= doc_start[:, None]).astype(jnp.float32)
    segment = (before_count[:, None] + later).reshape(row_count)
    conv_in = jnp.concatenate([x_in, bc_all], 1)
    tail = conv_in[row_count - keep_rows :]
    tail_seg = (segment[row_count - keep_rows :] - segment[row_count - 1]).astype(jnp.bfloat16)
    got_both = shifted(jnp.concatenate([tail, tail_seg[:, None]], 1), "seq", 1)
    got_tail, got_seg = got_both[:, : tail.shape[1]], got_both[:, tail.shape[1]]
    extended = jnp.concatenate([got_tail, conv_in], 0)
    ext_seg = jnp.concatenate([got_seg.astype(jnp.float32), segment], 0)
    conv_weight = jnp.concatenate([conv_x, conv_bc], 1)
    conv_bias = jnp.concatenate([cbias_x, cbias_bc], 0)
    total = conv_bias[None, :] + conv_weight[taps - 1][None, :] * conv_in.astype(jnp.float32)
    for back_step in range(keep_rows):
        same = ext_seg[back_step : back_step + row_count] == segment
        total = total + jnp.where(
            same[:, None],
            conv_weight[back_step][None, :]
            * extended[back_step : back_step + row_count].astype(jnp.float32),
            0.0,
        )
    conv_out = jax.nn.silu(total).astype(jnp.bfloat16)
    rate = -jnp.exp(a_log)
    tile_dt = step_dt.reshape(tiles_dev, tile_len, heads_here)
    lower = (within[:, None] >= within[None, :]).astype(jnp.float32)
    cumul = jnp.einsum(
        "is,jsh->jih", lower, tile_dt * rate[None, None, :], precision=lax.Precision.HIGHEST
    )
    cumul_t = cumul.transpose(0, 2, 1)
    dt_t = tile_dt.transpose(0, 2, 1)
    last_part = later[:, tile_len - 1]
    tail_keep = (later == last_part[:, None]).astype(jnp.float32)
    to_end = jnp.exp(cumul[:, tile_len - 1 :, :] - cumul) * tile_dt * tail_keep[:, :, None]
    b_t = conv_out[:, inner_here : inner_here + state_dim].reshape(
        tiles_dev, tile_len, state_dim
    ).transpose(0, 2, 1)
    passing = jnp.exp(cumul[:, tile_len - 1, :]) * (1.0 - has_bound)[:, None]
    through = jnp.cumprod(passing, 0)
    prefix = jnp.concatenate([jnp.ones((1, heads_here), jnp.float32), through[:-1]], 0)
    widen = lambda per_head: jnp.repeat(per_head, head_dim, axis=-1)
    before_tile, run_state = contrib_tiles(
        conv_out, b_t, to_end, widen(passing)[:, None, :], inner_here, state_dim
    )
    position = lax.axis_index("seq")
    run_decay = widen(through[tiles_dev - 1])
    distance = 1
    def with_decay(state, decay):
        high = decay.astype(jnp.bfloat16)
        rest = decay - high.astype(jnp.float32)
        middle = rest.astype(jnp.bfloat16)
        low = (rest - middle.astype(jnp.float32)).astype(jnp.bfloat16)
        return jnp.concatenate([state.astype(jnp.bfloat16), high[None], middle[None], low[None]], 0)

    def unpack(got):
        got = got.astype(jnp.float32)
        return got[:state_dim], got[state_dim] + got[state_dim + 1] + got[state_dim + 2]

    while 2 * distance < seq_count:
        got_state, got_decay = unpack(shifted(with_decay(run_state, run_decay), "seq", distance))
        run_state = run_state + run_decay[None, :] * got_state
        run_decay = jnp.where(position >= distance, run_decay * got_decay, run_decay)
        distance *= 2
    near_state, near_decay = unpack(shifted(with_decay(run_state, run_decay), "seq", 1))
    far_state = shifted(run_state.astype(jnp.bfloat16), "seq", distance + 1).astype(jnp.float32)
    entering = near_state + near_decay[None, :] * far_state
    d_full = jnp.repeat(d_skip, head_dim)[None, :]
    gated, row_sq = mix_tiles(
        conv_out, zx, cumul, cumul_t, dt_t, later, before_tile, widen(prefix)[:, None, :],
        entering, d_full,
    )
    sums = lax.psum(row_sq.reshape(tiles_dev, tile_len), "head").reshape(row_count, 1)
    return (gated * lax.rsqrt(sums / INNER + EPSILON) * norm_gain[None, :]).astype(jnp.bfloat16)


def solution(mesh):
    return jax.shard_map(
        shards,
        mesh=mesh,
        in_specs=(
            P("seq", None, "head"),
            P("seq"),
            P("seq"),
            P(None, None, "head"),
            P(),
            P(None, "head"),
            P("head"),
            P("head"),
            P(None, "head"),
            P(),
            P("head"),
            P(),
            P("head"),
            P("head"),
        ),
        out_specs=P("seq", "head"),
        check_vma=False,
    )
```

```python
import jax
import jax.numpy as jnp
from jax import lax
from jax.experimental import pallas as pl
from jax.experimental.pallas import tpu as pltpu
from jax.sharding import PartitionSpec as P

INNER = 2048


EPSILON = 1e-05


def shifted(x, axis, by):
    devices = lax.axis_size(axis)
    pairs = [(i, i + by) for i in range(devices) if 0 <= i + by < devices]
    return lax.ppermute(x, axis, pairs)


def mix_tile(
    x_ref, b_ref, c_ref, cum_ref, cumt_ref, dtt_ref, partc_ref, partr_ref, before_ref, prefix_ref,
    enter_ref, gate_ref, d_ref, out_ref, sq_ref,
):
    f32 = jnp.float32
    group = cum_ref.shape[0]
    tile_len = cum_ref.shape[1]
    pairs = x_ref.shape[1] // 128
    row = lax.broadcasted_iota(jnp.int32, (tile_len, tile_len), 0)
    col = lax.broadcasted_iota(jnp.int32, (tile_len, tile_len), 1)
    first_half = lax.broadcasted_iota(jnp.int32, (tile_len, 128), 1) < 64
    for sub in range(group):
        rows = pl.ds(sub * tile_len, tile_len)
        c_mat = c_ref[rows, :]
        scores = lax.dot_general(
            c_mat, b_ref[rows, :], (((1,), (1,)), ((), ())), preferred_element_type=f32
        )
        cum = cum_ref[sub]
        cumt = cumt_ref[sub]
        dtt = dtt_ref[sub]
        part_col = partc_ref[sub]
        keep = (row >= col) & (part_col == partr_ref[sub])
        earlier = 1.0 - part_col
        total_sq = jnp.zeros((tile_len, 128), f32)
        for pair in range(pairs):
            cols = pl.ds(pair * 128, 128)
            x_pair = x_ref[rows, cols]
            slabs = []
            for half in range(2):
                head = 2 * pair + half
                diff = cum[:, head : head + 1] - cumt[head : head + 1, :]
                decay = jnp.where(keep, jnp.exp(jnp.where(keep, diff, 0.0)), 0.0)
                slabs.append((scores * decay * dtt[head : head + 1, :]).astype(jnp.bfloat16))
            weights = jnp.concatenate(slabs, axis=1)
            zero = jnp.zeros_like(x_pair)
            split_x = jnp.concatenate(
                [jnp.where(first_half, x_pair, zero), jnp.where(first_half, zero, x_pair)], axis=0
            )
            intra = jnp.dot(weights, split_x, preferred_element_type=f32)
            carried = (
                before_ref[sub, :, cols] + prefix_ref[sub, :, cols] * enter_ref[:, cols]
            ).astype(jnp.bfloat16)
            projected = jnp.dot(c_mat, carried, preferred_element_type=f32)
            grow = jnp.where(
                first_half,
                jnp.exp(cum[:, 2 * pair : 2 * pair + 1]),
                jnp.exp(cum[:, 2 * pair + 1 : 2 * pair + 2]),
            )
            inter = grow * earlier * projected
            mixed = intra + inter + d_ref[:, cols] * x_pair.astype(f32)
            gate = gate_ref[rows, cols].astype(f32)
            gated = mixed * (gate * (0.5 + 0.5 * jnp.tanh(0.5 * gate)))
            out_ref[rows, cols] = gated
            total_sq = total_sq + gated * gated
        sq_ref[rows, :] = jnp.sum(total_sq, axis=1, keepdims=True)


def contrib_tile(x_ref, bt_ref, end_ref, pass_ref, before_ref, total_ref):
    f32 = jnp.float32
    group = bt_ref.shape[0]
    tile_len = bt_ref.shape[2]
    pairs = x_ref.shape[1] // 128

    @pl.when(pl.program_id(0) == 0)
    def _():
        total_ref[...] = jnp.zeros_like(total_ref)

    first_half = lax.broadcasted_iota(jnp.int32, (tile_len, 128), 1) < 64
    for sub in range(group):
        b_t = bt_ref[sub]
        to_end = end_ref[sub]
        rows = pl.ds(sub * tile_len, tile_len)
        for pair in range(pairs):
            cols = pl.ds(pair * 128, 128)
            scale = jnp.where(
                first_half,
                to_end[:, 2 * pair : 2 * pair + 1],
                to_end[:, 2 * pair + 1 : 2 * pair + 2],
            )
            scaled = (x_ref[rows, cols].astype(f32) * scale).astype(jnp.bfloat16)
            contrib = jnp.dot(b_t, scaled, preferred_element_type=f32)
            state = total_ref[:, cols]
            before_ref[sub, :, cols] = state
            total_ref[:, cols] = pass_ref[sub, :, cols] * state + contrib


def contrib_tiles(conv_out, b_t, to_end, passing_wide, inner_here, state_dim):
    tiles_dev, tile_len, heads_here = to_end.shape
    group = 4 if tiles_dev % 4 == 0 else 1
    return pl.pallas_call(
        contrib_tile,
        grid=(tiles_dev // group,),
        in_specs=[
            pl.BlockSpec((group * tile_len, inner_here), lambda j: (j, 0)),
            pl.BlockSpec((group, state_dim, tile_len), lambda j: (j, 0, 0)),
            pl.BlockSpec((group, tile_len, heads_here), lambda j: (j, 0, 0)),
            pl.BlockSpec((group, 1, inner_here), lambda j: (j, 0, 0)),
        ],
        out_specs=[
            pl.BlockSpec((group, state_dim, inner_here), lambda j: (j, 0, 0)),
            pl.BlockSpec((state_dim, inner_here), lambda j: (0, 0)),
        ],
        out_shape=[
            jax.ShapeDtypeStruct((tiles_dev, state_dim, inner_here), jnp.float32),
            jax.ShapeDtypeStruct((state_dim, inner_here), jnp.float32),
        ],
        compiler_params=pltpu.CompilerParams(dimension_semantics=("arbitrary",)),
        cost_estimate=pl.CostEstimate(
            flops=tiles_dev * 2 * tile_len * inner_here * state_dim,
            transcendentals=0,
            bytes_accessed=tiles_dev * (tile_len * (inner_here + state_dim) * 2 + inner_here * state_dim * 4),
        ),
    )(conv_out, b_t, to_end, passing_wide)


def mix_tiles(conv_out, zx, cumul, cumul_t, dt_t, later, before_tile, prefix_wide, entering, d_full):
    tiles_dev, tile_len, heads_here = cumul.shape
    inner_here = before_tile.shape[2]
    state_dim = before_tile.shape[1]
    rows = tiles_dev * tile_len
    b_block = inner_here // 128
    c_block = b_block + state_dim // 128
    part_col = later.reshape(tiles_dev, tile_len, 1)
    part_row = later.reshape(tiles_dev, 1, tile_len)
    group = 2 if tiles_dev % 2 == 0 else 1
    per_tile = lambda j: (j, 0, 0)
    span = group * tile_len
    return pl.pallas_call(
        mix_tile,
        grid=(tiles_dev // group,),
        in_specs=[
            pl.BlockSpec((span, inner_here), lambda j: (j, 0)),
            pl.BlockSpec((span, state_dim), lambda j: (j, b_block)),
            pl.BlockSpec((span, state_dim), lambda j: (j, c_block)),
            pl.BlockSpec((group, tile_len, heads_here), per_tile),
            pl.BlockSpec((group, heads_here, tile_len), per_tile),
            pl.BlockSpec((group, heads_here, tile_len), per_tile),
            pl.BlockSpec((group, tile_len, 1), per_tile),
            pl.BlockSpec((group, 1, tile_len), per_tile),
            pl.BlockSpec((group, state_dim, inner_here), per_tile),
            pl.BlockSpec((group, 1, inner_here), per_tile),
            pl.BlockSpec((state_dim, inner_here), lambda j: (0, 0)),
            pl.BlockSpec((span, inner_here), lambda j: (j, 0)),
            pl.BlockSpec((1, inner_here), lambda j: (0, 0)),
        ],
        out_specs=[
            pl.BlockSpec((span, inner_here), lambda j: (j, 0)),
            pl.BlockSpec((span, 1), lambda j: (j, 0)),
        ],
        out_shape=[
            jax.ShapeDtypeStruct((rows, inner_here), jnp.float32),
            jax.ShapeDtypeStruct((rows, 1), jnp.float32),
        ],
        cost_estimate=pl.CostEstimate(
            flops=tiles_dev * (2 * tile_len * tile_len * (state_dim + 4 * inner_here + 2 * inner_here)),
            transcendentals=tiles_dev * tile_len * (tile_len * heads_here + 2 * inner_here),
            bytes_accessed=rows * inner_here * 10 + tiles_dev * inner_here * state_dim * 4,
        ),
    )(
        conv_out, conv_out, conv_out, cumul, cumul_t, dt_t, part_col, part_row,
        before_tile, prefix_wide, entering, zx, d_full,
    )


def shards(
    ingest,
    dest_tile,
    doc_start,
    w_zx,
    w_bc,
    w_dt,
    dt_bias,
    a_log,
    conv_x,
    conv_bc,
    cbias_x,
    cbias_bc,
    d_skip,
    norm_gain,
):
    seq_count = lax.axis_size("seq")
    tiles_dev = ingest.shape[0]
    tile_len = ingest.shape[1]
    columns = ingest.shape[2]
    row_count = tiles_dev * tile_len
    heads_here = a_log.shape[0]
    inner_here = conv_x.shape[1]
    head_dim = inner_here // heads_here
    state_dim = conv_bc.shape[1] // 2
    taps = conv_x.shape[0]
    keep_rows = taps - 1
    owner = dest_tile // tiles_dev
    slots = jnp.arange(seq_count, dtype=jnp.int32)
    pick = (owner[None, :] == slots[:, None]).astype(jnp.float32)
    outgoing = jnp.einsum(
        "sj,jrc->src", pick.astype(jnp.bfloat16), ingest, preferred_element_type=jnp.float32
    ).astype(jnp.bfloat16)
    incoming = lax.all_to_all(outgoing, "seq", split_axis=0, concat_axis=0, tiled=True)
    zx_cols, gather_dest = lax.optimization_barrier((w_zx.reshape(w_zx.shape[0], -1), dest_tile))
    every_dest = lax.all_gather(gather_dest, "seq", tiled=True).reshape(seq_count, tiles_dev)
    mine = every_dest // tiles_dev == lax.axis_index("seq")
    got_slot = jnp.sum(jnp.where(mine, every_dest % tiles_dev, 0), 1)
    local_slots = jnp.arange(tiles_dev, dtype=jnp.int32)
    place = (got_slot[None, :] == local_slots[:, None]).astype(jnp.bfloat16)
    arrived = jnp.einsum("js,src->jrc", place, incoming, preferred_element_type=jnp.float32).astype(
        jnp.bfloat16
    )
    own_rows = arrived.reshape(row_count, columns)
    weight_set = (zx_cols, w_bc, w_dt)
    if lax.axis_size("head") == 2:
        partner_rows = lax.ppermute(own_rows, "head", [(0, 1), (1, 0)])
        mine_at = lax.axis_index("head") * columns
        other_at = columns - mine_at

        def project(weight):
            own_part = lax.dynamic_slice_in_dim(weight, mine_at, columns, 0)
            other_part = lax.dynamic_slice_in_dim(weight, other_at, columns, 0)
            return jnp.dot(own_rows, own_part, preferred_element_type=jnp.float32) + jnp.dot(
                partner_rows, other_part, preferred_element_type=jnp.float32
            )

        acc_zx, acc_bc, acc_dt = tuple(project(weight) for weight in weight_set)
    else:
        piece = lax.all_gather(own_rows, "head", axis=1, tiled=True)
        acc_zx, acc_bc, acc_dt = tuple(
            (jnp.dot(piece, weight, preferred_element_type=jnp.float32) for weight in weight_set)
        )
    zx = acc_zx.astype(jnp.bfloat16)
    x_in = zx[:, inner_here:]
    bc_all = acc_bc.astype(jnp.bfloat16)
    step_dt = jax.nn.softplus(acc_dt + dt_bias[None, :])
    within = jnp.arange(tile_len, dtype=jnp.int32)
    has_bound = (doc_start < tile_len).astype(jnp.float32)
    before_count = jnp.cumsum(has_bound) - has_bound
    later = (within[None, :] >= doc_start[:, None]).astype(jnp.float32)
    segment = (before_count[:, None] + later).reshape(row_count)
    conv_in = jnp.concatenate([x_in, bc_all], 1)
    tail = conv_in[row_count - keep_rows :]
    tail_seg = (segment[row_count - keep_rows :] - segment[row_count - 1]).astype(jnp.bfloat16)
    got_both = shifted(jnp.concatenate([tail, tail_seg[:, None]], 1), "seq", 1)
    got_tail, got_seg = got_both[:, : tail.shape[1]], got_both[:, tail.shape[1]]
    extended = jnp.concatenate([got_tail, conv_in], 0)
    ext_seg = jnp.concatenate([got_seg.astype(jnp.float32), segment], 0)
    conv_weight = jnp.concatenate([conv_x, conv_bc], 1)
    conv_bias = jnp.concatenate([cbias_x, cbias_bc], 0)
    total = conv_bias[None, :] + conv_weight[taps - 1][None, :] * conv_in.astype(jnp.float32)
    for back_step in range(keep_rows):
        same = ext_seg[back_step : back_step + row_count] == segment
        total = total + jnp.where(
            same[:, None],
            conv_weight[back_step][None, :]
            * extended[back_step : back_step + row_count].astype(jnp.float32),
            0.0,
        )
    conv_out = jax.nn.silu(total).astype(jnp.bfloat16)
    rate = -jnp.exp(a_log)
    tile_dt = step_dt.reshape(tiles_dev, tile_len, heads_here)
    lower = (within[:, None] >= within[None, :]).astype(jnp.float32)
    cumul = jnp.einsum(
        "is,jsh->jih", lower, tile_dt * rate[None, None, :], precision=lax.Precision.HIGHEST
    )
    cumul_t = cumul.transpose(0, 2, 1)
    dt_t = tile_dt.transpose(0, 2, 1)
    last_part = later[:, tile_len - 1]
    tail_keep = (later == last_part[:, None]).astype(jnp.float32)
    to_end = jnp.exp(cumul[:, tile_len - 1 :, :] - cumul) * tile_dt * tail_keep[:, :, None]
    b_t = conv_out[:, inner_here : inner_here + state_dim].reshape(
        tiles_dev, tile_len, state_dim
    ).transpose(0, 2, 1)
    passing = jnp.exp(cumul[:, tile_len - 1, :]) * (1.0 - has_bound)[:, None]
    through = jnp.cumprod(passing, 0)
    prefix = jnp.concatenate([jnp.ones((1, heads_here), jnp.float32), through[:-1]], 0)
    widen = lambda per_head: jnp.repeat(per_head, head_dim, axis=-1)
    before_tile, run_state = contrib_tiles(
        conv_out, b_t, to_end, widen(passing)[:, None, :], inner_here, state_dim
    )
    position = lax.axis_index("seq")
    run_decay = widen(through[tiles_dev - 1])
    distance = 1
    def with_decay(state, decay):
        high = decay.astype(jnp.bfloat16)
        rest = decay - high.astype(jnp.float32)
        middle = rest.astype(jnp.bfloat16)
        low = (rest - middle.astype(jnp.float32)).astype(jnp.bfloat16)
        return jnp.concatenate([state.astype(jnp.bfloat16), high[None], middle[None], low[None]], 0)

    def unpack(got):
        got = got.astype(jnp.float32)
        return got[:state_dim], got[state_dim] + got[state_dim + 1] + got[state_dim + 2]

    while 2 * distance < seq_count:
        got_state, got_decay = unpack(shifted(with_decay(run_state, run_decay), "seq", distance))
        run_state = run_state + run_decay[None, :] * got_state
        run_decay = jnp.where(position >= distance, run_decay * got_decay, run_decay)
        distance *= 2
    near_state, near_decay = unpack(shifted(with_decay(run_state, run_decay), "seq", 1))
    far_state = shifted(run_state.astype(jnp.bfloat16), "seq", distance + 1).astype(jnp.float32)
    entering = near_state + near_decay[None, :] * far_state
    d_full = jnp.repeat(d_skip, head_dim)[None, :]
    gated, row_sq = mix_tiles(
        conv_out, zx, cumul, cumul_t, dt_t, later, before_tile, widen(prefix)[:, None, :],
        entering, d_full,
    )
    sums = lax.psum(row_sq.reshape(tiles_dev, tile_len), "head").reshape(row_count, 1)
    return (gated * lax.rsqrt(sums / INNER + EPSILON) * norm_gain[None, :]).astype(jnp.bfloat16)


def solution(mesh):
    return jax.shard_map(
        shards,
        mesh=mesh,
        in_specs=(
            P("seq", None, "head"),
            P("seq"),
            P("seq"),
            P(None, None, "head"),
            P(),
            P(None, "head"),
            P("head"),
            P("head"),
            P(None, "head"),
            P(),
            P("head"),
            P(),
            P("head"),
            P("head"),
        ),
        out_specs=P("seq", "head"),
        check_vma=False,
    )
```

```python
import jax
import jax.numpy as jnp
from jax import lax
from jax.experimental import pallas as pl
from jax.experimental.pallas import tpu as pltpu
from jax.sharding import PartitionSpec as P

INNER = 2048


EPSILON = 1e-05


def shifted(x, axis, by):
    devices = lax.axis_size(axis)
    pairs = [(i, i + by) for i in range(devices) if 0 <= i + by < devices]
    return lax.ppermute(x, axis, pairs)


def mix_tile(
    x_ref, b_ref, c_ref, cum_ref, cumt_ref, dtt_ref, partc_ref, partr_ref, before_ref, prefix_ref,
    enter_ref, gate_ref, d_ref, out_ref, sq_ref,
):
    f32 = jnp.float32
    group = cum_ref.shape[0]
    tile_len = cum_ref.shape[1]
    pairs = x_ref.shape[1] // 128
    row = lax.broadcasted_iota(jnp.int32, (tile_len, tile_len), 0)
    col = lax.broadcasted_iota(jnp.int32, (tile_len, tile_len), 1)
    first_half = lax.broadcasted_iota(jnp.int32, (tile_len, 128), 1) < 64
    for sub in range(group):
        rows = pl.ds(sub * tile_len, tile_len)
        c_mat = c_ref[rows, :]
        scores = lax.dot_general(
            c_mat, b_ref[rows, :], (((1,), (1,)), ((), ())), preferred_element_type=f32
        )
        cum = cum_ref[sub]
        cumt = cumt_ref[sub]
        dtt = dtt_ref[sub]
        part_col = partc_ref[sub]
        keep = (row >= col) & (part_col == partr_ref[sub])
        earlier = 1.0 - part_col
        total_sq = jnp.zeros((tile_len, 128), f32)
        for pair in range(pairs):
            cols = pl.ds(pair * 128, 128)
            x_pair = x_ref[rows, cols]
            slabs = []
            for half in range(2):
                head = 2 * pair + half
                diff = cum[:, head : head + 1] - cumt[head : head + 1, :]
                decay = jnp.where(keep, jnp.exp(jnp.where(keep, diff, 0.0)), 0.0)
                slabs.append((scores * decay * dtt[head : head + 1, :]).astype(jnp.bfloat16))
            weights = jnp.concatenate(slabs, axis=1)
            zero = jnp.zeros_like(x_pair)
            split_x = jnp.concatenate(
                [jnp.where(first_half, x_pair, zero), jnp.where(first_half, zero, x_pair)], axis=0
            )
            intra = jnp.dot(weights, split_x, preferred_element_type=f32)
            carried = (
                before_ref[sub, :, cols] + prefix_ref[sub, :, cols] * enter_ref[:, cols]
            ).astype(jnp.bfloat16)
            projected = jnp.dot(c_mat, carried, preferred_element_type=f32)
            grow = jnp.where(
                first_half,
                jnp.exp(cum[:, 2 * pair : 2 * pair + 1]),
                jnp.exp(cum[:, 2 * pair + 1 : 2 * pair + 2]),
            )
            inter = grow * earlier * projected
            mixed = intra + inter + d_ref[:, cols] * x_pair.astype(f32)
            gate = gate_ref[rows, cols].astype(f32)
            gated = mixed * (gate * (0.5 + 0.5 * jnp.tanh(0.5 * gate)))
            out_ref[rows, cols] = gated
            total_sq = total_sq + gated * gated
        sq_ref[rows, :] = jnp.sum(total_sq, axis=1, keepdims=True)


def contrib_tile(x_ref, bt_ref, end_ref, pass_ref, before_ref, total_ref):
    f32 = jnp.float32
    group = bt_ref.shape[0]
    tile_len = bt_ref.shape[2]
    pairs = x_ref.shape[1] // 128

    @pl.when(pl.program_id(0) == 0)
    def _():
        total_ref[...] = jnp.zeros_like(total_ref)

    first_half = lax.broadcasted_iota(jnp.int32, (tile_len, 128), 1) < 64
    for sub in range(group):
        b_t = bt_ref[sub]
        to_end = end_ref[sub]
        rows = pl.ds(sub * tile_len, tile_len)
        for pair in range(pairs):
            cols = pl.ds(pair * 128, 128)
            scale = jnp.where(
                first_half,
                to_end[:, 2 * pair : 2 * pair + 1],
                to_end[:, 2 * pair + 1 : 2 * pair + 2],
            )
            scaled = (x_ref[rows, cols].astype(f32) * scale).astype(jnp.bfloat16)
            contrib = jnp.dot(b_t, scaled, preferred_element_type=f32)
            state = total_ref[:, cols]
            before_ref[sub, :, cols] = state
            total_ref[:, cols] = pass_ref[sub, :, cols] * state + contrib


def contrib_tiles(conv_out, b_t, to_end, passing_wide, inner_here, state_dim):
    tiles_dev, tile_len, heads_here = to_end.shape
    group = 8 if tiles_dev % 8 == 0 else 1
    return pl.pallas_call(
        contrib_tile,
        grid=(tiles_dev // group,),
        in_specs=[
            pl.BlockSpec((group * tile_len, inner_here), lambda j: (j, 0)),
            pl.BlockSpec((group, state_dim, tile_len), lambda j: (j, 0, 0)),
            pl.BlockSpec((group, tile_len, heads_here), lambda j: (j, 0, 0)),
            pl.BlockSpec((group, 1, inner_here), lambda j: (j, 0, 0)),
        ],
        out_specs=[
            pl.BlockSpec((group, state_dim, inner_here), lambda j: (j, 0, 0)),
            pl.BlockSpec((state_dim, inner_here), lambda j: (0, 0)),
        ],
        out_shape=[
            jax.ShapeDtypeStruct((tiles_dev, state_dim, inner_here), jnp.float32),
            jax.ShapeDtypeStruct((state_dim, inner_here), jnp.float32),
        ],
        compiler_params=pltpu.CompilerParams(dimension_semantics=("arbitrary",)),
        cost_estimate=pl.CostEstimate(
            flops=tiles_dev * 2 * tile_len * inner_here * state_dim,
            transcendentals=0,
            bytes_accessed=tiles_dev * (tile_len * (inner_here + state_dim) * 2 + inner_here * state_dim * 4),
        ),
    )(conv_out, b_t, to_end, passing_wide)


def mix_tiles(conv_out, zx, cumul, cumul_t, dt_t, later, before_tile, prefix_wide, entering, d_full):
    tiles_dev, tile_len, heads_here = cumul.shape
    inner_here = before_tile.shape[2]
    state_dim = before_tile.shape[1]
    rows = tiles_dev * tile_len
    b_block = inner_here // 128
    c_block = b_block + state_dim // 128
    part_col = later.reshape(tiles_dev, tile_len, 1)
    part_row = later.reshape(tiles_dev, 1, tile_len)
    group = 4 if tiles_dev % 4 == 0 else 1
    per_tile = lambda j: (j, 0, 0)
    span = group * tile_len
    return pl.pallas_call(
        mix_tile,
        grid=(tiles_dev // group,),
        in_specs=[
            pl.BlockSpec((span, inner_here), lambda j: (j, 0)),
            pl.BlockSpec((span, state_dim), lambda j: (j, b_block)),
            pl.BlockSpec((span, state_dim), lambda j: (j, c_block)),
            pl.BlockSpec((group, tile_len, heads_here), per_tile),
            pl.BlockSpec((group, heads_here, tile_len), per_tile),
            pl.BlockSpec((group, heads_here, tile_len), per_tile),
            pl.BlockSpec((group, tile_len, 1), per_tile),
            pl.BlockSpec((group, 1, tile_len), per_tile),
            pl.BlockSpec((group, state_dim, inner_here), per_tile),
            pl.BlockSpec((group, 1, inner_here), per_tile),
            pl.BlockSpec((state_dim, inner_here), lambda j: (0, 0)),
            pl.BlockSpec((span, inner_here), lambda j: (j, 0)),
            pl.BlockSpec((1, inner_here), lambda j: (0, 0)),
        ],
        out_specs=[
            pl.BlockSpec((span, inner_here), lambda j: (j, 0)),
            pl.BlockSpec((span, 1), lambda j: (j, 0)),
        ],
        out_shape=[
            jax.ShapeDtypeStruct((rows, inner_here), jnp.float32),
            jax.ShapeDtypeStruct((rows, 1), jnp.float32),
        ],
        cost_estimate=pl.CostEstimate(
            flops=tiles_dev * (2 * tile_len * tile_len * (state_dim + 4 * inner_here + 2 * inner_here)),
            transcendentals=tiles_dev * tile_len * (tile_len * heads_here + 2 * inner_here),
            bytes_accessed=rows * inner_here * 10 + tiles_dev * inner_here * state_dim * 4,
        ),
    )(
        conv_out, conv_out, conv_out, cumul, cumul_t, dt_t, part_col, part_row,
        before_tile, prefix_wide, entering, zx, d_full,
    )


def shards(
    ingest,
    dest_tile,
    doc_start,
    w_zx,
    w_bc,
    w_dt,
    dt_bias,
    a_log,
    conv_x,
    conv_bc,
    cbias_x,
    cbias_bc,
    d_skip,
    norm_gain,
):
    seq_count = lax.axis_size("seq")
    tiles_dev = ingest.shape[0]
    tile_len = ingest.shape[1]
    columns = ingest.shape[2]
    row_count = tiles_dev * tile_len
    heads_here = a_log.shape[0]
    inner_here = conv_x.shape[1]
    head_dim = inner_here // heads_here
    state_dim = conv_bc.shape[1] // 2
    taps = conv_x.shape[0]
    keep_rows = taps - 1
    owner = dest_tile // tiles_dev
    slots = jnp.arange(seq_count, dtype=jnp.int32)
    pick = (owner[None, :] == slots[:, None]).astype(jnp.float32)
    outgoing = jnp.einsum(
        "sj,jrc->src", pick.astype(jnp.bfloat16), ingest, preferred_element_type=jnp.float32
    ).astype(jnp.bfloat16)
    incoming = lax.all_to_all(outgoing, "seq", split_axis=0, concat_axis=0, tiled=True)
    zx_cols, gather_dest = lax.optimization_barrier((w_zx.reshape(w_zx.shape[0], -1), dest_tile))
    every_dest = lax.all_gather(gather_dest, "seq", tiled=True).reshape(seq_count, tiles_dev)
    mine = every_dest // tiles_dev == lax.axis_index("seq")
    got_slot = jnp.sum(jnp.where(mine, every_dest % tiles_dev, 0), 1)
    local_slots = jnp.arange(tiles_dev, dtype=jnp.int32)
    place = (got_slot[None, :] == local_slots[:, None]).astype(jnp.bfloat16)
    arrived = jnp.einsum("js,src->jrc", place, incoming, preferred_element_type=jnp.float32).astype(
        jnp.bfloat16
    )
    own_rows = arrived.reshape(row_count, columns)
    weight_set = (zx_cols, w_bc, w_dt)
    if lax.axis_size("head") == 2:
        partner_rows = lax.ppermute(own_rows, "head", [(0, 1), (1, 0)])
        mine_at = lax.axis_index("head") * columns
        other_at = columns - mine_at

        def project(weight):
            own_part = lax.dynamic_slice_in_dim(weight, mine_at, columns, 0)
            other_part = lax.dynamic_slice_in_dim(weight, other_at, columns, 0)
            return jnp.dot(own_rows, own_part, preferred_element_type=jnp.float32) + jnp.dot(
                partner_rows, other_part, preferred_element_type=jnp.float32
            )

        acc_zx, acc_bc, acc_dt = tuple(project(weight) for weight in weight_set)
    else:
        piece = lax.all_gather(own_rows, "head", axis=1, tiled=True)
        acc_zx, acc_bc, acc_dt = tuple(
            (jnp.dot(piece, weight, preferred_element_type=jnp.float32) for weight in weight_set)
        )
    zx = acc_zx.astype(jnp.bfloat16)
    x_in = zx[:, inner_here:]
    bc_all = acc_bc.astype(jnp.bfloat16)
    step_dt = jax.nn.softplus(acc_dt + dt_bias[None, :])
    within = jnp.arange(tile_len, dtype=jnp.int32)
    has_bound = (doc_start < tile_len).astype(jnp.float32)
    before_count = jnp.cumsum(has_bound) - has_bound
    later = (within[None, :] >= doc_start[:, None]).astype(jnp.float32)
    segment = (before_count[:, None] + later).reshape(row_count)
    conv_in = jnp.concatenate([x_in, bc_all], 1)
    tail = conv_in[row_count - keep_rows :]
    tail_seg = (segment[row_count - keep_rows :] - segment[row_count - 1]).astype(jnp.bfloat16)
    got_both = shifted(jnp.concatenate([tail, tail_seg[:, None]], 1), "seq", 1)
    got_tail, got_seg = got_both[:, : tail.shape[1]], got_both[:, tail.shape[1]]
    extended = jnp.concatenate([got_tail, conv_in], 0)
    ext_seg = jnp.concatenate([got_seg.astype(jnp.float32), segment], 0)
    conv_weight = jnp.concatenate([conv_x, conv_bc], 1)
    conv_bias = jnp.concatenate([cbias_x, cbias_bc], 0)
    total = conv_bias[None, :] + conv_weight[taps - 1][None, :] * conv_in.astype(jnp.float32)
    for back_step in range(keep_rows):
        same = ext_seg[back_step : back_step + row_count] == segment
        total = total + jnp.where(
            same[:, None],
            conv_weight[back_step][None, :]
            * extended[back_step : back_step + row_count].astype(jnp.float32),
            0.0,
        )
    conv_out = jax.nn.silu(total).astype(jnp.bfloat16)
    rate = -jnp.exp(a_log)
    tile_dt = step_dt.reshape(tiles_dev, tile_len, heads_here)
    lower = (within[:, None] >= within[None, :]).astype(jnp.float32)
    cumul = jnp.einsum(
        "is,jsh->jih", lower, tile_dt * rate[None, None, :], precision=lax.Precision.HIGHEST
    )
    cumul_t = cumul.transpose(0, 2, 1)
    dt_t = tile_dt.transpose(0, 2, 1)
    last_part = later[:, tile_len - 1]
    tail_keep = (later == last_part[:, None]).astype(jnp.float32)
    to_end = jnp.exp(cumul[:, tile_len - 1 :, :] - cumul) * tile_dt * tail_keep[:, :, None]
    b_t = conv_out[:, inner_here : inner_here + state_dim].reshape(
        tiles_dev, tile_len, state_dim
    ).transpose(0, 2, 1)
    passing = jnp.exp(cumul[:, tile_len - 1, :]) * (1.0 - has_bound)[:, None]
    through = jnp.cumprod(passing, 0)
    prefix = jnp.concatenate([jnp.ones((1, heads_here), jnp.float32), through[:-1]], 0)
    widen = lambda per_head: jnp.repeat(per_head, head_dim, axis=-1)
    before_tile, run_state = contrib_tiles(
        conv_out, b_t, to_end, widen(passing)[:, None, :], inner_here, state_dim
    )
    position = lax.axis_index("seq")
    run_decay = widen(through[tiles_dev - 1])
    distance = 1
    def with_decay(state, decay):
        high = decay.astype(jnp.bfloat16)
        rest = decay - high.astype(jnp.float32)
        middle = rest.astype(jnp.bfloat16)
        low = (rest - middle.astype(jnp.float32)).astype(jnp.bfloat16)
        return jnp.concatenate([state.astype(jnp.bfloat16), high[None], middle[None], low[None]], 0)

    def unpack(got):
        got = got.astype(jnp.float32)
        return got[:state_dim], got[state_dim] + got[state_dim + 1] + got[state_dim + 2]

    while 2 * distance < seq_count:
        got_state, got_decay = unpack(shifted(with_decay(run_state, run_decay), "seq", distance))
        run_state = run_state + run_decay[None, :] * got_state
        run_decay = jnp.where(position >= distance, run_decay * got_decay, run_decay)
        distance *= 2
    near_state, near_decay = unpack(shifted(with_decay(run_state, run_decay), "seq", 1))
    far_state = shifted(run_state.astype(jnp.bfloat16), "seq", distance + 1).astype(jnp.float32)
    entering = near_state + near_decay[None, :] * far_state
    d_full = jnp.repeat(d_skip, head_dim)[None, :]
    gated, row_sq = mix_tiles(
        conv_out, zx, cumul, cumul_t, dt_t, later, before_tile, widen(prefix)[:, None, :],
        entering, d_full,
    )
    sums = lax.psum(row_sq.reshape(tiles_dev, tile_len), "head").reshape(row_count, 1)
    return (gated * lax.rsqrt(sums / INNER + EPSILON) * norm_gain[None, :]).astype(jnp.bfloat16)


def solution(mesh):
    return jax.shard_map(
        shards,
        mesh=mesh,
        in_specs=(
            P("seq", None, "head"),
            P("seq"),
            P("seq"),
            P(None, None, "head"),
            P(),
            P(None, "head"),
            P("head"),
            P("head"),
            P(None, "head"),
            P(),
            P("head"),
            P(),
            P("head"),
            P("head"),
        ),
        out_specs=P("seq", "head"),
        check_vma=False,
    )
```

```python
import jax
import jax.numpy as jnp
from jax import lax
from jax.experimental import pallas as pl
from jax.experimental.pallas import tpu as pltpu
from jax.sharding import PartitionSpec as P

INNER = 2048


EPSILON = 1e-05


def shifted(x, axis, by):
    devices = lax.axis_size(axis)
    pairs = [(i, i + by) for i in range(devices) if 0 <= i + by < devices]
    return lax.ppermute(x, axis, pairs)


def mix_tile(
    x_ref, b_ref, c_ref, cum_ref, cumt_ref, dtt_ref, partc_ref, partr_ref, before_ref, prefix_ref,
    enter_ref, gate_ref, d_ref, out_ref, sq_ref,
):
    f32 = jnp.float32
    group = cum_ref.shape[0]
    tile_len = cum_ref.shape[1]
    pairs = x_ref.shape[1] // 128
    row = lax.broadcasted_iota(jnp.int32, (tile_len, tile_len), 0)
    col = lax.broadcasted_iota(jnp.int32, (tile_len, tile_len), 1)
    first_half = lax.broadcasted_iota(jnp.int32, (tile_len, 128), 1) < 64
    for sub in range(group):
        rows = pl.ds(sub * tile_len, tile_len)
        c_mat = c_ref[rows, :]
        scores = lax.dot_general(
            c_mat, b_ref[rows, :], (((1,), (1,)), ((), ())), preferred_element_type=f32
        )
        cum = cum_ref[sub]
        cumt = cumt_ref[sub]
        dtt = dtt_ref[sub]
        part_col = partc_ref[sub]
        keep = (row >= col) & (part_col == partr_ref[sub])
        earlier = 1.0 - part_col
        total_sq = jnp.zeros((tile_len, 128), f32)
        for pair in range(pairs):
            cols = pl.ds(pair * 128, 128)
            x_pair = x_ref[rows, cols]
            slabs = []
            for half in range(2):
                head = 2 * pair + half
                diff = cum[:, head : head + 1] - cumt[head : head + 1, :]
                decay = jnp.where(keep, jnp.exp(jnp.where(keep, diff, 0.0)), 0.0)
                slabs.append((scores * decay * dtt[head : head + 1, :]).astype(jnp.bfloat16))
            weights = jnp.concatenate(slabs, axis=1)
            zero = jnp.zeros_like(x_pair)
            split_x = jnp.concatenate(
                [jnp.where(first_half, x_pair, zero), jnp.where(first_half, zero, x_pair)], axis=0
            )
            intra = jnp.dot(weights, split_x, preferred_element_type=f32)
            carried = (
                before_ref[sub, :, cols] + prefix_ref[sub, :, cols] * enter_ref[:, cols]
            ).astype(jnp.bfloat16)
            projected = jnp.dot(c_mat, carried, preferred_element_type=f32)
            grow = jnp.where(
                first_half,
                jnp.exp(cum[:, 2 * pair : 2 * pair + 1]),
                jnp.exp(cum[:, 2 * pair + 1 : 2 * pair + 2]),
            )
            inter = grow * earlier * projected
            mixed = intra + inter + d_ref[:, cols] * x_pair.astype(f32)
            gate = gate_ref[rows, cols].astype(f32)
            gated = mixed * (gate * (0.5 + 0.5 * jnp.tanh(0.5 * gate)))
            out_ref[rows, cols] = gated
            total_sq = total_sq + gated * gated
        sq_ref[sub] = jnp.sum(total_sq, axis=1).reshape(1, tile_len)


def contrib_tile(x_ref, bt_ref, end_ref, pass_ref, before_ref, total_ref):
    f32 = jnp.float32
    group = bt_ref.shape[0]
    tile_len = bt_ref.shape[2]
    pairs = x_ref.shape[1] // 128

    @pl.when(pl.program_id(0) == 0)
    def _():
        total_ref[...] = jnp.zeros_like(total_ref)

    first_half = lax.broadcasted_iota(jnp.int32, (tile_len, 128), 1) < 64
    for sub in range(group):
        b_t = bt_ref[sub]
        to_end = end_ref[sub]
        rows = pl.ds(sub * tile_len, tile_len)
        for pair in range(pairs):
            cols = pl.ds(pair * 128, 128)
            scale = jnp.where(
                first_half,
                to_end[:, 2 * pair : 2 * pair + 1],
                to_end[:, 2 * pair + 1 : 2 * pair + 2],
            )
            scaled = (x_ref[rows, cols].astype(f32) * scale).astype(jnp.bfloat16)
            contrib = jnp.dot(b_t, scaled, preferred_element_type=f32)
            state = total_ref[:, cols]
            before_ref[sub, :, cols] = state
            total_ref[:, cols] = pass_ref[sub, :, cols] * state + contrib


def contrib_tiles(conv_out, b_t, to_end, passing_wide, inner_here, state_dim):
    tiles_dev, tile_len, heads_here = to_end.shape
    group = 4 if tiles_dev % 4 == 0 else 1
    return pl.pallas_call(
        contrib_tile,
        grid=(tiles_dev // group,),
        in_specs=[
            pl.BlockSpec((group * tile_len, inner_here), lambda j: (j, 0)),
            pl.BlockSpec((group, state_dim, tile_len), lambda j: (j, 0, 0)),
            pl.BlockSpec((group, tile_len, heads_here), lambda j: (j, 0, 0)),
            pl.BlockSpec((group, 1, inner_here), lambda j: (j, 0, 0)),
        ],
        out_specs=[
            pl.BlockSpec((group, state_dim, inner_here), lambda j: (j, 0, 0)),
            pl.BlockSpec((state_dim, inner_here), lambda j: (0, 0)),
        ],
        out_shape=[
            jax.ShapeDtypeStruct((tiles_dev, state_dim, inner_here), jnp.float32),
            jax.ShapeDtypeStruct((state_dim, inner_here), jnp.float32),
        ],
        compiler_params=pltpu.CompilerParams(dimension_semantics=("arbitrary",)),
        cost_estimate=pl.CostEstimate(
            flops=tiles_dev * 2 * tile_len * inner_here * state_dim,
            transcendentals=0,
            bytes_accessed=tiles_dev * (tile_len * (inner_here + state_dim) * 2 + inner_here * state_dim * 4),
        ),
    )(conv_out, b_t, to_end, passing_wide)


def mix_tiles(conv_out, zx, cumul, cumul_t, dt_t, later, before_tile, prefix_wide, entering, d_full):
    tiles_dev, tile_len, heads_here = cumul.shape
    inner_here = before_tile.shape[2]
    state_dim = before_tile.shape[1]
    rows = tiles_dev * tile_len
    b_block = inner_here // 128
    c_block = b_block + state_dim // 128
    part_col = later.reshape(tiles_dev, tile_len, 1)
    part_row = later.reshape(tiles_dev, 1, tile_len)
    group = 2 if tiles_dev % 2 == 0 else 1
    per_tile = lambda j: (j, 0, 0)
    span = group * tile_len
    return pl.pallas_call(
        mix_tile,
        grid=(tiles_dev // group,),
        in_specs=[
            pl.BlockSpec((span, inner_here), lambda j: (j, 0)),
            pl.BlockSpec((span, state_dim), lambda j: (j, b_block)),
            pl.BlockSpec((span, state_dim), lambda j: (j, c_block)),
            pl.BlockSpec((group, tile_len, heads_here), per_tile),
            pl.BlockSpec((group, heads_here, tile_len), per_tile),
            pl.BlockSpec((group, heads_here, tile_len), per_tile),
            pl.BlockSpec((group, tile_len, 1), per_tile),
            pl.BlockSpec((group, 1, tile_len), per_tile),
            pl.BlockSpec((group, state_dim, inner_here), per_tile),
            pl.BlockSpec((group, 1, inner_here), per_tile),
            pl.BlockSpec((state_dim, inner_here), lambda j: (0, 0)),
            pl.BlockSpec((span, inner_here), lambda j: (j, 0)),
            pl.BlockSpec((1, inner_here), lambda j: (0, 0)),
        ],
        out_specs=[
            pl.BlockSpec((span, inner_here), lambda j: (j, 0)),
            pl.BlockSpec((group, 1, tile_len), per_tile),
        ],
        out_shape=[
            jax.ShapeDtypeStruct((rows, inner_here), jnp.float32),
            jax.ShapeDtypeStruct((tiles_dev, 1, tile_len), jnp.float32),
        ],
        cost_estimate=pl.CostEstimate(
            flops=tiles_dev * (2 * tile_len * tile_len * (state_dim + 4 * inner_here + 2 * inner_here)),
            transcendentals=tiles_dev * tile_len * (tile_len * heads_here + 2 * inner_here),
            bytes_accessed=rows * inner_here * 10 + tiles_dev * inner_here * state_dim * 4,
        ),
    )(
        conv_out, conv_out, conv_out, cumul, cumul_t, dt_t, part_col, part_row,
        before_tile, prefix_wide, entering, zx, d_full,
    )


def shards(
    ingest,
    dest_tile,
    doc_start,
    w_zx,
    w_bc,
    w_dt,
    dt_bias,
    a_log,
    conv_x,
    conv_bc,
    cbias_x,
    cbias_bc,
    d_skip,
    norm_gain,
):
    seq_count = lax.axis_size("seq")
    tiles_dev = ingest.shape[0]
    tile_len = ingest.shape[1]
    columns = ingest.shape[2]
    row_count = tiles_dev * tile_len
    heads_here = a_log.shape[0]
    inner_here = conv_x.shape[1]
    head_dim = inner_here // heads_here
    state_dim = conv_bc.shape[1] // 2
    taps = conv_x.shape[0]
    keep_rows = taps - 1
    owner = dest_tile // tiles_dev
    slots = jnp.arange(seq_count, dtype=jnp.int32)
    pick = (owner[None, :] == slots[:, None]).astype(jnp.float32)
    outgoing = jnp.einsum(
        "sj,jrc->src", pick.astype(jnp.bfloat16), ingest, preferred_element_type=jnp.float32
    ).astype(jnp.bfloat16)
    incoming = lax.all_to_all(outgoing, "seq", split_axis=0, concat_axis=0, tiled=True)
    zx_cols, gather_dest = lax.optimization_barrier((w_zx.reshape(w_zx.shape[0], -1), dest_tile))
    every_dest = lax.all_gather(gather_dest, "seq", tiled=True).reshape(seq_count, tiles_dev)
    mine = every_dest // tiles_dev == lax.axis_index("seq")
    got_slot = jnp.sum(jnp.where(mine, every_dest % tiles_dev, 0), 1)
    local_slots = jnp.arange(tiles_dev, dtype=jnp.int32)
    place = (got_slot[None, :] == local_slots[:, None]).astype(jnp.bfloat16)
    arrived = jnp.einsum("js,src->jrc", place, incoming, preferred_element_type=jnp.float32).astype(
        jnp.bfloat16
    )
    own_rows = arrived.reshape(row_count, columns)
    weight_set = (zx_cols, w_bc, w_dt)
    if lax.axis_size("head") == 2:
        partner_rows = lax.ppermute(own_rows, "head", [(0, 1), (1, 0)])
        mine_at = lax.axis_index("head") * columns
        other_at = columns - mine_at

        def project(weight):
            own_part = lax.dynamic_slice_in_dim(weight, mine_at, columns, 0)
            other_part = lax.dynamic_slice_in_dim(weight, other_at, columns, 0)
            return jnp.dot(own_rows, own_part, preferred_element_type=jnp.float32) + jnp.dot(
                partner_rows, other_part, preferred_element_type=jnp.float32
            )

        acc_zx, acc_bc, acc_dt = tuple(project(weight) for weight in weight_set)
    else:
        piece = lax.all_gather(own_rows, "head", axis=1, tiled=True)
        acc_zx, acc_bc, acc_dt = tuple(
            (jnp.dot(piece, weight, preferred_element_type=jnp.float32) for weight in weight_set)
        )
    zx = acc_zx.astype(jnp.bfloat16)
    x_in = zx[:, inner_here:]
    bc_all = acc_bc.astype(jnp.bfloat16)
    step_dt = jax.nn.softplus(acc_dt + dt_bias[None, :])
    within = jnp.arange(tile_len, dtype=jnp.int32)
    has_bound = (doc_start < tile_len).astype(jnp.float32)
    before_count = jnp.cumsum(has_bound) - has_bound
    later = (within[None, :] >= doc_start[:, None]).astype(jnp.float32)
    segment = (before_count[:, None] + later).reshape(row_count)
    conv_in = jnp.concatenate([x_in, bc_all], 1)
    tail = conv_in[row_count - keep_rows :]
    tail_seg = (segment[row_count - keep_rows :] - segment[row_count - 1]).astype(jnp.bfloat16)
    got_both = shifted(jnp.concatenate([tail, tail_seg[:, None]], 1), "seq", 1)
    got_tail, got_seg = got_both[:, : tail.shape[1]], got_both[:, tail.shape[1]]
    extended = jnp.concatenate([got_tail, conv_in], 0)
    ext_seg = jnp.concatenate([got_seg.astype(jnp.float32), segment], 0)
    conv_weight = jnp.concatenate([conv_x, conv_bc], 1)
    conv_bias = jnp.concatenate([cbias_x, cbias_bc], 0)
    total = conv_bias[None, :] + conv_weight[taps - 1][None, :] * conv_in.astype(jnp.float32)
    for back_step in range(keep_rows):
        same = ext_seg[back_step : back_step + row_count] == segment
        total = total + jnp.where(
            same[:, None],
            conv_weight[back_step][None, :]
            * extended[back_step : back_step + row_count].astype(jnp.float32),
            0.0,
        )
    conv_out = jax.nn.silu(total).astype(jnp.bfloat16)
    rate = -jnp.exp(a_log)
    tile_dt = step_dt.reshape(tiles_dev, tile_len, heads_here)
    lower = (within[:, None] >= within[None, :]).astype(jnp.float32)
    cumul = jnp.einsum(
        "is,jsh->jih", lower, tile_dt * rate[None, None, :], precision=lax.Precision.HIGHEST
    )
    cumul_t = cumul.transpose(0, 2, 1)
    dt_t = tile_dt.transpose(0, 2, 1)
    last_part = later[:, tile_len - 1]
    tail_keep = (later == last_part[:, None]).astype(jnp.float32)
    to_end = jnp.exp(cumul[:, tile_len - 1 :, :] - cumul) * tile_dt * tail_keep[:, :, None]
    b_t = conv_out[:, inner_here : inner_here + state_dim].reshape(
        tiles_dev, tile_len, state_dim
    ).transpose(0, 2, 1)
    passing = jnp.exp(cumul[:, tile_len - 1, :]) * (1.0 - has_bound)[:, None]
    through = jnp.cumprod(passing, 0)
    prefix = jnp.concatenate([jnp.ones((1, heads_here), jnp.float32), through[:-1]], 0)
    widen = lambda per_head: jnp.repeat(per_head, head_dim, axis=-1)
    before_tile, run_state = contrib_tiles(
        conv_out, b_t, to_end, widen(passing)[:, None, :], inner_here, state_dim
    )
    position = lax.axis_index("seq")
    run_decay = widen(through[tiles_dev - 1])
    distance = 1
    def with_decay(state, decay):
        high = decay.astype(jnp.bfloat16)
        rest = decay - high.astype(jnp.float32)
        middle = rest.astype(jnp.bfloat16)
        low = (rest - middle.astype(jnp.float32)).astype(jnp.bfloat16)
        return jnp.concatenate([state.astype(jnp.bfloat16), high[None], middle[None], low[None]], 0)

    def unpack(got):
        got = got.astype(jnp.float32)
        return got[:state_dim], got[state_dim] + got[state_dim + 1] + got[state_dim + 2]

    while 2 * distance < seq_count:
        got_state, got_decay = unpack(shifted(with_decay(run_state, run_decay), "seq", distance))
        run_state = run_state + run_decay[None, :] * got_state
        run_decay = jnp.where(position >= distance, run_decay * got_decay, run_decay)
        distance *= 2
    near_state, near_decay = unpack(shifted(with_decay(run_state, run_decay), "seq", 1))
    far_state = shifted(run_state.astype(jnp.bfloat16), "seq", distance + 1).astype(jnp.float32)
    entering = near_state + near_decay[None, :] * far_state
    d_full = jnp.repeat(d_skip, head_dim)[None, :]
    gated, row_sq = mix_tiles(
        conv_out, zx, cumul, cumul_t, dt_t, later, before_tile, widen(prefix)[:, None, :],
        entering, d_full,
    )
    sums = lax.psum(row_sq.reshape(tiles_dev, tile_len), "head").reshape(row_count, 1)
    return (gated * lax.rsqrt(sums / INNER + EPSILON) * norm_gain[None, :]).astype(jnp.bfloat16)


def solution(mesh):
    return jax.shard_map(
        shards,
        mesh=mesh,
        in_specs=(
            P("seq", None, "head"),
            P("seq"),
            P("seq"),
            P(None, None, "head"),
            P(),
            P(None, "head"),
            P("head"),
            P("head"),
            P(None, "head"),
            P(),
            P("head"),
            P(),
            P("head"),
            P("head"),
        ),
        out_specs=P("seq", "head"),
        check_vma=False,
    )
```
